256 devices in a mesh: dp: 8 (over x, core), seq: 32 (over y, z).
Axes of the slice: x: 4, y: 4, z: 8, core: 2. Of those that a mesh axis runs over, the one named last changes fastest.
Arguments:
- activations: bfloat16 [8, 4096, 2048], P('dp', 'seq'), may hold values from -16 to 16
- w_query: bfloat16 [2048, 2048], P('seq')
- w_key: bfloat16 [2048, 256], P('seq')
- w_value: bfloat16 [2048, 256], P('seq'), may hold values from -0.125 to 0.125
- key_blocks: int32 [32, 32, 7], replicated, may hold values from 0 to 31, as said below
- random_count: int32 [32], replicated, may hold values from 1 to 3, 64 in all
- grad_out: bfloat16 [8, 4096, 2048], P('dp', 'seq'), may hold values from -6 to 6
Outputs:
- attn_out: bfloat16 [8, 4096, 2048], P('dp', 'seq')
- grad_x: bfloat16 [8, 4096, 2048], P('dp', 'seq')
- grad_wq: bfloat16 [2048, 2048], P('seq')
- grad_wk: bfloat16 [2048, 256], P('seq')
- grad_wv: bfloat16 [2048, 256], P('seq')
The draws below stay inside these ranges and needn't reach their ends.
Inputs may be any that keep to these rules, and one draw needn't show every extreme that they name: `key_blocks`: row b of head h: columns 0 to 2 are b - 1, b and b + 1 modulo 32; column 3 is one block of the head, the same in all its rows; columns 4 to 6 are three blocks that differ from each other and from the row's first four entries. Head h uses the first random_count[h] of its three random key blocks; the counts sum to 64.
All inputs are finite; a program needn't handle non-finite values.
Results may differ from the reference program's by a relative error of at most 0.025.
The reference program's roundings to bfloat16 on the way count: a program that leaves them out, or rounds other values in their place, can miss the bound.
Values may be sent and summed in bfloat16 or wider, within the bound.
No kernel may reach another device: no remote copies, remote signals or barrier semaphores. Data moves between devices by JAX's collectives and lax.ppermute only.
A program may use at most 128 MiB of HBM per device.

```python
import math
import jax
import jax.numpy as jnp
import numpy as np
from jax import lax

D = 2048
HD = 64
GROUP = 8
TOK_DEV = 128
H = 32
KVH = 4
LEN = 4096
NB = 32
BATCH = 8
N_SEQ = 32


def draw_activations(key, part):
    full_shape = (BATCH, LEN, D)
    values = jnp.clip(jax.random.normal(key, full_shape, jnp.float32), -6.0, 6.0)
    return values.astype(jnp.bfloat16)


def projection_pair(key):
    own_key = jax.random.fold_in(key, 31)
    shared_key = jax.random.fold_in(key, 32)
    key_matrix = jnp.clip(jax.random.normal(shared_key, (D, KVH * HD), jnp.float32), -5.0, 5.0) / math.sqrt(D)
    own_part = jnp.clip(jax.random.normal(own_key, (D, H * HD), jnp.float32), -5.0, 5.0) / math.sqrt(D)
    query_matrix = 2.0 * own_part
    return (query_matrix, key_matrix)


def draw_w_query(key, part):
    return projection_pair(key)[0].astype(jnp.bfloat16)


def draw_w_key(key, part):
    return projection_pair(key)[1].astype(jnp.bfloat16)


def draw_key_blocks(key, part):
    order_key = jax.random.fold_in(key, 41)
    global_key = jax.random.fold_in(key, 42)
    block_rows = jnp.arange(NB, dtype=jnp.int32)
    window = jnp.stack([(block_rows - 1) % NB, block_rows, (block_rows + 1) % NB], axis=1)
    window = jnp.broadcast_to(window[None], (H, NB, 3))
    chosen_global = jax.random.randint(global_key, (H, 1, 1), 0, NB, dtype=jnp.int32)
    global_col = jnp.broadcast_to(chosen_global, (H, NB, 1))
    fixed_part = jnp.concatenate([window, global_col], axis=2).astype(jnp.int32)
    row_keys = jax.random.split(order_key, H * NB)
    rank_table = jax.vmap(lambda row_key: jax.random.permutation(row_key, NB))(row_keys).reshape(H, NB, NB).astype(jnp.int32)
    candidates = jnp.arange(NB, dtype=jnp.int32)
    occupied = jnp.any(candidates[None, None, None, :] == fixed_part[:, :, :, None], axis=2)
    rank_score = rank_table + NB * occupied.astype(jnp.int32)
    picked = lax.top_k(-rank_score, 3)[1].astype(jnp.int32)
    return jnp.concatenate([fixed_part, picked], axis=2)


def level_of(key, shape, cuts, low, high):
    factor_of = 1.0
    for position, blocks in cuts:
        heights = jax.random.uniform(jax.random.fold_in(jax.random.fold_in(key, 6), position), (blocks,), jnp.float32, low / len(cuts), high / len(cuts))
        factor_of = factor_of * jnp.repeat(jnp.exp(heights), shape[position] // blocks).reshape((-1,) + (1,) * (len(shape) - 1 - position))
    return factor_of


def profile(amount, total, bound, slope):
    loads = [(1 << 20) // math.isqrt(rank ** slope) + 1 for rank in range(2, amount + 1)]
    surplus, counts = total - bound - (amount - 1), [1] * (amount - 1)
    while surplus > 0:
        free = [i for i in range(amount - 1) if counts[i] < bound]
        whole, left = sum([loads[i] for i in free]), surplus
        for i in free:
            more = min(bound - counts[i], max(1, left * loads[i] // whole), surplus)
            counts[i] = counts[i] + more
            surplus = surplus - more
    return np.array([bound] + counts)


def ragged_sizes(stream_key, count, total, most, skew):
    if count == 2:
        one = jax.random.randint(stream_key, (), max(1, total - most), min(most, total - 1) + 1)
        return jnp.stack([one, total - one])
    lengths = jnp.asarray(profile(count, total, most, skew), jnp.int32)
    pairs = (count - 1) // 2
    source_of, receiver = lengths[1:1 + 2 * pairs:2], lengths[2:2 + 2 * pairs:2]
    room = jnp.minimum(source_of - 1, most - receiver)
    shifted = jax.random.randint(jax.random.fold_in(stream_key, 1), (pairs,), 0, 1 << 20) % (room + 1)
    lengths = lengths.at[1:1 + 2 * pairs:2].set(source_of - shifted).at[2:2 + 2 * pairs:2].set(receiver + shifted)
    return lengths[jax.random.permutation(jax.random.fold_in(stream_key, 2), count)]


def gaussian(rng, dims, spread, reach, shards=(), kind=jnp.bfloat16):
    values = jax.random.normal(rng, dims, jnp.float32) * spread
    if len(shards) > 0:
        values = level_of(rng, dims, shards, -0.22, 0.18) * values
    return jnp.clip(values, min=-reach, max=reach).astype(kind)


def setup_inputs(seed: int = 0) -> dict:
    splits = jax.random.split(jax.random.key(seed), 8)
    activations = draw_activations(jax.random.fold_in(splits[7], 71), 0)
    w_query = draw_w_query(jax.random.fold_in(splits[7], 71), 0)
    w_key = draw_w_key(jax.random.fold_in(splits[7], 71), 0)
    w_value = gaussian(splits[3], (D, KVH * HD), D ** -0.5, 0.125, ((0, 32),))
    key_blocks = draw_key_blocks(jax.random.fold_in(splits[7], 71), 0)
    random_count = ragged_sizes(splits[5], H, 2 * H, 3, 2).astype(jnp.int32)
    grad_out = gaussian(splits[6], (BATCH, LEN, H * HD), 1.0, 6.0, ((0, 8), (1, 32)))
    return {"activations": activations, "w_query": w_query, "w_key": w_key, "w_value": w_value, "key_blocks": key_blocks, "random_count": random_count, "grad_out": grad_out}


masked_score = -1e+30
query_group = 4

def head_pass(queries, key_rows, value_rows, grad_head, blocks, extra_count):
    seq_len, head_width = queries.shape
    block_count, slot_count = blocks.shape
    block_len = seq_len // block_count
    score_scale = head_width ** (-0.5)
    key_tiles = key_rows.reshape(block_count, block_len, head_width)
    value_tiles = value_rows.reshape(block_count, block_len, head_width)
    usable = jnp.repeat(jnp.arange(slot_count) < 4 + extra_count, block_len)
    rounds = block_count // query_group
    query_steps = queries.reshape(rounds, query_group, block_len, head_width)
    grad_steps = grad_head.reshape(rounds, query_group, block_len, head_width)
    block_steps = blocks.reshape(rounds, query_group, slot_count)

    def one_step(running, inputs):
        q_part, g_part, chosen = inputs
        k_part = key_tiles[chosen].reshape(query_group, slot_count * block_len, head_width)
        v_part = value_tiles[chosen].reshape(query_group, slot_count * block_len, head_width)
        scores = jnp.einsum('gqe,gke->gqk', q_part.astype(jnp.float32), k_part.astype(jnp.float32)) * score_scale
        scores = jnp.where(usable, scores, masked_score)
        highest = lax.optimization_barrier(jnp.max(scores, axis=-1, keepdims=True))
        exponent = jnp.exp(scores - highest)
        shares = exponent / lax.optimization_barrier(jnp.sum(exponent, axis=-1, keepdims=True))
        shares_low = shares.astype(jnp.bfloat16)
        attended = jnp.einsum('gqk,gke->gqe', shares_low.astype(jnp.float32), v_part.astype(jnp.float32)).astype(jnp.bfloat16)
        grad_shares = jnp.einsum('gqe,gke->gqk', g_part.astype(jnp.float32), v_part.astype(jnp.float32))
        weighted = lax.optimization_barrier(jnp.sum(grad_shares * shares, axis=-1, keepdims=True))
        grad_scores = (shares * (grad_shares - weighted)).astype(jnp.bfloat16)
        grad_query = (jnp.einsum('gqk,gke->gqe', grad_scores.astype(jnp.float32), k_part.astype(jnp.float32)) * score_scale).astype(jnp.bfloat16)
        grad_keys = jnp.einsum('gqk,gqe->gke', grad_scores.astype(jnp.float32), q_part.astype(jnp.float32)) * score_scale
        grad_values = jnp.einsum('gqk,gqe->gke', shares_low.astype(jnp.float32), g_part.astype(jnp.float32))
        pieces = jnp.concatenate([grad_keys, grad_values], axis=-1).reshape(query_group * slot_count, block_len, 2 * head_width)
        running = running.at[chosen.reshape(-1)].add(pieces)
        return (running, (attended, grad_query))
    initial = jnp.zeros((block_count, block_len, 2 * head_width), jnp.float32)
    summed, (attended, grad_query) = lax.scan(one_step, initial, (query_steps, grad_steps, block_steps))
    return (attended.reshape(seq_len, head_width), grad_query.reshape(seq_len, head_width), summed.reshape(seq_len, 2 * head_width))

def reference(activations, w_query, w_key, w_value, key_blocks, random_count, grad_out):
    factor = 1.0 / math.sqrt(BATCH * LEN)

    def one_sequence(inputs):
        tokens, grad_rows = inputs
        queries = jnp.dot(tokens, w_query, preferred_element_type=jnp.float32).astype(jnp.bfloat16)
        key_proj = jnp.dot(tokens, w_key, preferred_element_type=jnp.float32).astype(jnp.bfloat16)
        value_proj = jnp.dot(tokens, w_value, preferred_element_type=jnp.float32).astype(jnp.bfloat16)
        head_q = queries.reshape(LEN, H, HD).transpose(1, 0, 2)
        head_g = grad_rows.reshape(LEN, H, HD).transpose(1, 0, 2)
        key_heads = key_proj.reshape(LEN, KVH, HD).transpose(1, 0, 2)
        value_heads = value_proj.reshape(LEN, KVH, HD).transpose(1, 0, 2)

        def per_head(head_index):
            kv_index = head_index // GROUP
            return head_pass(head_q[head_index], key_heads[kv_index], value_heads[kv_index], head_g[head_index], key_blocks[head_index], random_count[head_index])
        attended, grad_q, grad_kv = lax.map(per_head, jnp.arange(H, dtype=jnp.int32))
        grad_kv_low = lax.optimization_barrier(grad_kv.astype(jnp.bfloat16))
        kv_sum = lax.optimization_barrier(jnp.sum(grad_kv_low.reshape(KVH, GROUP, LEN, 2 * HD).astype(jnp.float32), axis=1)).astype(jnp.bfloat16)
        out_rows = attended.transpose(1, 0, 2).reshape(LEN, H * HD)
        grad_q_rows = grad_q.transpose(1, 0, 2).reshape(LEN, H * HD)
        grad_k_rows = kv_sum[:, :, :HD].transpose(1, 0, 2).reshape(LEN, KVH * HD)
        grad_v_rows = kv_sum[:, :, HD:].transpose(1, 0, 2).reshape(LEN, KVH * HD)
        grad_x_rows = (jnp.dot(grad_q_rows, w_query.T, preferred_element_type=jnp.float32) + jnp.dot(grad_k_rows, w_key.T, preferred_element_type=jnp.float32) + jnp.dot(grad_v_rows, w_value.T, preferred_element_type=jnp.float32)).astype(jnp.bfloat16)
        combined = jnp.concatenate([grad_q_rows, grad_k_rows, grad_v_rows], axis=1)
        return (out_rows, grad_x_rows, combined)
    attn_out, grad_x, combined = lax.map(one_sequence, (activations, grad_out))

    def add_term(running, run_index):
        sequence = run_index // N_SEQ
        shard = run_index % N_SEQ
        token_seq = lax.dynamic_index_in_dim(activations, sequence, 0, keepdims=False)
        grad_seq = lax.dynamic_index_in_dim(combined, sequence, 0, keepdims=False)
        token_run = lax.dynamic_slice_in_dim(token_seq, (shard * TOK_DEV).astype(jnp.int32), TOK_DEV, 0)
        grad_run = lax.dynamic_slice_in_dim(grad_seq, (shard * TOK_DEV).astype(jnp.int32), TOK_DEV, 0)
        grad_term = jnp.dot(token_run.T, grad_run, preferred_element_type=jnp.float32) * factor
        term_low = lax.optimization_barrier(grad_term.astype(jnp.bfloat16))
        return (running + term_low.astype(jnp.float32), None)
    start_sum = jnp.zeros((D, (H + 2 * KVH) * HD), jnp.float32)
    grad_sum, _ = lax.scan(add_term, start_sum, jnp.arange(BATCH * N_SEQ, dtype=jnp.int32))
    grad_all = grad_sum.astype(jnp.bfloat16)
    grad_wq = grad_all[:, :H * HD]
    grad_wk = grad_all[:, H * HD:H * HD + KVH * HD]
    grad_wv = grad_all[:, H * HD + KVH * HD:]
    return (attn_out, grad_x, grad_wq, grad_wk, grad_wv)
```

```python
import math

import jax
import jax.numpy as jnp
from jax import lax
from jax.sharding import PartitionSpec as P

HD = 64
GROUP = 8


masked_score = -1e30
query_group = 4


def head_pass(queries, key_rows, value_rows, grad_head, blocks, extra_count):
    seq_len, head_width = queries.shape
    block_count, slot_count = blocks.shape
    block_len = seq_len // block_count
    score_scale = head_width ** (-0.5)
    key_tiles = key_rows.reshape(block_count, block_len, head_width)
    value_tiles = value_rows.reshape(block_count, block_len, head_width)
    usable = jnp.repeat(jnp.arange(slot_count) < 4 + extra_count, block_len)
    rounds = block_count // query_group
    query_steps = queries.reshape(rounds, query_group, block_len, head_width)
    grad_steps = grad_head.reshape(rounds, query_group, block_len, head_width)
    block_steps = blocks.reshape(rounds, query_group, slot_count)

    def one_step(running, inputs):
        q_part, g_part, chosen = inputs
        k_part = key_tiles[chosen].reshape(query_group, slot_count * block_len, head_width)
        v_part = value_tiles[chosen].reshape(query_group, slot_count * block_len, head_width)
        scores = (
            jnp.einsum("gqe,gke->gqk", q_part, k_part, preferred_element_type=jnp.float32)
            * score_scale
        )
        scores = jnp.where(usable, scores, masked_score)
        highest = jnp.max(scores, axis=-1, keepdims=True)
        exponent = jnp.exp(scores - highest)
        shares = exponent / jnp.sum(exponent, axis=-1, keepdims=True)
        shares_low = shares.astype(jnp.bfloat16)
        attended = jnp.einsum(
            "gqk,gke->gqe", shares_low, v_part, preferred_element_type=jnp.float32
        ).astype(jnp.bfloat16)
        grad_shares = jnp.einsum("gqe,gke->gqk", g_part, v_part, preferred_element_type=jnp.float32)
        weighted = jnp.sum(grad_shares * shares, axis=-1, keepdims=True)
        grad_scores = (shares * (grad_shares - weighted)).astype(jnp.bfloat16)
        grad_query = (
            jnp.einsum("gqk,gke->gqe", grad_scores, k_part, preferred_element_type=jnp.float32)
            * score_scale
        ).astype(jnp.bfloat16)
        grad_keys = (
            jnp.einsum("gqk,gqe->gke", grad_scores, q_part, preferred_element_type=jnp.float32)
            * score_scale
        )
        grad_values = jnp.einsum(
            "gqk,gqe->gke", shares_low, g_part, preferred_element_type=jnp.float32
        )
        pieces = jnp.concatenate([grad_keys, grad_values], axis=-1).reshape(
            query_group * slot_count, block_len, 2 * head_width
        )
        running = running.at[chosen.reshape(-1)].add(pieces)
        return (running, (attended, grad_query))

    initial = jnp.zeros((block_count, block_len, 2 * head_width), jnp.float32)
    summed, (attended, grad_query) = lax.scan(
        one_step, initial, (query_steps, grad_steps, block_steps)
    )
    return (
        attended.reshape(seq_len, head_width),
        grad_query.reshape(seq_len, head_width),
        summed.reshape(seq_len, 2 * head_width),
    )


def per_device(activations, w_query, w_key, w_value, key_blocks, random_count, grad_out):
    seq_devices = lax.axis_size("seq")
    dp_devices = lax.axis_size("dp")
    position = lax.axis_index("seq")
    dp_index = lax.axis_index("dp")
    tokens = activations[0]
    grad_rows = grad_out[0]
    tok_count = tokens.shape[0]
    heads = w_query.shape[1] // HD
    kv_heads = w_key.shape[1] // HD
    query_cols = heads * HD
    kv_cols = kv_heads * HD
    all_cols = query_cols + 2 * kv_cols
    w_local = jnp.concatenate([w_query, w_key, w_value], axis=1)
    w_full = lax.all_gather(w_local, "seq", axis=0, tiled=True)
    projected = jnp.dot(tokens, w_full, preferred_element_type=jnp.float32).astype(jnp.bfloat16)
    queries = projected[:, :query_cols]
    key_proj = projected[:, query_cols : query_cols + kv_cols]
    value_proj = projected[:, query_cols + kv_cols :]
    query_pieces = queries.reshape(tok_count, heads, HD).transpose(1, 0, 2)
    grad_pieces = grad_rows.reshape(tok_count, heads, HD).transpose(1, 0, 2)
    paired = jnp.concatenate(
        [key_proj.reshape(tok_count, kv_heads, HD), value_proj.reshape(tok_count, kv_heads, HD)],
        axis=2,
    )
    kv_pieces = jnp.repeat(paired.transpose(1, 0, 2), GROUP, axis=0)
    sent = jnp.concatenate([query_pieces, grad_pieces, kv_pieces], axis=2)
    landed = lax.all_to_all(sent, "seq", split_axis=0, concat_axis=1, tiled=True)[0]
    head_q = landed[:, :HD]
    head_grad = landed[:, HD : 2 * HD]
    head_k = landed[:, 2 * HD : 3 * HD]
    head_v = landed[:, 3 * HD :]
    blocks_mine = lax.dynamic_index_in_dim(key_blocks, position, 0, keepdims=False)
    count_mine = lax.dynamic_index_in_dim(random_count, position, 0, keepdims=False)
    attended, grad_query, grad_kv = head_pass(
        head_q, head_k, head_v, head_grad, blocks_mine, count_mine
    )
    back_sent = jnp.concatenate(
        [
            attended.reshape(seq_devices, tok_count, HD),
            grad_query.reshape(seq_devices, tok_count, HD),
            grad_kv.astype(jnp.bfloat16).reshape(seq_devices, tok_count, 2 * HD),
        ],
        axis=2,
    )
    back = lax.all_to_all(back_sent, "seq", split_axis=0, concat_axis=0, tiled=True)
    back_out = back[:, :, :HD]
    back_query = back[:, :, HD : 2 * HD]
    back_kv = back[:, :, 2 * HD :]
    out_rows = back_out.transpose(1, 0, 2).reshape(tok_count, heads * HD)
    grad_q_rows = back_query.transpose(1, 0, 2).reshape(tok_count, heads * HD)
    kv_sum = jnp.sum(
        back_kv.reshape(kv_heads, GROUP, tok_count, 2 * HD), axis=1, dtype=jnp.float32
    ).astype(jnp.bfloat16)
    grad_k_rows = kv_sum[:, :, :HD].transpose(1, 0, 2).reshape(tok_count, kv_heads * HD)
    grad_v_rows = kv_sum[:, :, HD:].transpose(1, 0, 2).reshape(tok_count, kv_heads * HD)
    combined = jnp.concatenate([grad_q_rows, grad_k_rows, grad_v_rows], axis=1)
    contract = (((1,), (1,)), ((), ()))
    grad_x_rows = lax.dot_general(
        combined, w_full, contract, preferred_element_type=jnp.float32
    ).astype(jnp.bfloat16)
    factor = 1.0 / math.sqrt(tok_count * seq_devices * dp_devices)
    over_tokens = (((0,), (0,)), ((), ()))
    term = (
        lax.dot_general(tokens, combined, over_tokens, preferred_element_type=jnp.float32)
        * factor
    ).astype(jnp.bfloat16)
    half = all_cols // 2
    core = dp_index % 2
    pairs = [(i, i ^ 1) for i in range(dp_devices)]
    keep = lax.dynamic_slice_in_dim(term, core * half, half, axis=1)
    give = lax.dynamic_slice_in_dim(term, (1 - core) * half, half, axis=1)
    got = lax.ppermute(give, "dp", pairs)
    chip_sum = (keep.astype(jnp.float32) + got.astype(jnp.float32)).astype(jnp.bfloat16)
    part = lax.psum_scatter(chip_sum, "seq", scatter_dimension=0, tiled=True)
    step = 2
    while step < dp_devices:
        mates = [(i, i ^ step) for i in range(dp_devices)]
        other = lax.ppermute(part, "dp", mates)
        part = (part.astype(jnp.float32) + other.astype(jnp.float32)).astype(jnp.bfloat16)
        step *= 2
    other_half = lax.ppermute(part, "dp", pairs)
    first = jnp.where(core == 0, part, other_half)
    second = jnp.where(core == 0, other_half, part)
    grad_all = jnp.concatenate([first, second], axis=1)
    grad_wq = grad_all[:, :query_cols]
    grad_wk = grad_all[:, query_cols : query_cols + kv_cols]
    grad_wv = grad_all[:, query_cols + kv_cols :]
    return (out_rows[None], grad_x_rows[None], grad_wq, grad_wk, grad_wv)


def solution(mesh):
    placed = (
        P("dp", "seq", None),
        P("seq", None),
        P("seq", None),
        P("seq", None),
        P(),
        P(),
        P("dp", "seq", None),
    )
    return jax.shard_map(
        per_device,
        mesh=mesh,
        in_specs=placed,
        out_specs=(
            P("dp", "seq", None),
            P("dp", "seq", None),
            P("seq", None),
            P("seq", None),
            P("seq", None),
        ),
        check_vma=False,
    )
```

```python
import math

import jax
import jax.numpy as jnp
from jax import lax
from jax.sharding import PartitionSpec as P

HD = 64
GROUP = 8


masked_score = -1e30
query_group = 4
RING_Z = 8


def head_pass(queries, key_rows, value_rows, grad_head, blocks, extra_count):
    seq_len, head_width = queries.shape
    block_count, slot_count = blocks.shape
    block_len = seq_len // block_count
    score_scale = head_width ** (-0.5)
    key_tiles = key_rows.reshape(block_count, block_len, head_width)
    value_tiles = value_rows.reshape(block_count, block_len, head_width)
    q_part = queries.reshape(block_count, block_len, head_width)
    g_part = grad_head.reshape(block_count, block_len, head_width)
    usable = jnp.repeat(jnp.arange(slot_count) < 4 + extra_count, block_len)
    k_part = key_tiles[blocks].reshape(block_count, slot_count * block_len, head_width)
    v_part = value_tiles[blocks].reshape(block_count, slot_count * block_len, head_width)
    scores = (
        jnp.einsum("gqe,gke->gqk", q_part, k_part, preferred_element_type=jnp.float32)
        * score_scale
    )
    scores = jnp.where(usable, scores, masked_score)
    highest = jnp.max(scores, axis=-1, keepdims=True)
    exponent = jnp.exp(scores - highest)
    shares = exponent / jnp.sum(exponent, axis=-1, keepdims=True)
    shares_low = shares.astype(jnp.bfloat16)
    attended = jnp.einsum(
        "gqk,gke->gqe", shares_low, v_part, preferred_element_type=jnp.float32
    ).astype(jnp.bfloat16)
    grad_shares = jnp.einsum("gqe,gke->gqk", g_part, v_part, preferred_element_type=jnp.float32)
    weighted = jnp.sum(grad_shares * shares, axis=-1, keepdims=True)
    grad_scores = (shares * (grad_shares - weighted)).astype(jnp.bfloat16)
    grad_query = (
        jnp.einsum("gqk,gke->gqe", grad_scores, k_part, preferred_element_type=jnp.float32)
        * score_scale
    ).astype(jnp.bfloat16)
    grad_keys = (
        jnp.einsum("gqk,gqe->gke", grad_scores, q_part, preferred_element_type=jnp.float32)
        * score_scale
    )
    grad_values = jnp.einsum(
        "gqk,gqe->gke", shares_low, g_part, preferred_element_type=jnp.float32
    )
    pieces = jnp.concatenate([grad_keys, grad_values], axis=-1).reshape(
        block_count * slot_count, block_len * 2 * head_width
    )
    owner = (
        blocks.reshape(1, block_count * slot_count)
        == jnp.arange(block_count, dtype=blocks.dtype)[:, None]
    ).astype(jnp.float32)
    summed = jnp.dot(owner, pieces, precision=lax.Precision.HIGHEST)
    return (
        attended.reshape(seq_len, head_width),
        grad_query.reshape(seq_len, head_width),
        summed.reshape(seq_len, 2 * head_width),
    )


def ring_reduce_scatter(parts, ring, stride, position):
    seq_devices = lax.axis_size("seq")
    group = ring * stride
    me = (position // stride) % ring
    width = parts.shape[-1] // 2
    ahead = [
        (s, (s // group) * group + (((s // stride) % ring + 1) % ring) * stride + s % stride)
        for s in range(seq_devices)
    ]
    behind = [(b, a) for (a, b) in ahead]
    total = []
    for side, perm, sign in ((0, ahead, 1), (1, behind, -1)):
        own = parts[..., side * width : (side + 1) * width]

        def chunk(k):
            return lax.dynamic_index_in_dim(own, (me - sign * (1 + k)) % ring, 0, keepdims=False)

        buf = chunk(0)
        for k in range(ring - 1):
            got = lax.ppermute(buf, "seq", perm)
            buf = (got.astype(jnp.float32) + chunk(k + 1).astype(jnp.float32)).astype(jnp.bfloat16)
        total.append(buf)
    return jnp.concatenate(total, axis=-1)


def per_device(activations, w_query, w_key, w_value, key_blocks, random_count, grad_out):
    seq_devices = lax.axis_size("seq")
    dp_devices = lax.axis_size("dp")
    position = lax.axis_index("seq")
    dp_index = lax.axis_index("dp")
    tokens = activations[0]
    grad_rows = grad_out[0]
    tok_count = tokens.shape[0]
    heads = w_query.shape[1] // HD
    kv_heads = w_key.shape[1] // HD
    query_cols = heads * HD
    kv_cols = kv_heads * HD
    all_cols = query_cols + 2 * kv_cols
    w_local = jnp.concatenate([w_query, w_key, w_value], axis=1)
    w_full = lax.all_gather(w_local, "seq", axis=0, tiled=True)
    projected = jnp.dot(tokens, w_full, preferred_element_type=jnp.float32).astype(jnp.bfloat16)
    queries = projected[:, :query_cols]
    key_proj = projected[:, query_cols : query_cols + kv_cols]
    value_proj = projected[:, query_cols + kv_cols :]
    query_pieces = queries.reshape(tok_count, heads, HD).transpose(1, 0, 2)
    grad_pieces = grad_rows.reshape(tok_count, heads, HD).transpose(1, 0, 2)
    paired = jnp.concatenate(
        [key_proj.reshape(tok_count, kv_heads, HD), value_proj.reshape(tok_count, kv_heads, HD)],
        axis=2,
    )
    kv_pieces = jnp.repeat(paired.transpose(1, 0, 2), GROUP, axis=0)
    sent = jnp.concatenate([query_pieces, grad_pieces, kv_pieces], axis=2)
    landed = lax.all_to_all(sent, "seq", split_axis=0, concat_axis=1, tiled=True)[0]
    head_q = landed[:, :HD]
    head_grad = landed[:, HD : 2 * HD]
    head_k = landed[:, 2 * HD : 3 * HD]
    head_v = landed[:, 3 * HD :]
    blocks_mine = lax.dynamic_index_in_dim(key_blocks, position, 0, keepdims=False)
    count_mine = lax.dynamic_index_in_dim(random_count, position, 0, keepdims=False)
    attended, grad_query, grad_kv = head_pass(
        head_q, head_k, head_v, head_grad, blocks_mine, count_mine
    )
    back_sent = jnp.concatenate(
        [
            attended.reshape(seq_devices, tok_count, HD),
            grad_query.reshape(seq_devices, tok_count, HD),
            grad_kv.astype(jnp.bfloat16).reshape(seq_devices, tok_count, 2 * HD),
        ],
        axis=2,
    )
    back = lax.all_to_all(back_sent, "seq", split_axis=0, concat_axis=0, tiled=True)
    back_out = back[:, :, :HD]
    back_query = back[:, :, HD : 2 * HD]
    back_kv = back[:, :, 2 * HD :]
    out_rows = back_out.transpose(1, 0, 2).reshape(tok_count, heads * HD)
    grad_q_rows = back_query.transpose(1, 0, 2).reshape(tok_count, heads * HD)
    kv_sum = jnp.sum(
        back_kv.reshape(kv_heads, GROUP, tok_count, 2 * HD), axis=1, dtype=jnp.float32
    ).astype(jnp.bfloat16)
    grad_k_rows = kv_sum[:, :, :HD].transpose(1, 0, 2).reshape(tok_count, kv_heads * HD)
    grad_v_rows = kv_sum[:, :, HD:].transpose(1, 0, 2).reshape(tok_count, kv_heads * HD)
    combined = jnp.concatenate([grad_q_rows, grad_k_rows, grad_v_rows], axis=1)
    contract = (((1,), (1,)), ((), ()))
    grad_x_rows = lax.dot_general(
        combined, w_full, contract, preferred_element_type=jnp.float32
    ).astype(jnp.bfloat16)
    factor = 1.0 / math.sqrt(tok_count * seq_devices * dp_devices)
    over_tokens = (((0,), (0,)), ((), ()))
    term = (
        lax.dot_general(tokens, combined, over_tokens, preferred_element_type=jnp.float32)
        * factor
    ).astype(jnp.bfloat16)
    half = all_cols // 2
    core = dp_index % 2
    pairs = [(i, i ^ 1) for i in range(dp_devices)]
    keep = lax.dynamic_slice_in_dim(term, core * half, half, axis=1)
    give = lax.dynamic_slice_in_dim(term, (1 - core) * half, half, axis=1)
    got = lax.ppermute(give, "dp", pairs)
    chip_sum = (keep.astype(jnp.float32) + got.astype(jnp.float32)).astype(jnp.bfloat16)
    rows = chip_sum.shape[0] // seq_devices
    by_z = chip_sum.reshape(seq_devices // RING_Z, RING_Z, rows, half).transpose(1, 0, 2, 3)
    by_y = ring_reduce_scatter(by_z, RING_Z, 1, position)
    part = ring_reduce_scatter(by_y, seq_devices // RING_Z, RING_Z, position)
    step = 2
    while step < dp_devices:
        mates = [(i, i ^ step) for i in range(dp_devices)]
        other = lax.ppermute(part, "dp", mates)
        part = (part.astype(jnp.float32) + other.astype(jnp.float32)).astype(jnp.bfloat16)
        step *= 2
    other_half = lax.ppermute(part, "dp", pairs)
    first = jnp.where(core == 0, part, other_half)
    second = jnp.where(core == 0, other_half, part)
    grad_all = jnp.concatenate([first, second], axis=1)
    grad_wq = grad_all[:, :query_cols]
    grad_wk = grad_all[:, query_cols : query_cols + kv_cols]
    grad_wv = grad_all[:, query_cols + kv_cols :]
    return (out_rows[None], grad_x_rows[None], grad_wq, grad_wk, grad_wv)


def solution(mesh):
    placed = (
        P("dp", "seq", None),
        P("seq", None),
        P("seq", None),
        P("seq", None),
        P(),
        P(),
        P("dp", "seq", None),
    )
    return jax.shard_map(
        per_device,
        mesh=mesh,
        in_specs=placed,
        out_specs=(
            P("dp", "seq", None),
            P("dp", "seq", None),
            P("seq", None),
            P("seq", None),
            P("seq", None),
        ),
        check_vma=False,
    )
```

```python
import math

import jax
import jax.numpy as jnp
from jax import lax
from jax.experimental import pallas as pl
from jax.experimental.pallas import tpu as pltpu
from jax.sharding import PartitionSpec as P

HD = 64
GROUP = 8


masked_score = -1e30
query_group = 4
RING_Z = 8


def head_kernel(table_ref, count_ref, q_ref, g_ref, k_ref, v_ref,
                out_ref, gq_ref, dk_ref, dv_ref):
    b = pl.program_id(0)
    slot_count = table_ref.shape[0] // pl.num_programs(0)
    head_width = q_ref.shape[-1]
    score_scale = head_width ** (-0.5)

    @pl.when(b == 0)
    def _():
        dk_ref[...] = jnp.zeros_like(dk_ref)
        dv_ref[...] = jnp.zeros_like(dv_ref)

    q = q_ref[0]
    g = g_ref[0]
    used = 4 + count_ref[0]
    chosen = [table_ref[b * slot_count + j] for j in range(slot_count)]
    keys = [k_ref[c] for c in chosen]
    vals = [v_ref[c] for c in chosen]
    nt = (((1,), (1,)), ((), ()))
    tn = (((0,), (0,)), ((), ()))
    scores = []
    for j in range(slot_count):
        s = lax.dot_general(q, keys[j], nt, preferred_element_type=jnp.float32) * score_scale
        if j >= 4:
            s = jnp.where(j < used, s, masked_score)
        scores.append(s)
    highest = scores[0].max(axis=-1, keepdims=True)
    for s in scores[1:]:
        highest = jnp.maximum(highest, s.max(axis=-1, keepdims=True))
    exps = [jnp.exp(s - highest) for s in scores]
    denom = exps[0].sum(axis=-1, keepdims=True)
    for e in exps[1:]:
        denom = denom + e.sum(axis=-1, keepdims=True)
    shares = [e / denom for e in exps]
    shares_low = [p.astype(jnp.bfloat16) for p in shares]
    attended = jnp.dot(shares_low[0], vals[0], preferred_element_type=jnp.float32)
    for j in range(1, slot_count):
        attended = attended + jnp.dot(shares_low[j], vals[j], preferred_element_type=jnp.float32)
    out_ref[0] = attended.astype(out_ref.dtype)
    grad_shares = [lax.dot_general(g, vals[j], nt, preferred_element_type=jnp.float32)
                   for j in range(slot_count)]
    weighted = (grad_shares[0] * shares[0]).sum(axis=-1, keepdims=True)
    for j in range(1, slot_count):
        weighted = weighted + (grad_shares[j] * shares[j]).sum(axis=-1, keepdims=True)
    grad_scores = [(shares[j] * (grad_shares[j] - weighted)).astype(jnp.bfloat16)
                   for j in range(slot_count)]
    grad_query = jnp.dot(grad_scores[0], keys[0], preferred_element_type=jnp.float32)
    for j in range(1, slot_count):
        grad_query = grad_query + jnp.dot(grad_scores[j], keys[j], preferred_element_type=jnp.float32)
    gq_ref[0] = (grad_query * score_scale).astype(gq_ref.dtype)
    for j in range(slot_count):
        dk = lax.dot_general(grad_scores[j], q, tn, preferred_element_type=jnp.float32) * score_scale
        dv = lax.dot_general(shares_low[j], g, tn, preferred_element_type=jnp.float32)
        dk_ref[chosen[j]] += dk
        dv_ref[chosen[j]] += dv


def head_pass(queries, key_rows, value_rows, grad_head, blocks, extra_count):
    seq_len, head_width = queries.shape
    block_count, slot_count = blocks.shape
    block_len = seq_len // block_count
    tiles = (block_count, block_len, head_width)
    one_block = pl.BlockSpec((1, block_len, head_width), lambda b, t, c: (b, 0, 0))
    whole = pl.BlockSpec(tiles, lambda b, t, c: (0, 0, 0))
    grid_spec = pltpu.PrefetchScalarGridSpec(
        num_scalar_prefetch=2,
        grid=(block_count,),
        in_specs=[one_block, one_block, whole, whole],
        out_specs=[one_block, one_block, whole, whole],
    )
    flops = 2 * seq_len * slot_count * block_len * head_width * 6
    attended, grad_query, grad_k, grad_v = pl.pallas_call(
        head_kernel,
        grid_spec=grid_spec,
        out_shape=[
            jax.ShapeDtypeStruct(tiles, jnp.bfloat16),
            jax.ShapeDtypeStruct(tiles, jnp.bfloat16),
            jax.ShapeDtypeStruct(tiles, jnp.float32),
            jax.ShapeDtypeStruct(tiles, jnp.float32),
        ],
        compiler_params=pltpu.CompilerParams(dimension_semantics=("arbitrary",)),
        cost_estimate=pl.CostEstimate(
            flops=flops,
            transcendentals=seq_len * slot_count * block_len,
            bytes_accessed=seq_len * head_width * 2 * 6 + seq_len * head_width * 4 * 2,
        ),
    )(
        blocks.reshape(-1),
        jnp.reshape(extra_count, (1,)),
        queries.reshape(tiles),
        grad_head.reshape(tiles),
        key_rows.reshape(tiles),
        value_rows.reshape(tiles),
    )
    summed = jnp.concatenate([grad_k, grad_v], axis=-1)
    return (
        attended.reshape(seq_len, head_width),
        grad_query.reshape(seq_len, head_width),
        summed.reshape(seq_len, 2 * head_width),
    )


def ring_reduce_scatter(parts, ring, stride, position):
    seq_devices = lax.axis_size("seq")
    group = ring * stride
    me = (position // stride) % ring
    width = parts.shape[-1] // 2
    ahead = [
        (s, (s // group) * group + (((s // stride) % ring + 1) % ring) * stride + s % stride)
        for s in range(seq_devices)
    ]
    behind = [(b, a) for (a, b) in ahead]
    total = []
    for side, perm, sign in ((0, ahead, 1), (1, behind, -1)):
        own = parts[..., side * width : (side + 1) * width]

        def chunk(k):
            return lax.dynamic_index_in_dim(own, (me - sign * (1 + k)) % ring, 0, keepdims=False)

        buf = chunk(0)
        for k in range(ring - 1):
            got = lax.ppermute(buf, "seq", perm)
            buf = (got.astype(jnp.float32) + chunk(k + 1).astype(jnp.float32)).astype(jnp.bfloat16)
        total.append(buf)
    return jnp.concatenate(total, axis=-1)


def per_device(activations, w_query, w_key, w_value, key_blocks, random_count, grad_out):
    seq_devices = lax.axis_size("seq")
    dp_devices = lax.axis_size("dp")
    position = lax.axis_index("seq")
    dp_index = lax.axis_index("dp")
    tokens = activations[0]
    grad_rows = grad_out[0]
    tok_count = tokens.shape[0]
    heads = w_query.shape[1] // HD
    kv_heads = w_key.shape[1] // HD
    query_cols = heads * HD
    kv_cols = kv_heads * HD
    all_cols = query_cols + 2 * kv_cols
    w_local = jnp.concatenate([w_query, w_key, w_value], axis=1)
    w_full = lax.all_gather(w_local, "seq", axis=0, tiled=True)
    projected = jnp.dot(tokens, w_full, preferred_element_type=jnp.float32).astype(jnp.bfloat16)
    queries = projected[:, :query_cols]
    key_proj = projected[:, query_cols : query_cols + kv_cols]
    value_proj = projected[:, query_cols + kv_cols :]
    query_pieces = queries.reshape(tok_count, heads, HD).transpose(1, 0, 2)
    grad_pieces = grad_rows.reshape(tok_count, heads, HD).transpose(1, 0, 2)
    paired = jnp.concatenate(
        [key_proj.reshape(tok_count, kv_heads, HD), value_proj.reshape(tok_count, kv_heads, HD)],
        axis=2,
    )
    kv_pieces = jnp.repeat(paired.transpose(1, 0, 2), GROUP, axis=0)
    sent = jnp.concatenate([query_pieces, grad_pieces, kv_pieces], axis=2)
    landed = lax.all_to_all(sent, "seq", split_axis=0, concat_axis=1, tiled=True)[0]
    head_q = landed[:, :HD]
    head_grad = landed[:, HD : 2 * HD]
    head_k = landed[:, 2 * HD : 3 * HD]
    head_v = landed[:, 3 * HD :]
    blocks_mine = lax.dynamic_index_in_dim(key_blocks, position, 0, keepdims=False)
    count_mine = lax.dynamic_index_in_dim(random_count, position, 0, keepdims=False)
    attended, grad_query, grad_kv = head_pass(
        head_q, head_k, head_v, head_grad, blocks_mine, count_mine
    )
    back_sent = jnp.concatenate(
        [
            attended.reshape(seq_devices, tok_count, HD),
            grad_query.reshape(seq_devices, tok_count, HD),
            grad_kv.astype(jnp.bfloat16).reshape(seq_devices, tok_count, 2 * HD),
        ],
        axis=2,
    )
    back = lax.all_to_all(back_sent, "seq", split_axis=0, concat_axis=0, tiled=True)
    back_out = back[:, :, :HD]
    back_query = back[:, :, HD : 2 * HD]
    back_kv = back[:, :, 2 * HD :]
    out_rows = back_out.transpose(1, 0, 2).reshape(tok_count, heads * HD)
    grad_q_rows = back_query.transpose(1, 0, 2).reshape(tok_count, heads * HD)
    kv_sum = jnp.sum(
        back_kv.reshape(kv_heads, GROUP, tok_count, 2 * HD), axis=1, dtype=jnp.float32
    ).astype(jnp.bfloat16)
    grad_k_rows = kv_sum[:, :, :HD].transpose(1, 0, 2).reshape(tok_count, kv_heads * HD)
    grad_v_rows = kv_sum[:, :, HD:].transpose(1, 0, 2).reshape(tok_count, kv_heads * HD)
    combined = jnp.concatenate([grad_q_rows, grad_k_rows, grad_v_rows], axis=1)
    contract = (((1,), (1,)), ((), ()))
    grad_x_rows = lax.dot_general(
        combined, w_full, contract, preferred_element_type=jnp.float32
    ).astype(jnp.bfloat16)
    factor = 1.0 / math.sqrt(tok_count * seq_devices * dp_devices)
    over_tokens = (((0,), (0,)), ((), ()))
    term = (
        lax.dot_general(tokens, combined, over_tokens, preferred_element_type=jnp.float32)
        * factor
    ).astype(jnp.bfloat16)
    half = all_cols // 2
    core = dp_index % 2
    pairs = [(i, i ^ 1) for i in range(dp_devices)]
    keep = lax.dynamic_slice_in_dim(term, core * half, half, axis=1)
    give = lax.dynamic_slice_in_dim(term, (1 - core) * half, half, axis=1)
    got = lax.ppermute(give, "dp", pairs)
    chip_sum = (keep.astype(jnp.float32) + got.astype(jnp.float32)).astype(jnp.bfloat16)
    rows = chip_sum.shape[0] // seq_devices
    by_z = chip_sum.reshape(seq_devices // RING_Z, RING_Z, rows, half).transpose(1, 0, 2, 3)
    by_y = ring_reduce_scatter(by_z, RING_Z, 1, position)
    part = ring_reduce_scatter(by_y, seq_devices // RING_Z, RING_Z, position)
    step = 2
    while step < dp_devices:
        mates = [(i, i ^ step) for i in range(dp_devices)]
        other = lax.ppermute(part, "dp", mates)
        part = (part.astype(jnp.float32) + other.astype(jnp.float32)).astype(jnp.bfloat16)
        step *= 2
    other_half = lax.ppermute(part, "dp", pairs)
    first = jnp.where(core == 0, part, other_half)
    second = jnp.where(core == 0, other_half, part)
    grad_all = jnp.concatenate([first, second], axis=1)
    grad_wq = grad_all[:, :query_cols]
    grad_wk = grad_all[:, query_cols : query_cols + kv_cols]
    grad_wv = grad_all[:, query_cols + kv_cols :]
    return (out_rows[None], grad_x_rows[None], grad_wq, grad_wk, grad_wv)


def solution(mesh):
    placed = (
        P("dp", "seq", None),
        P("seq", None),
        P("seq", None),
        P("seq", None),
        P(),
        P(),
        P("dp", "seq", None),
    )
    return jax.shard_map(
        per_device,
        mesh=mesh,
        in_specs=placed,
        out_specs=(
            P("dp", "seq", None),
            P("dp", "seq", None),
            P("seq", None),
            P("seq", None),
            P("seq", None),
        ),
        check_vma=False,
    )
```

```python
import math

import jax
import jax.numpy as jnp
from jax import lax
from jax.experimental import pallas as pl
from jax.experimental.pallas import tpu as pltpu
from jax.sharding import PartitionSpec as P

HD = 64
GROUP = 8


masked_score = -1e30
query_group = 4
RING_Z = 8


def head_kernel(table_ref, count_ref, q_ref, g_ref, k_ref, v_ref,
                out_ref, gq_ref, dk_ref, dv_ref):
    b = pl.program_id(0)
    slot_count = table_ref.shape[0] // pl.num_programs(0)
    head_width = q_ref.shape[-1]
    score_scale = head_width ** (-0.5)

    @pl.when(b == 0)
    def _():
        dk_ref[...] = jnp.zeros_like(dk_ref)
        dv_ref[...] = jnp.zeros_like(dv_ref)

    q = q_ref[0]
    g = g_ref[0]
    used = 4 + count_ref[0]
    chosen = [table_ref[b * slot_count + j] for j in range(slot_count)]
    keys = [k_ref[c] for c in chosen]
    vals = [v_ref[c] for c in chosen]
    nt = (((1,), (1,)), ((), ()))
    tn = (((0,), (0,)), ((), ()))
    scores = []
    for j in range(slot_count):
        s = lax.dot_general(q, keys[j], nt, preferred_element_type=jnp.float32) * score_scale
        if j >= 4:
            s = jnp.where(j < used, s, masked_score)
        scores.append(s)
    highest = scores[0].max(axis=-1, keepdims=True)
    for s in scores[1:]:
        highest = jnp.maximum(highest, s.max(axis=-1, keepdims=True))
    exps = [jnp.exp(s - highest) for s in scores]
    denom = exps[0].sum(axis=-1, keepdims=True)
    for e in exps[1:]:
        denom = denom + e.sum(axis=-1, keepdims=True)
    shares = [e / denom for e in exps]
    shares_low = [p.astype(jnp.bfloat16) for p in shares]
    attended = jnp.dot(shares_low[0], vals[0], preferred_element_type=jnp.float32)
    for j in range(1, slot_count):
        attended = attended + jnp.dot(shares_low[j], vals[j], preferred_element_type=jnp.float32)
    out_ref[0] = attended.astype(out_ref.dtype)
    grad_shares = [lax.dot_general(g, vals[j], nt, preferred_element_type=jnp.float32)
                   for j in range(slot_count)]
    weighted = (grad_shares[0] * shares[0]).sum(axis=-1, keepdims=True)
    for j in range(1, slot_count):
        weighted = weighted + (grad_shares[j] * shares[j]).sum(axis=-1, keepdims=True)
    grad_scores = [(shares[j] * (grad_shares[j] - weighted)).astype(jnp.bfloat16)
                   for j in range(slot_count)]
    grad_query = jnp.dot(grad_scores[0], keys[0], preferred_element_type=jnp.float32)
    for j in range(1, slot_count):
        grad_query = grad_query + jnp.dot(grad_scores[j], keys[j], preferred_element_type=jnp.float32)
    gq_ref[0] = (grad_query * score_scale).astype(gq_ref.dtype)
    for j in range(slot_count):
        dk = lax.dot_general(grad_scores[j], q, tn, preferred_element_type=jnp.float32) * score_scale
        dv = lax.dot_general(shares_low[j], g, tn, preferred_element_type=jnp.float32)
        dk_ref[chosen[j]] += dk
        dv_ref[chosen[j]] += dv


def head_pass(queries, key_rows, value_rows, grad_head, blocks, extra_count):
    seq_len, head_width = queries.shape
    block_count, slot_count = blocks.shape
    block_len = seq_len // block_count
    tiles = (block_count, block_len, head_width)
    one_block = pl.BlockSpec((1, block_len, head_width), lambda b, t, c: (b, 0, 0))
    whole = pl.BlockSpec(tiles, lambda b, t, c: (0, 0, 0))
    grid_spec = pltpu.PrefetchScalarGridSpec(
        num_scalar_prefetch=2,
        grid=(block_count,),
        in_specs=[one_block, one_block, whole, whole],
        out_specs=[one_block, one_block, whole, whole],
    )
    flops = 2 * seq_len * slot_count * block_len * head_width * 6
    attended, grad_query, grad_k, grad_v = pl.pallas_call(
        head_kernel,
        grid_spec=grid_spec,
        out_shape=[
            jax.ShapeDtypeStruct(tiles, jnp.bfloat16),
            jax.ShapeDtypeStruct(tiles, jnp.bfloat16),
            jax.ShapeDtypeStruct(tiles, jnp.float32),
            jax.ShapeDtypeStruct(tiles, jnp.float32),
        ],
        compiler_params=pltpu.CompilerParams(dimension_semantics=("arbitrary",)),
        cost_estimate=pl.CostEstimate(
            flops=flops,
            transcendentals=seq_len * slot_count * block_len,
            bytes_accessed=seq_len * head_width * 2 * 6 + seq_len * head_width * 4 * 2,
        ),
    )(
        blocks.reshape(-1),
        jnp.reshape(extra_count, (1,)),
        queries.reshape(tiles),
        grad_head.reshape(tiles),
        key_rows.reshape(tiles),
        value_rows.reshape(tiles),
    )
    summed = jnp.concatenate([grad_k, grad_v], axis=-1)
    return (
        attended.reshape(seq_len, head_width),
        grad_query.reshape(seq_len, head_width),
        summed.reshape(seq_len, 2 * head_width),
    )


def ring_reduce_scatter(parts, ring, stride, position):
    seq_devices = lax.axis_size("seq")
    group = ring * stride
    me = (position // stride) % ring
    width = parts.shape[-1] // 2
    ahead = [
        (s, (s // group) * group + (((s // stride) % ring + 1) % ring) * stride + s % stride)
        for s in range(seq_devices)
    ]
    behind = [(b, a) for (a, b) in ahead]
    total = []
    for side, perm, sign in ((0, ahead, 1), (1, behind, -1)):
        own = parts[..., side * width : (side + 1) * width]

        def chunk(k):
            return lax.dynamic_index_in_dim(own, (me - sign * (1 + k)) % ring, 0, keepdims=False)

        buf = chunk(0)
        for k in range(ring - 1):
            got = lax.ppermute(buf, "seq", perm)
            buf = (got.astype(jnp.float32) + chunk(k + 1).astype(jnp.float32)).astype(jnp.bfloat16)
        total.append(buf)
    return jnp.concatenate(total, axis=-1)


def per_device(activations, w_query, w_key, w_value, key_blocks, random_count, grad_out):
    seq_devices = lax.axis_size("seq")
    dp_devices = lax.axis_size("dp")
    position = lax.axis_index("seq")
    dp_index = lax.axis_index("dp")
    tokens = activations[0]
    grad_rows = grad_out[0]
    tok_count = tokens.shape[0]
    heads = w_query.shape[1] // HD
    kv_heads = w_key.shape[1] // HD
    query_cols = heads * HD
    kv_cols = kv_heads * HD
    all_cols = query_cols + 2 * kv_cols
    w_local = jnp.concatenate([w_query, w_key, w_value], axis=1)
    half = all_cols // 2
    core = dp_index % 2
    pairs = [(i, i ^ 1) for i in range(dp_devices)]
    grad_pieces = grad_rows.reshape(tok_count, heads, HD).transpose(1, 0, 2)
    head_grad = lax.all_to_all(grad_pieces, "seq", split_axis=0, concat_axis=1, tiled=True)[0]
    w_mine = lax.all_gather(
        lax.dynamic_slice_in_dim(w_local, core * half, half, axis=1), "seq", axis=0, tiled=True
    )
    w_other = lax.ppermute(w_mine, "dp", pairs)
    proj_mine = jnp.dot(tokens, w_mine, preferred_element_type=jnp.float32).astype(jnp.bfloat16)
    proj_other = jnp.dot(tokens, w_other, preferred_element_type=jnp.float32).astype(jnp.bfloat16)
    projected = jnp.concatenate(
        [jnp.where(core == 0, proj_mine, proj_other), jnp.where(core == 0, proj_other, proj_mine)],
        axis=1,
    )
    queries = projected[:, :query_cols]
    key_proj = projected[:, query_cols : query_cols + kv_cols]
    value_proj = projected[:, query_cols + kv_cols :]
    query_pieces = queries.reshape(tok_count, heads, HD).transpose(1, 0, 2)
    paired = jnp.concatenate(
        [key_proj.reshape(tok_count, kv_heads, HD), value_proj.reshape(tok_count, kv_heads, HD)],
        axis=2,
    )
    kv_pieces = jnp.repeat(paired.transpose(1, 0, 2), GROUP, axis=0)
    sent = jnp.concatenate([query_pieces, kv_pieces], axis=2)
    landed = lax.all_to_all(sent, "seq", split_axis=0, concat_axis=1, tiled=True)[0]
    head_q = landed[:, :HD]
    head_k = landed[:, HD : 2 * HD]
    head_v = landed[:, 2 * HD :]
    blocks_mine = lax.dynamic_index_in_dim(key_blocks, position, 0, keepdims=False)
    count_mine = lax.dynamic_index_in_dim(random_count, position, 0, keepdims=False)
    attended, grad_query, grad_kv = head_pass(
        head_q, head_k, head_v, head_grad, blocks_mine, count_mine
    )
    back_sent = jnp.concatenate(
        [
            attended.reshape(seq_devices, tok_count, HD),
            grad_query.reshape(seq_devices, tok_count, HD),
            grad_kv.astype(jnp.bfloat16).reshape(seq_devices, tok_count, 2 * HD),
        ],
        axis=2,
    )
    back = lax.all_to_all(back_sent, "seq", split_axis=0, concat_axis=0, tiled=True)
    back_out = back[:, :, :HD]
    back_query = back[:, :, HD : 2 * HD]
    back_kv = back[:, :, 2 * HD :]
    out_rows = back_out.transpose(1, 0, 2).reshape(tok_count, heads * HD)
    grad_q_rows = back_query.transpose(1, 0, 2).reshape(tok_count, heads * HD)
    kv_sum = jnp.sum(
        back_kv.reshape(kv_heads, GROUP, tok_count, 2 * HD), axis=1, dtype=jnp.float32
    ).astype(jnp.bfloat16)
    grad_k_rows = kv_sum[:, :, :HD].transpose(1, 0, 2).reshape(tok_count, kv_heads * HD)
    grad_v_rows = kv_sum[:, :, HD:].transpose(1, 0, 2).reshape(tok_count, kv_heads * HD)
    combined = jnp.concatenate([grad_q_rows, grad_k_rows, grad_v_rows], axis=1)
    contract = (((1,), (1,)), ((), ()))
    comb_mine = lax.dynamic_slice_in_dim(combined, core * half, half, axis=1)
    comb_other = lax.dynamic_slice_in_dim(combined, (1 - core) * half, half, axis=1)
    grad_x_rows = (
        lax.dot_general(comb_mine, w_mine, contract, preferred_element_type=jnp.float32)
        + lax.dot_general(comb_other, w_other, contract, preferred_element_type=jnp.float32)
    ).astype(jnp.bfloat16)
    factor = 1.0 / math.sqrt(tok_count * seq_devices * dp_devices)
    over_tokens = (((0,), (0,)), ((), ()))
    def term_of(columns):
        return (
            lax.dot_general(tokens, columns, over_tokens, preferred_element_type=jnp.float32)
            * factor
        ).astype(jnp.bfloat16)

    got = lax.ppermute(term_of(comb_other), "dp", pairs)
    keep = term_of(comb_mine)
    chip_sum = (keep.astype(jnp.float32) + got.astype(jnp.float32)).astype(jnp.bfloat16)
    rows = chip_sum.shape[0] // seq_devices
    by_z = chip_sum.reshape(seq_devices // RING_Z, RING_Z, rows, half).transpose(1, 0, 2, 3)
    by_y = ring_reduce_scatter(by_z, RING_Z, 1, position)
    part = ring_reduce_scatter(by_y, seq_devices // RING_Z, RING_Z, position)
    step = 2
    while step < dp_devices:
        mates = [(i, i ^ step) for i in range(dp_devices)]
        other = lax.ppermute(part, "dp", mates)
        part = (part.astype(jnp.float32) + other.astype(jnp.float32)).astype(jnp.bfloat16)
        step *= 2
    other_half = lax.ppermute(part, "dp", pairs)
    first = jnp.where(core == 0, part, other_half)
    second = jnp.where(core == 0, other_half, part)
    grad_all = jnp.concatenate([first, second], axis=1)
    grad_wq = grad_all[:, :query_cols]
    grad_wk = grad_all[:, query_cols : query_cols + kv_cols]
    grad_wv = grad_all[:, query_cols + kv_cols :]
    return (out_rows[None], grad_x_rows[None], grad_wq, grad_wk, grad_wv)


def solution(mesh):
    placed = (
        P("dp", "seq", None),
        P("seq", None),
        P("seq", None),
        P("seq", None),
        P(),
        P(),
        P("dp", "seq", None),
    )
    return jax.shard_map(
        per_device,
        mesh=mesh,
        in_specs=placed,
        out_specs=(
            P("dp", "seq", None),
            P("dp", "seq", None),
            P("seq", None),
            P("seq", None),
            P("seq", None),
        ),
        check_vma=False,
    )
```

```python
import math

import jax
import jax.numpy as jnp
from jax import lax
from jax.experimental import pallas as pl
from jax.experimental.pallas import tpu as pltpu
from jax.sharding import PartitionSpec as P

HD = 64
GROUP = 8


masked_score = -1e30
query_group = 4
RING_Z = 8


def head_kernel(table_ref, count_ref, q_ref, g_ref, k_ref, v_ref,
                out_ref, gq_ref, dk_ref, dv_ref):
    b = pl.program_id(0)
    slot_count = table_ref.shape[0] // pl.num_programs(0)
    head_width = q_ref.shape[-1]
    score_scale = head_width ** (-0.5)

    @pl.when(b == 0)
    def _():
        dk_ref[...] = jnp.zeros_like(dk_ref)
        dv_ref[...] = jnp.zeros_like(dv_ref)

    q = q_ref[0]
    g = g_ref[0]
    used = 4 + count_ref[0]
    chosen = [table_ref[b * slot_count + j] for j in range(slot_count)]
    keys = [k_ref[c] for c in chosen]
    vals = [v_ref[c] for c in chosen]
    nt = (((1,), (1,)), ((), ()))
    tn = (((0,), (0,)), ((), ()))
    scores = []
    for j in range(slot_count):
        s = lax.dot_general(q, keys[j], nt, preferred_element_type=jnp.float32) * score_scale
        if j >= 4:
            s = jnp.where(j < used, s, masked_score)
        scores.append(s)
    highest = scores[0].max(axis=-1, keepdims=True)
    for s in scores[1:]:
        highest = jnp.maximum(highest, s.max(axis=-1, keepdims=True))
    exps = [jnp.exp(s - highest) for s in scores]
    denom = exps[0].sum(axis=-1, keepdims=True)
    for e in exps[1:]:
        denom = denom + e.sum(axis=-1, keepdims=True)
    shares = [e / denom for e in exps]
    shares_low = [p.astype(jnp.bfloat16) for p in shares]
    attended = jnp.dot(shares_low[0], vals[0], preferred_element_type=jnp.float32)
    for j in range(1, slot_count):
        attended = attended + jnp.dot(shares_low[j], vals[j], preferred_element_type=jnp.float32)
    out_ref[0] = attended.astype(out_ref.dtype)
    grad_shares = [lax.dot_general(g, vals[j], nt, preferred_element_type=jnp.float32)
                   for j in range(slot_count)]
    weighted = (grad_shares[0] * shares[0]).sum(axis=-1, keepdims=True)
    for j in range(1, slot_count):
        weighted = weighted + (grad_shares[j] * shares[j]).sum(axis=-1, keepdims=True)
    grad_scores = [(shares[j] * (grad_shares[j] - weighted)).astype(jnp.bfloat16)
                   for j in range(slot_count)]
    grad_query = jnp.dot(grad_scores[0], keys[0], preferred_element_type=jnp.float32)
    for j in range(1, slot_count):
        grad_query = grad_query + jnp.dot(grad_scores[j], keys[j], preferred_element_type=jnp.float32)
    gq_ref[0] = (grad_query * score_scale).astype(gq_ref.dtype)
    for j in range(slot_count):
        dk = lax.dot_general(grad_scores[j], q, tn, preferred_element_type=jnp.float32) * score_scale
        dv = lax.dot_general(shares_low[j], g, tn, preferred_element_type=jnp.float32)
        dk_ref[chosen[j]] += dk
        dv_ref[chosen[j]] += dv


def head_pass(queries, key_rows, value_rows, grad_head, blocks, extra_count):
    seq_len, head_width = queries.shape
    block_count, slot_count = blocks.shape
    block_len = seq_len // block_count
    tiles = (block_count, block_len, head_width)
    one_block = pl.BlockSpec((1, block_len, head_width), lambda b, t, c: (b, 0, 0))
    whole = pl.BlockSpec(tiles, lambda b, t, c: (0, 0, 0))
    grid_spec = pltpu.PrefetchScalarGridSpec(
        num_scalar_prefetch=2,
        grid=(block_count,),
        in_specs=[one_block, one_block, whole, whole],
        out_specs=[one_block, one_block, whole, whole],
    )
    flops = 2 * seq_len * slot_count * block_len * head_width * 6
    attended, grad_query, grad_k, grad_v = pl.pallas_call(
        head_kernel,
        grid_spec=grid_spec,
        out_shape=[
            jax.ShapeDtypeStruct(tiles, jnp.bfloat16),
            jax.ShapeDtypeStruct(tiles, jnp.bfloat16),
            jax.ShapeDtypeStruct(tiles, jnp.float32),
            jax.ShapeDtypeStruct(tiles, jnp.float32),
        ],
        compiler_params=pltpu.CompilerParams(dimension_semantics=("arbitrary",)),
        cost_estimate=pl.CostEstimate(
            flops=flops,
            transcendentals=seq_len * slot_count * block_len,
            bytes_accessed=seq_len * head_width * 2 * 6 + seq_len * head_width * 4 * 2,
        ),
    )(
        blocks.reshape(-1),
        jnp.reshape(extra_count, (1,)),
        queries.reshape(tiles),
        grad_head.reshape(tiles),
        key_rows.reshape(tiles),
        value_rows.reshape(tiles),
    )
    summed = jnp.concatenate([grad_k, grad_v], axis=-1)
    return (
        attended.reshape(seq_len, head_width),
        grad_query.reshape(seq_len, head_width),
        summed.reshape(seq_len, 2 * head_width),
    )


def ring_reduce_scatter(chunk, ring, stride, position):
    seq_devices = lax.axis_size("seq")
    group = ring * stride
    me = (position // stride) % ring
    ahead = [
        (s, (s // group) * group + (((s // stride) % ring + 1) % ring) * stride + s % stride)
        for s in range(seq_devices)
    ]
    behind = [(b, a) for (a, b) in ahead]
    total = []
    for side, perm, sign in ((0, ahead, 1), (1, behind, -1)):
        buf = chunk((me - sign) % ring, side)
        for k in range(ring - 1):
            got = lax.ppermute(buf, "seq", perm)
            own = chunk((me - sign * (2 + k)) % ring, side)
            buf = (got.astype(jnp.float32) + own.astype(jnp.float32)).astype(jnp.bfloat16)
        total.append(buf)
    return jnp.concatenate(total, axis=-1)


def direct_sum(pieces, axis_name, size, stride, mine):
    devices = lax.axis_size(axis_name)
    group = size * stride
    got = [lax.dynamic_index_in_dim(pieces, mine, 0, keepdims=False)]
    for d in range(1, size):
        perm = [
            (i, (i // group) * group + (((i // stride) % size + d) % size) * stride + i % stride)
            for i in range(devices)
        ]
        got.append(lax.ppermute(
            lax.dynamic_index_in_dim(pieces, (mine + d) % size, 0, keepdims=False), axis_name, perm
        ))
    return got


def per_device(activations, w_query, w_key, w_value, key_blocks, random_count, grad_out):
    seq_devices = lax.axis_size("seq")
    dp_devices = lax.axis_size("dp")
    position = lax.axis_index("seq")
    dp_index = lax.axis_index("dp")
    tokens = activations[0]
    grad_rows = grad_out[0]
    tok_count = tokens.shape[0]
    heads = w_query.shape[1] // HD
    kv_heads = w_key.shape[1] // HD
    query_cols = heads * HD
    kv_cols = kv_heads * HD
    all_cols = query_cols + 2 * kv_cols
    w_local = jnp.concatenate([w_query, w_key, w_value], axis=1)
    half = all_cols // 2
    core = dp_index % 2
    pairs = [(i, i ^ 1) for i in range(dp_devices)]
    grad_pieces = grad_rows.reshape(tok_count, heads, HD).transpose(1, 0, 2)
    head_grad = lax.all_to_all(grad_pieces, "seq", split_axis=0, concat_axis=1, tiled=True)[0]
    w_mine = lax.all_gather(
        lax.dynamic_slice_in_dim(w_local, core * half, half, axis=1), "seq", axis=0, tiled=True
    )
    w_other = lax.ppermute(w_mine, "dp", pairs)
    proj_mine = jnp.dot(tokens, w_mine, preferred_element_type=jnp.float32).astype(jnp.bfloat16)
    proj_other = jnp.dot(tokens, w_other, preferred_element_type=jnp.float32).astype(jnp.bfloat16)
    projected = jnp.concatenate(
        [jnp.where(core == 0, proj_mine, proj_other), jnp.where(core == 0, proj_other, proj_mine)],
        axis=1,
    )
    queries = projected[:, :query_cols]
    key_proj = projected[:, query_cols : query_cols + kv_cols]
    value_proj = projected[:, query_cols + kv_cols :]
    query_pieces = queries.reshape(tok_count, heads, HD).transpose(1, 0, 2)
    paired = jnp.concatenate(
        [key_proj.reshape(tok_count, kv_heads, HD), value_proj.reshape(tok_count, kv_heads, HD)],
        axis=2,
    )
    kv_pieces = jnp.repeat(paired.transpose(1, 0, 2), GROUP, axis=0)
    sent = jnp.concatenate([query_pieces, kv_pieces], axis=2)
    landed = lax.all_to_all(sent, "seq", split_axis=0, concat_axis=1, tiled=True)[0]
    head_q = landed[:, :HD]
    head_k = landed[:, HD : 2 * HD]
    head_v = landed[:, 2 * HD :]
    blocks_mine = lax.dynamic_index_in_dim(key_blocks, position, 0, keepdims=False)
    count_mine = lax.dynamic_index_in_dim(random_count, position, 0, keepdims=False)
    attended, grad_query, grad_kv = head_pass(
        head_q, head_k, head_v, head_grad, blocks_mine, count_mine
    )
    back_sent = jnp.concatenate(
        [
            attended.reshape(seq_devices, tok_count, HD),
            grad_query.reshape(seq_devices, tok_count, HD),
            grad_kv.astype(jnp.bfloat16).reshape(seq_devices, tok_count, 2 * HD),
        ],
        axis=2,
    )
    back = lax.all_to_all(back_sent, "seq", split_axis=0, concat_axis=0, tiled=True)
    back_out = back[:, :, :HD]
    back_query = back[:, :, HD : 2 * HD]
    back_kv = back[:, :, 2 * HD :]
    out_rows = back_out.transpose(1, 0, 2).reshape(tok_count, heads * HD)
    grad_q_rows = back_query.transpose(1, 0, 2).reshape(tok_count, heads * HD)
    kv_sum = jnp.sum(
        back_kv.reshape(kv_heads, GROUP, tok_count, 2 * HD), axis=1, dtype=jnp.float32
    ).astype(jnp.bfloat16)
    grad_k_rows = kv_sum[:, :, :HD].transpose(1, 0, 2).reshape(tok_count, kv_heads * HD)
    grad_v_rows = kv_sum[:, :, HD:].transpose(1, 0, 2).reshape(tok_count, kv_heads * HD)
    combined = jnp.concatenate([grad_q_rows, grad_k_rows, grad_v_rows], axis=1)
    contract = (((1,), (1,)), ((), ()))
    comb_mine = lax.dynamic_slice_in_dim(combined, core * half, half, axis=1)
    comb_other = lax.dynamic_slice_in_dim(combined, (1 - core) * half, half, axis=1)
    grad_x_rows = (
        lax.dot_general(comb_mine, w_mine, contract, preferred_element_type=jnp.float32)
        + lax.dot_general(comb_other, w_other, contract, preferred_element_type=jnp.float32)
    ).astype(jnp.bfloat16)
    factor = 1.0 / math.sqrt(tok_count * seq_devices * dp_devices)
    over_tokens = (((0,), (0,)), ((), ()))
    def term_of(columns):
        return (
            lax.dot_general(tokens, columns, over_tokens, preferred_element_type=jnp.float32)
            * factor
        ).astype(jnp.bfloat16)

    got = lax.ppermute(term_of(comb_other), "dp", pairs)
    keep = term_of(comb_mine)
    rows = keep.shape[0] // seq_devices
    y_count = seq_devices // RING_Z
    keep4 = keep.reshape(y_count, RING_Z, rows, half)
    got4 = got.reshape(y_count, RING_Z, rows, half)
    quarter = half // 2

    def chip_chunk(i, side):
        a = lax.dynamic_index_in_dim(keep4, i, 1, keepdims=False)[..., side * quarter : (side + 1) * quarter]
        b = lax.dynamic_index_in_dim(got4, i, 1, keepdims=False)[..., side * quarter : (side + 1) * quarter]
        return (a.astype(jnp.float32) + b.astype(jnp.float32)).astype(jnp.bfloat16)

    by_y = ring_reduce_scatter(chip_chunk, RING_Z, 1, position)
    from_y = direct_sum(by_y, "seq", y_count, RING_Z, position // RING_Z)
    total = from_y[0].astype(jnp.float32)
    for piece in from_y[1:]:
        total = total + piece.astype(jnp.float32)
    part = total.astype(jnp.bfloat16)
    chips = dp_devices // 2
    chip = dp_index // 2
    from_x = direct_sum(jnp.broadcast_to(part, (chips,) + part.shape), "dp", chips, 2, chip)
    by_offset = jnp.stack(from_x)
    in_order = jnp.take(by_offset, (chip - jnp.arange(chips)) % chips, axis=0)
    part = jnp.sum(in_order.astype(jnp.float32), axis=0).astype(jnp.bfloat16)
    other_half = lax.ppermute(part, "dp", pairs)
    first = jnp.where(core == 0, part, other_half)
    second = jnp.where(core == 0, other_half, part)
    grad_all = jnp.concatenate([first, second], axis=1)
    grad_wq = grad_all[:, :query_cols]
    grad_wk = grad_all[:, query_cols : query_cols + kv_cols]
    grad_wv = grad_all[:, query_cols + kv_cols :]
    return (out_rows[None], grad_x_rows[None], grad_wq, grad_wk, grad_wv)


def solution(mesh):
    placed = (
        P("dp", "seq", None),
        P("seq", None),
        P("seq", None),
        P("seq", None),
        P(),
        P(),
        P("dp", "seq", None),
    )
    return jax.shard_map(
        per_device,
        mesh=mesh,
        in_specs=placed,
        out_specs=(
            P("dp", "seq", None),
            P("dp", "seq", None),
            P("seq", None),
            P("seq", None),
            P("seq", None),
        ),
        check_vma=False,
    )
```

```python
import math

import jax
import jax.numpy as jnp
from jax import lax
from jax.experimental import pallas as pl
from jax.experimental.pallas import tpu as pltpu
from jax.sharding import PartitionSpec as P

HD = 64
GROUP = 8


masked_score = -1e30
query_group = 4
RING_Z = 8


def head_kernel(table_ref, count_ref, q_ref, g_ref, k_ref, v_ref,
                out_ref, gq_ref, dk_ref, dv_ref):
    b = pl.program_id(0)
    slot_count = table_ref.shape[0] // pl.num_programs(0)
    head_width = q_ref.shape[-1]
    score_scale = head_width ** (-0.5)

    @pl.when(b == 0)
    def _():
        dk_ref[...] = jnp.zeros_like(dk_ref)
        dv_ref[...] = jnp.zeros_like(dv_ref)

    q = q_ref[0]
    g = g_ref[0]
    used = 4 + count_ref[0]
    chosen = [table_ref[b * slot_count + j] for j in range(slot_count)]
    keys = [k_ref[c] for c in chosen]
    vals = [v_ref[c] for c in chosen]
    nt = (((1,), (1,)), ((), ()))
    tn = (((0,), (0,)), ((), ()))
    scores = []
    for j in range(slot_count):
        s = lax.dot_general(q, keys[j], nt, preferred_element_type=jnp.float32) * score_scale
        if j >= 4:
            s = jnp.where(j < used, s, masked_score)
        scores.append(s)
    highest = scores[0].max(axis=-1, keepdims=True)
    for s in scores[1:]:
        highest = jnp.maximum(highest, s.max(axis=-1, keepdims=True))
    exps = [jnp.exp(s - highest) for s in scores]
    denom = exps[0].sum(axis=-1, keepdims=True)
    for e in exps[1:]:
        denom = denom + e.sum(axis=-1, keepdims=True)
    shares = [e / denom for e in exps]
    shares_low = [p.astype(jnp.bfloat16) for p in shares]
    attended = jnp.dot(shares_low[0], vals[0], preferred_element_type=jnp.float32)
    for j in range(1, slot_count):
        attended = attended + jnp.dot(shares_low[j], vals[j], preferred_element_type=jnp.float32)
    out_ref[0] = attended.astype(out_ref.dtype)
    grad_shares = [lax.dot_general(g, vals[j], nt, preferred_element_type=jnp.float32)
                   for j in range(slot_count)]
    weighted = (grad_shares[0] * shares[0]).sum(axis=-1, keepdims=True)
    for j in range(1, slot_count):
        weighted = weighted + (grad_shares[j] * shares[j]).sum(axis=-1, keepdims=True)
    grad_scores = [(shares[j] * (grad_shares[j] - weighted)).astype(jnp.bfloat16)
                   for j in range(slot_count)]
    grad_query = jnp.dot(grad_scores[0], keys[0], preferred_element_type=jnp.float32)
    for j in range(1, slot_count):
        grad_query = grad_query + jnp.dot(grad_scores[j], keys[j], preferred_element_type=jnp.float32)
    gq_ref[0] = (grad_query * score_scale).astype(gq_ref.dtype)
    for j in range(slot_count):
        dk = lax.dot_general(grad_scores[j], q, tn, preferred_element_type=jnp.float32) * score_scale
        dv = lax.dot_general(shares_low[j], g, tn, preferred_element_type=jnp.float32)
        dk_ref[chosen[j]] += dk
        dv_ref[chosen[j]] += dv


def head_pass(queries, key_rows, value_rows, grad_head, blocks, extra_count):
    seq_len, head_width = queries.shape
    block_count, slot_count = blocks.shape
    block_len = seq_len // block_count
    tiles = (block_count, block_len, head_width)
    one_block = pl.BlockSpec((1, block_len, head_width), lambda b, t, c: (b, 0, 0))
    whole = pl.BlockSpec(tiles, lambda b, t, c: (0, 0, 0))
    grid_spec = pltpu.PrefetchScalarGridSpec(
        num_scalar_prefetch=2,
        grid=(block_count,),
        in_specs=[one_block, one_block, whole, whole],
        out_specs=[one_block, one_block, whole, whole],
    )
    flops = 2 * seq_len * slot_count * block_len * head_width * 6
    attended, grad_query, grad_k, grad_v = pl.pallas_call(
        head_kernel,
        grid_spec=grid_spec,
        out_shape=[
            jax.ShapeDtypeStruct(tiles, jnp.bfloat16),
            jax.ShapeDtypeStruct(tiles, jnp.bfloat16),
            jax.ShapeDtypeStruct(tiles, jnp.float32),
            jax.ShapeDtypeStruct(tiles, jnp.float32),
        ],
        compiler_params=pltpu.CompilerParams(dimension_semantics=("arbitrary",)),
        cost_estimate=pl.CostEstimate(
            flops=flops,
            transcendentals=seq_len * slot_count * block_len,
            bytes_accessed=seq_len * head_width * 2 * 6 + seq_len * head_width * 4 * 2,
        ),
    )(
        blocks.reshape(-1),
        jnp.reshape(extra_count, (1,)),
        queries.reshape(tiles),
        grad_head.reshape(tiles),
        key_rows.reshape(tiles),
        value_rows.reshape(tiles),
    )
    summed = jnp.concatenate([grad_k, grad_v], axis=-1)
    return (
        attended.reshape(seq_len, head_width),
        grad_query.reshape(seq_len, head_width),
        summed.reshape(seq_len, 2 * head_width),
    )


def ring_reduce_scatter(chunk, ring, stride, position):
    seq_devices = lax.axis_size("seq")
    group = ring * stride
    me = (position // stride) % ring
    ahead = [
        (s, (s // group) * group + (((s // stride) % ring + 1) % ring) * stride + s % stride)
        for s in range(seq_devices)
    ]
    behind = [(b, a) for (a, b) in ahead]
    total = []
    for side, perm, sign in ((0, ahead, 1), (1, behind, -1)):
        buf = chunk((me - sign) % ring, side)
        for k in range(ring - 1):
            got = lax.ppermute(buf, "seq", perm)
            own = chunk((me - sign * (2 + k)) % ring, side)
            buf = (got.astype(jnp.float32) + own.astype(jnp.float32)).astype(jnp.bfloat16)
        total.append(buf)
    return jnp.concatenate(total, axis=-1)


def direct_sum(pieces, axis_name, size, stride, mine):
    devices = lax.axis_size(axis_name)
    group = size * stride
    got = [lax.dynamic_index_in_dim(pieces, mine, 0, keepdims=False)]
    for d in range(1, size):
        perm = [
            (i, (i // group) * group + (((i // stride) % size + d) % size) * stride + i % stride)
            for i in range(devices)
        ]
        got.append(lax.ppermute(
            lax.dynamic_index_in_dim(pieces, (mine + d) % size, 0, keepdims=False), axis_name, perm
        ))
    return got


def per_device(activations, w_query, w_key, w_value, key_blocks, random_count, grad_out):
    seq_devices = lax.axis_size("seq")
    dp_devices = lax.axis_size("dp")
    position = lax.axis_index("seq")
    dp_index = lax.axis_index("dp")
    tokens = activations[0]
    grad_rows = grad_out[0]
    tok_count = tokens.shape[0]
    heads = w_query.shape[1] // HD
    kv_heads = w_key.shape[1] // HD
    query_cols = heads * HD
    kv_cols = kv_heads * HD
    all_cols = query_cols + 2 * kv_cols
    w_local = jnp.concatenate([w_query, w_key, w_value], axis=1)
    half = all_cols // 2
    core = dp_index % 2
    pairs = [(i, i ^ 1) for i in range(dp_devices)]
    grad_pieces = grad_rows.reshape(tok_count, heads, HD).transpose(1, 0, 2)
    head_grad = lax.all_to_all(grad_pieces, "seq", split_axis=0, concat_axis=1, tiled=True)[0]
    w_mine = lax.all_gather(
        lax.dynamic_slice_in_dim(w_local, core * half, half, axis=1), "seq", axis=0, tiled=True
    )
    w_other = lax.ppermute(w_mine, "dp", pairs)
    proj_mine = jnp.dot(tokens, w_mine, preferred_element_type=jnp.float32).astype(jnp.bfloat16)
    proj_other = jnp.dot(tokens, w_other, preferred_element_type=jnp.float32).astype(jnp.bfloat16)
    projected = jnp.zeros((tok_count, all_cols), jnp.bfloat16)
    projected = lax.dynamic_update_slice_in_dim(projected, proj_mine, core * half, axis=1)
    projected = lax.dynamic_update_slice_in_dim(projected, proj_other, (1 - core) * half, axis=1)
    queries = projected[:, :query_cols]
    key_proj = projected[:, query_cols : query_cols + kv_cols]
    value_proj = projected[:, query_cols + kv_cols :]
    query_pieces = queries.reshape(tok_count, heads, HD).transpose(1, 0, 2)
    paired = jnp.concatenate(
        [key_proj.reshape(tok_count, kv_heads, HD), value_proj.reshape(tok_count, kv_heads, HD)],
        axis=2,
    )
    kv_pieces = jnp.repeat(paired.transpose(1, 0, 2), GROUP, axis=0)
    sent = jnp.concatenate([query_pieces, kv_pieces], axis=2)
    landed = lax.all_to_all(sent, "seq", split_axis=0, concat_axis=1, tiled=True)[0]
    head_q = landed[:, :HD]
    head_k = landed[:, HD : 2 * HD]
    head_v = landed[:, 2 * HD :]
    blocks_mine = lax.dynamic_index_in_dim(key_blocks, position, 0, keepdims=False)
    count_mine = lax.dynamic_index_in_dim(random_count, position, 0, keepdims=False)
    attended, grad_query, grad_kv = head_pass(
        head_q, head_k, head_v, head_grad, blocks_mine, count_mine
    )
    back_sent = jnp.concatenate(
        [
            attended.reshape(seq_devices, tok_count, HD),
            grad_query.reshape(seq_devices, tok_count, HD),
            grad_kv.astype(jnp.bfloat16).reshape(seq_devices, tok_count, 2 * HD),
        ],
        axis=2,
    )
    back = lax.all_to_all(back_sent, "seq", split_axis=0, concat_axis=0, tiled=True)
    back_out = back[:, :, :HD]
    back_query = back[:, :, HD : 2 * HD]
    back_kv = back[:, :, 2 * HD :]
    out_rows = back_out.transpose(1, 0, 2).reshape(tok_count, heads * HD)
    grad_q_rows = back_query.transpose(1, 0, 2).reshape(tok_count, heads * HD)
    kv_sum = jnp.sum(
        back_kv.reshape(kv_heads, GROUP, tok_count, 2 * HD), axis=1, dtype=jnp.float32
    ).astype(jnp.bfloat16)
    grad_k_rows = kv_sum[:, :, :HD].transpose(1, 0, 2).reshape(tok_count, kv_heads * HD)
    grad_v_rows = kv_sum[:, :, HD:].transpose(1, 0, 2).reshape(tok_count, kv_heads * HD)
    combined = jnp.concatenate([grad_q_rows, grad_k_rows, grad_v_rows], axis=1)
    contract = (((1,), (1,)), ((), ()))
    comb_mine = lax.dynamic_slice_in_dim(combined, core * half, half, axis=1)
    comb_other = lax.dynamic_slice_in_dim(combined, (1 - core) * half, half, axis=1)
    grad_x_rows = (
        lax.dot_general(comb_mine, w_mine, contract, preferred_element_type=jnp.float32)
        + lax.dot_general(comb_other, w_other, contract, preferred_element_type=jnp.float32)
    ).astype(jnp.bfloat16)
    factor = 1.0 / math.sqrt(tok_count * seq_devices * dp_devices)
    over_tokens = (((0,), (0,)), ((), ()))
    y_count = seq_devices // RING_Z
    rows = tokens.shape[1] // seq_devices
    tokens_zy = (
        tokens.reshape(tok_count, y_count, RING_Z, rows).transpose(0, 2, 1, 3).reshape(tok_count, -1)
    )

    def term_of(columns):
        return (
            lax.dot_general(tokens_zy, columns, over_tokens, preferred_element_type=jnp.float32)
            * factor
        ).astype(jnp.bfloat16)

    got = lax.ppermute(term_of(comb_other), "dp", pairs)
    keep = term_of(comb_mine)
    grad_x_rows, keep = lax.optimization_barrier((grad_x_rows, keep))
    keep4 = keep.reshape(RING_Z, y_count, rows, half)
    got4 = got.reshape(RING_Z, y_count, rows, half)
    quarter = half // 2

    def chip_chunk(i, side):
        a = lax.dynamic_index_in_dim(keep4, i, 0, keepdims=False)[..., side * quarter : (side + 1) * quarter]
        b = lax.dynamic_index_in_dim(got4, i, 0, keepdims=False)[..., side * quarter : (side + 1) * quarter]
        return (a.astype(jnp.float32) + b.astype(jnp.float32)).astype(jnp.bfloat16)

    by_y = ring_reduce_scatter(chip_chunk, RING_Z, 1, position)
    from_y = direct_sum(by_y, "seq", y_count, RING_Z, position // RING_Z)
    total = from_y[0].astype(jnp.float32)
    for piece in from_y[1:]:
        total = total + piece.astype(jnp.float32)
    part = total.astype(jnp.bfloat16)
    chips = dp_devices // 2
    chip = dp_index // 2
    from_x = direct_sum(jnp.broadcast_to(part, (chips,) + part.shape), "dp", chips, 2, chip)
    by_offset = jnp.stack(from_x)
    in_order = jnp.take(by_offset, (chip - jnp.arange(chips)) % chips, axis=0)
    part = jnp.sum(in_order.astype(jnp.float32), axis=0).astype(jnp.bfloat16)
    other_half = lax.ppermute(part, "dp", pairs)
    first = jnp.where(core == 0, part, other_half)
    second = jnp.where(core == 0, other_half, part)
    grad_all = jnp.concatenate([first, second], axis=1)
    grad_wq = grad_all[:, :query_cols]
    grad_wk = grad_all[:, query_cols : query_cols + kv_cols]
    grad_wv = grad_all[:, query_cols + kv_cols :]
    return (out_rows[None], grad_x_rows[None], grad_wq, grad_wk, grad_wv)


def solution(mesh):
    placed = (
        P("dp", "seq", None),
        P("seq", None),
        P("seq", None),
        P("seq", None),
        P(),
        P(),
        P("dp", "seq", None),
    )
    return jax.shard_map(
        per_device,
        mesh=mesh,
        in_specs=placed,
        out_specs=(
            P("dp", "seq", None),
            P("dp", "seq", None),
            P("seq", None),
            P("seq", None),
            P("seq", None),
        ),
        check_vma=False,
    )
```

```python
import math

import jax
import jax.numpy as jnp
from jax import lax
from jax.experimental import pallas as pl
from jax.experimental.pallas import tpu as pltpu
from jax.sharding import PartitionSpec as P

HD = 64
GROUP = 8


masked_score = -1e30
query_group = 4
RING_Z = 8


def head_kernel(table_ref, count_ref, q_ref, g_ref, k_ref, v_ref,
                out_ref, gq_ref, dk_ref, dv_ref):
    b = pl.program_id(0)
    slot_count = table_ref.shape[0] // pl.num_programs(0)
    head_width = q_ref.shape[-1]
    score_scale = head_width ** (-0.5)

    @pl.when(b == 0)
    def _():
        dk_ref[...] = jnp.zeros_like(dk_ref)
        dv_ref[...] = jnp.zeros_like(dv_ref)

    q = q_ref[0]
    g = g_ref[0]
    used = 4 + count_ref[0]
    chosen = [table_ref[b * slot_count + j] for j in range(slot_count)]
    keys = [k_ref[c] for c in chosen]
    vals = [v_ref[c] for c in chosen]
    nt = (((1,), (1,)), ((), ()))
    tn = (((0,), (0,)), ((), ()))
    scores = []
    for j in range(slot_count):
        s = lax.dot_general(q, keys[j], nt, preferred_element_type=jnp.float32) * score_scale
        if j >= 4:
            s = jnp.where(j < used, s, masked_score)
        scores.append(s)
    highest = scores[0].max(axis=-1, keepdims=True)
    for s in scores[1:]:
        highest = jnp.maximum(highest, s.max(axis=-1, keepdims=True))
    exps = [jnp.exp(s - highest) for s in scores]
    denom = exps[0].sum(axis=-1, keepdims=True)
    for e in exps[1:]:
        denom = denom + e.sum(axis=-1, keepdims=True)
    shares = [e / denom for e in exps]
    shares_low = [p.astype(jnp.bfloat16) for p in shares]
    attended = jnp.dot(shares_low[0], vals[0], preferred_element_type=jnp.float32)
    for j in range(1, slot_count):
        attended = attended + jnp.dot(shares_low[j], vals[j], preferred_element_type=jnp.float32)
    out_ref[0] = attended.astype(out_ref.dtype)
    grad_shares = [lax.dot_general(g, vals[j], nt, preferred_element_type=jnp.float32)
                   for j in range(slot_count)]
    weighted = (grad_shares[0] * shares[0]).sum(axis=-1, keepdims=True)
    for j in range(1, slot_count):
        weighted = weighted + (grad_shares[j] * shares[j]).sum(axis=-1, keepdims=True)
    grad_scores = [(shares[j] * (grad_shares[j] - weighted)).astype(jnp.bfloat16)
                   for j in range(slot_count)]
    grad_query = jnp.dot(grad_scores[0], keys[0], preferred_element_type=jnp.float32)
    for j in range(1, slot_count):
        grad_query = grad_query + jnp.dot(grad_scores[j], keys[j], preferred_element_type=jnp.float32)
    gq_ref[0] = (grad_query * score_scale).astype(gq_ref.dtype)
    for j in range(slot_count):
        dk = lax.dot_general(grad_scores[j], q, tn, preferred_element_type=jnp.float32) * score_scale
        dv = lax.dot_general(shares_low[j], g, tn, preferred_element_type=jnp.float32)
        dk_ref[chosen[j]] += dk
        dv_ref[chosen[j]] += dv


def head_pass(queries, key_rows, value_rows, grad_head, blocks, extra_count):
    seq_len, head_width = queries.shape
    block_count, slot_count = blocks.shape
    block_len = seq_len // block_count
    tiles = (block_count, block_len, head_width)
    one_block = pl.BlockSpec((1, block_len, head_width), lambda b, t, c: (b, 0, 0))
    whole = pl.BlockSpec(tiles, lambda b, t, c: (0, 0, 0))
    grid_spec = pltpu.PrefetchScalarGridSpec(
        num_scalar_prefetch=2,
        grid=(block_count,),
        in_specs=[one_block, one_block, whole, whole],
        out_specs=[one_block, one_block, whole, whole],
    )
    flops = 2 * seq_len * slot_count * block_len * head_width * 6
    attended, grad_query, grad_k, grad_v = pl.pallas_call(
        head_kernel,
        grid_spec=grid_spec,
        out_shape=[
            jax.ShapeDtypeStruct(tiles, jnp.bfloat16),
            jax.ShapeDtypeStruct(tiles, jnp.bfloat16),
            jax.ShapeDtypeStruct(tiles, jnp.float32),
            jax.ShapeDtypeStruct(tiles, jnp.float32),
        ],
        compiler_params=pltpu.CompilerParams(dimension_semantics=("arbitrary",)),
        cost_estimate=pl.CostEstimate(
            flops=flops,
            transcendentals=seq_len * slot_count * block_len,
            bytes_accessed=seq_len * head_width * 2 * 6 + seq_len * head_width * 4 * 2,
        ),
    )(
        blocks.reshape(-1),
        jnp.reshape(extra_count, (1,)),
        queries.reshape(tiles),
        grad_head.reshape(tiles),
        key_rows.reshape(tiles),
        value_rows.reshape(tiles),
    )
    summed = jnp.concatenate([grad_k, grad_v], axis=-1)
    return (
        attended.reshape(seq_len, head_width),
        grad_query.reshape(seq_len, head_width),
        summed.reshape(seq_len, 2 * head_width),
    )


def ring_reduce_scatter(chunk, ring, stride, position):
    seq_devices = lax.axis_size("seq")
    group = ring * stride
    me = (position // stride) % ring
    ahead = [
        (s, (s // group) * group + (((s // stride) % ring + 1) % ring) * stride + s % stride)
        for s in range(seq_devices)
    ]
    behind = [(b, a) for (a, b) in ahead]
    total = []
    for side, perm, sign in ((0, ahead, 1), (1, behind, -1)):
        buf = chunk((me - sign) % ring, side)
        for k in range(ring - 1):
            got = lax.ppermute(buf, "seq", perm)
            own = chunk((me - sign * (2 + k)) % ring, side)
            buf = (got.astype(jnp.float32) + own.astype(jnp.float32)).astype(jnp.bfloat16)
        total.append(buf)
    return jnp.concatenate(total, axis=-1)


def direct_sum(pieces, axis_name, size, stride, mine):
    devices = lax.axis_size(axis_name)
    group = size * stride
    got = [lax.dynamic_index_in_dim(pieces, mine, 0, keepdims=False)]
    for d in range(1, size):
        perm = [
            (i, (i // group) * group + (((i // stride) % size + d) % size) * stride + i % stride)
            for i in range(devices)
        ]
        got.append(lax.ppermute(
            lax.dynamic_index_in_dim(pieces, (mine + d) % size, 0, keepdims=False), axis_name, perm
        ))
    return got


def per_device(activations, w_query, w_key, w_value, key_blocks, random_count, grad_out):
    seq_devices = lax.axis_size("seq")
    dp_devices = lax.axis_size("dp")
    position = lax.axis_index("seq")
    dp_index = lax.axis_index("dp")
    tokens = activations[0]
    grad_rows = grad_out[0]
    tok_count = tokens.shape[0]
    heads = w_query.shape[1] // HD
    kv_heads = w_key.shape[1] // HD
    query_cols = heads * HD
    kv_cols = kv_heads * HD
    all_cols = query_cols + 2 * kv_cols
    w_local = jnp.concatenate([w_query, w_key, w_value], axis=1)
    half = all_cols // 2
    core = dp_index % 2
    pairs = [(i, i ^ 1) for i in range(dp_devices)]
    grad_pieces = grad_rows.reshape(tok_count, heads, HD).transpose(1, 0, 2)
    head_grad = lax.all_to_all(grad_pieces, "seq", split_axis=0, concat_axis=1, tiled=True)[0]
    w_mine = lax.all_gather(
        lax.dynamic_slice_in_dim(w_local, core * half, half, axis=1), "seq", axis=0, tiled=True
    )
    w_other = lax.ppermute(w_mine, "dp", pairs)
    proj_mine = jnp.dot(tokens, w_mine, preferred_element_type=jnp.float32).astype(jnp.bfloat16)
    proj_other = jnp.dot(tokens, w_other, preferred_element_type=jnp.float32).astype(jnp.bfloat16)
    projected = jnp.zeros((tok_count, all_cols), jnp.bfloat16)
    projected = lax.dynamic_update_slice_in_dim(projected, proj_mine, core * half, axis=1)
    projected = lax.dynamic_update_slice_in_dim(projected, proj_other, (1 - core) * half, axis=1)
    queries = projected[:, :query_cols]
    key_proj = projected[:, query_cols : query_cols + kv_cols]
    value_proj = projected[:, query_cols + kv_cols :]
    query_pieces = queries.reshape(tok_count, heads, HD).transpose(1, 0, 2)
    paired = jnp.concatenate(
        [key_proj.reshape(tok_count, kv_heads, HD), value_proj.reshape(tok_count, kv_heads, HD)],
        axis=2,
    )
    kv_pieces = jnp.repeat(paired.transpose(1, 0, 2), GROUP, axis=0)
    sent = jnp.concatenate([query_pieces, kv_pieces], axis=2)
    landed = lax.all_to_all(sent, "seq", split_axis=0, concat_axis=1, tiled=True)[0]
    head_q = landed[:, :HD]
    head_k = landed[:, HD : 2 * HD]
    head_v = landed[:, 2 * HD :]
    blocks_mine = lax.dynamic_index_in_dim(key_blocks, position, 0, keepdims=False)
    count_mine = lax.dynamic_index_in_dim(random_count, position, 0, keepdims=False)
    attended, grad_query, grad_kv = head_pass(
        head_q, head_k, head_v, head_grad, blocks_mine, count_mine
    )
    back_sent = jnp.concatenate(
        [
            attended.reshape(seq_devices, tok_count, HD),
            grad_query.reshape(seq_devices, tok_count, HD),
            grad_kv.astype(jnp.bfloat16).reshape(seq_devices, tok_count, 2 * HD),
        ],
        axis=2,
    )
    back = lax.all_to_all(back_sent, "seq", split_axis=0, concat_axis=0, tiled=True)
    back_out = back[:, :, :HD]
    back_query = back[:, :, HD : 2 * HD]
    back_kv = back[:, :, 2 * HD :]
    out_rows = back_out.transpose(1, 0, 2).reshape(tok_count, heads * HD)
    grad_q_rows = back_query.transpose(1, 0, 2).reshape(tok_count, heads * HD)
    kv_sum = jnp.sum(
        back_kv.reshape(kv_heads, GROUP, tok_count, 2 * HD), axis=1, dtype=jnp.float32
    ).astype(jnp.bfloat16)
    grad_k_rows = kv_sum[:, :, :HD].transpose(1, 0, 2).reshape(tok_count, kv_heads * HD)
    grad_v_rows = kv_sum[:, :, HD:].transpose(1, 0, 2).reshape(tok_count, kv_heads * HD)
    combined = jnp.concatenate([grad_q_rows, grad_k_rows, grad_v_rows], axis=1)
    contract = (((1,), (1,)), ((), ()))
    comb_mine = lax.dynamic_slice_in_dim(combined, core * half, half, axis=1)
    comb_other = lax.dynamic_slice_in_dim(combined, (1 - core) * half, half, axis=1)
    grad_x_rows = (
        lax.dot_general(comb_mine, w_mine, contract, preferred_element_type=jnp.float32)
        + lax.dot_general(comb_other, w_other, contract, preferred_element_type=jnp.float32)
    ).astype(jnp.bfloat16)
    factor = 1.0 / math.sqrt(tok_count * seq_devices * dp_devices)
    over_tokens = (((0,), (0,)), ((), ()))
    y_count = seq_devices // RING_Z
    rows = tokens.shape[1] // seq_devices
    span = y_count * rows
    quarter = half // 2
    tok4 = tokens.reshape(tok_count, y_count, RING_Z, rows)
    z_me = position % RING_Z

    def ring_tokens(sign):
        order = (z_me - sign * (1 + jnp.arange(RING_Z))) % RING_Z
        return jnp.take(tok4, order, axis=2).transpose(0, 2, 1, 3).reshape(tok_count, -1)

    def term_t(columns, toks):
        return (
            lax.dot_general(columns, toks, over_tokens, preferred_element_type=jnp.float32)
            * factor
        ).astype(jnp.bfloat16)

    signs = (1, -1)
    toks = [ring_tokens(sign) for sign in signs]
    give = jnp.stack(
        [term_t(comb_other[:, i * quarter : (i + 1) * quarter], toks[i]) for i in range(2)]
    )
    got = lax.ppermute(give, "dp", pairs)
    keep = [term_t(comb_mine[:, i * quarter : (i + 1) * quarter], toks[i]) for i in range(2)]
    grad_x_rows, keep = lax.optimization_barrier((grad_x_rows, keep))
    ahead = [(s, (s // RING_Z) * RING_Z + (s % RING_Z + 1) % RING_Z) for s in range(seq_devices)]
    behind = [(b, a) for (a, b) in ahead]
    ends = []
    for i, perm in enumerate((ahead, behind)):

        def chunk(k):
            piece = slice(k * span, (k + 1) * span)
            return (
                keep[i][:, piece].astype(jnp.float32) + got[i][:, piece].astype(jnp.float32)
            ).astype(jnp.bfloat16)

        buf = chunk(0)
        for k in range(RING_Z - 1):
            arrived = lax.ppermute(buf, "seq", perm)
            buf = (arrived.astype(jnp.float32) + chunk(k + 1).astype(jnp.float32)).astype(jnp.bfloat16)
        ends.append(buf)
    by_y = jnp.concatenate(ends, axis=0).reshape(half, y_count, rows).transpose(1, 2, 0)
    from_y = direct_sum(by_y, "seq", y_count, RING_Z, position // RING_Z)
    total = from_y[0].astype(jnp.float32)
    for piece in from_y[1:]:
        total = total + piece.astype(jnp.float32)
    part = total.astype(jnp.bfloat16)
    chips = dp_devices // 2
    chip = dp_index // 2
    from_x = direct_sum(jnp.broadcast_to(part, (chips,) + part.shape), "dp", chips, 2, chip)
    by_offset = jnp.stack(from_x)
    in_order = jnp.take(by_offset, (chip - jnp.arange(chips)) % chips, axis=0)
    part = jnp.sum(in_order.astype(jnp.float32), axis=0).astype(jnp.bfloat16)
    other_half = lax.ppermute(part, "dp", pairs)
    first = jnp.where(core == 0, part, other_half)
    second = jnp.where(core == 0, other_half, part)
    grad_all = jnp.concatenate([first, second], axis=1)
    grad_wq = grad_all[:, :query_cols]
    grad_wk = grad_all[:, query_cols : query_cols + kv_cols]
    grad_wv = grad_all[:, query_cols + kv_cols :]
    return (out_rows[None], grad_x_rows[None], grad_wq, grad_wk, grad_wv)


def solution(mesh):
    placed = (
        P("dp", "seq", None),
        P("seq", None),
        P("seq", None),
        P("seq", None),
        P(),
        P(),
        P("dp", "seq", None),
    )
    return jax.shard_map(
        per_device,
        mesh=mesh,
        in_specs=placed,
        out_specs=(
            P("dp", "seq", None),
            P("dp", "seq", None),
            P("seq", None),
            P("seq", None),
            P("seq", None),
        ),
        check_vma=False,
    )
```

```python
import math

import jax
import jax.numpy as jnp
from jax import lax
from jax.experimental import pallas as pl
from jax.experimental.pallas import tpu as pltpu
from jax.sharding import PartitionSpec as P

HD = 64
GROUP = 8


masked_score = -1e30
query_group = 4
RING_Z = 8


def head_kernel(table_ref, count_ref, q_ref, g_ref, k_ref, v_ref,
                out_ref, gq_ref, dk_ref, dv_ref, k_cat, v_cat):
    b = pl.program_id(0)
    slot_count = table_ref.shape[0] // pl.num_programs(0)
    block_len = q_ref.shape[1]
    head_width = q_ref.shape[-1]
    score_scale = head_width ** (-0.5)

    @pl.when(b == 0)
    def _():
        dk_ref[...] = jnp.zeros_like(dk_ref)
        dv_ref[...] = jnp.zeros_like(dv_ref)

    q = q_ref[0]
    g = g_ref[0]
    used = 4 + count_ref[0]
    chosen = [table_ref[b * slot_count + j] for j in range(slot_count)]
    for j in range(slot_count):
        k_cat[j * block_len : (j + 1) * block_len, :] = k_ref[chosen[j]]
        v_cat[j * block_len : (j + 1) * block_len, :] = v_ref[chosen[j]]
    keys = k_cat[...]
    vals = v_cat[...]
    nt = (((1,), (1,)), ((), ()))
    tn = (((0,), (0,)), ((), ()))
    scores = lax.dot_general(q, keys, nt, preferred_element_type=jnp.float32) * score_scale
    slot_of = lax.broadcasted_iota(jnp.int32, (1, slot_count * block_len), 1) // block_len
    scores = jnp.where(slot_of < used, scores, masked_score)
    highest = scores.max(axis=-1, keepdims=True)
    exps = jnp.exp(scores - highest)
    shares = exps / exps.sum(axis=-1, keepdims=True)
    shares_low = shares.astype(jnp.bfloat16)
    attended = jnp.dot(shares_low, vals, preferred_element_type=jnp.float32)
    out_ref[0] = attended.astype(out_ref.dtype)
    grad_shares = lax.dot_general(g, vals, nt, preferred_element_type=jnp.float32)
    weighted = (grad_shares * shares).sum(axis=-1, keepdims=True)
    grad_scores = (shares * (grad_shares - weighted)).astype(jnp.bfloat16)
    grad_query = jnp.dot(grad_scores, keys, preferred_element_type=jnp.float32)
    gq_ref[0] = (grad_query * score_scale).astype(gq_ref.dtype)
    dk = lax.dot_general(grad_scores, q, tn, preferred_element_type=jnp.float32) * score_scale
    dv = lax.dot_general(shares_low, g, tn, preferred_element_type=jnp.float32)
    for j in range(slot_count):
        dk_ref[chosen[j]] += dk[j * block_len : (j + 1) * block_len]
        dv_ref[chosen[j]] += dv[j * block_len : (j + 1) * block_len]


def head_pass(queries, key_rows, value_rows, grad_head, blocks, extra_count):
    seq_len, head_width = queries.shape
    block_count, slot_count = blocks.shape
    block_len = seq_len // block_count
    tiles = (block_count, block_len, head_width)
    one_block = pl.BlockSpec((1, block_len, head_width), lambda b, t, c: (b, 0, 0))
    whole = pl.BlockSpec(tiles, lambda b, t, c: (0, 0, 0))
    grid_spec = pltpu.PrefetchScalarGridSpec(
        num_scalar_prefetch=2,
        grid=(block_count,),
        in_specs=[one_block, one_block, whole, whole],
        out_specs=[one_block, one_block, whole, whole],
        scratch_shapes=[
            pltpu.VMEM((slot_count * block_len, head_width), jnp.bfloat16),
            pltpu.VMEM((slot_count * block_len, head_width), jnp.bfloat16),
        ],
    )
    flops = 2 * seq_len * slot_count * block_len * head_width * 6
    attended, grad_query, grad_k, grad_v = pl.pallas_call(
        head_kernel,
        grid_spec=grid_spec,
        out_shape=[
            jax.ShapeDtypeStruct(tiles, jnp.bfloat16),
            jax.ShapeDtypeStruct(tiles, jnp.bfloat16),
            jax.ShapeDtypeStruct(tiles, jnp.float32),
            jax.ShapeDtypeStruct(tiles, jnp.float32),
        ],
        compiler_params=pltpu.CompilerParams(dimension_semantics=("arbitrary",)),
        cost_estimate=pl.CostEstimate(
            flops=flops,
            transcendentals=seq_len * slot_count * block_len,
            bytes_accessed=seq_len * head_width * 2 * 6 + seq_len * head_width * 4 * 2,
        ),
    )(
        blocks.reshape(-1),
        jnp.reshape(extra_count, (1,)),
        queries.reshape(tiles),
        grad_head.reshape(tiles),
        key_rows.reshape(tiles),
        value_rows.reshape(tiles),
    )
    summed = jnp.concatenate([grad_k, grad_v], axis=-1)
    return (
        attended.reshape(seq_len, head_width),
        grad_query.reshape(seq_len, head_width),
        summed.reshape(seq_len, 2 * head_width),
    )


def ring_reduce_scatter(chunk, ring, stride, position):
    seq_devices = lax.axis_size("seq")
    group = ring * stride
    me = (position // stride) % ring
    ahead = [
        (s, (s // group) * group + (((s // stride) % ring + 1) % ring) * stride + s % stride)
        for s in range(seq_devices)
    ]
    behind = [(b, a) for (a, b) in ahead]
    total = []
    for side, perm, sign in ((0, ahead, 1), (1, behind, -1)):
        buf = chunk((me - sign) % ring, side)
        for k in range(ring - 1):
            got = lax.ppermute(buf, "seq", perm)
            own = chunk((me - sign * (2 + k)) % ring, side)
            buf = (got.astype(jnp.float32) + own.astype(jnp.float32)).astype(jnp.bfloat16)
        total.append(buf)
    return jnp.concatenate(total, axis=-1)


def direct_sum(pieces, axis_name, size, stride, mine):
    devices = lax.axis_size(axis_name)
    group = size * stride
    got = [lax.dynamic_index_in_dim(pieces, mine, 0, keepdims=False)]
    for d in range(1, size):
        perm = [
            (i, (i // group) * group + (((i // stride) % size + d) % size) * stride + i % stride)
            for i in range(devices)
        ]
        got.append(lax.ppermute(
            lax.dynamic_index_in_dim(pieces, (mine + d) % size, 0, keepdims=False), axis_name, perm
        ))
    return got


def per_device(activations, w_query, w_key, w_value, key_blocks, random_count, grad_out):
    seq_devices = lax.axis_size("seq")
    dp_devices = lax.axis_size("dp")
    position = lax.axis_index("seq")
    dp_index = lax.axis_index("dp")
    tokens = activations[0]
    grad_rows = grad_out[0]
    tok_count = tokens.shape[0]
    heads = w_query.shape[1] // HD
    kv_heads = w_key.shape[1] // HD
    query_cols = heads * HD
    kv_cols = kv_heads * HD
    all_cols = query_cols + 2 * kv_cols
    w_local = jnp.concatenate([w_query, w_key, w_value], axis=1)
    half = all_cols // 2
    core = dp_index % 2
    pairs = [(i, i ^ 1) for i in range(dp_devices)]
    grad_pieces = grad_rows.reshape(tok_count, heads, HD).transpose(1, 0, 2)
    head_grad = lax.all_to_all(grad_pieces, "seq", split_axis=0, concat_axis=1, tiled=True)[0]
    w_mine = lax.all_gather(
        lax.dynamic_slice_in_dim(w_local, core * half, half, axis=1), "seq", axis=0, tiled=True
    )
    w_other = lax.ppermute(w_mine, "dp", pairs)
    proj_mine = jnp.dot(tokens, w_mine, preferred_element_type=jnp.float32).astype(jnp.bfloat16)
    proj_other = jnp.dot(tokens, w_other, preferred_element_type=jnp.float32).astype(jnp.bfloat16)
    projected = jnp.zeros((tok_count, all_cols), jnp.bfloat16)
    projected = lax.dynamic_update_slice_in_dim(projected, proj_mine, core * half, axis=1)
    projected = lax.dynamic_update_slice_in_dim(projected, proj_other, (1 - core) * half, axis=1)
    queries = projected[:, :query_cols]
    key_proj = projected[:, query_cols : query_cols + kv_cols]
    value_proj = projected[:, query_cols + kv_cols :]
    query_pieces = queries.reshape(tok_count, heads, HD).transpose(1, 0, 2)
    paired = jnp.concatenate(
        [key_proj.reshape(tok_count, kv_heads, HD), value_proj.reshape(tok_count, kv_heads, HD)],
        axis=2,
    )
    kv_pieces = jnp.repeat(paired.transpose(1, 0, 2), GROUP, axis=0)
    sent = jnp.concatenate([query_pieces, kv_pieces], axis=2)
    landed = lax.all_to_all(sent, "seq", split_axis=0, concat_axis=1, tiled=True)[0]
    head_q = landed[:, :HD]
    head_k = landed[:, HD : 2 * HD]
    head_v = landed[:, 2 * HD :]
    blocks_mine = lax.dynamic_index_in_dim(key_blocks, position, 0, keepdims=False)
    count_mine = lax.dynamic_index_in_dim(random_count, position, 0, keepdims=False)
    attended, grad_query, grad_kv = head_pass(
        head_q, head_k, head_v, head_grad, blocks_mine, count_mine
    )
    back_sent = jnp.concatenate(
        [
            attended.reshape(seq_devices, tok_count, HD),
            grad_query.reshape(seq_devices, tok_count, HD),
            grad_kv.astype(jnp.bfloat16).reshape(seq_devices, tok_count, 2 * HD),
        ],
        axis=2,
    )
    back = lax.all_to_all(back_sent, "seq", split_axis=0, concat_axis=0, tiled=True)
    back_out = back[:, :, :HD]
    back_query = back[:, :, HD : 2 * HD]
    back_kv = back[:, :, 2 * HD :]
    out_rows = back_out.transpose(1, 0, 2).reshape(tok_count, heads * HD)
    grad_q_rows = back_query.transpose(1, 0, 2).reshape(tok_count, heads * HD)
    kv_sum = jnp.sum(
        back_kv.reshape(kv_heads, GROUP, tok_count, 2 * HD), axis=1, dtype=jnp.float32
    ).astype(jnp.bfloat16)
    grad_k_rows = kv_sum[:, :, :HD].transpose(1, 0, 2).reshape(tok_count, kv_heads * HD)
    grad_v_rows = kv_sum[:, :, HD:].transpose(1, 0, 2).reshape(tok_count, kv_heads * HD)
    combined = jnp.concatenate([grad_q_rows, grad_k_rows, grad_v_rows], axis=1)
    contract = (((1,), (1,)), ((), ()))
    comb_mine = lax.dynamic_slice_in_dim(combined, core * half, half, axis=1)
    comb_other = lax.dynamic_slice_in_dim(combined, (1 - core) * half, half, axis=1)
    grad_x_rows = (
        lax.dot_general(comb_mine, w_mine, contract, preferred_element_type=jnp.float32)
        + lax.dot_general(comb_other, w_other, contract, preferred_element_type=jnp.float32)
    ).astype(jnp.bfloat16)
    factor = 1.0 / math.sqrt(tok_count * seq_devices * dp_devices)
    over_tokens = (((0,), (0,)), ((), ()))
    y_count = seq_devices // RING_Z
    rows = tokens.shape[1] // seq_devices
    span = y_count * rows
    quarter = half // 2
    tok4 = tokens.reshape(tok_count, y_count, RING_Z, rows)
    z_me = position % RING_Z

    def ring_tokens(sign):
        order = (z_me - sign * (1 + jnp.arange(RING_Z))) % RING_Z
        return jnp.take(tok4, order, axis=2).transpose(0, 2, 1, 3).reshape(tok_count, -1)

    def term_t(columns, toks):
        return (
            lax.dot_general(columns, toks, over_tokens, preferred_element_type=jnp.float32)
            * factor
        ).astype(jnp.bfloat16)

    signs = (1, -1)
    toks = [ring_tokens(sign) for sign in signs]
    give = jnp.stack(
        [term_t(comb_other[:, i * quarter : (i + 1) * quarter], toks[i]) for i in range(2)]
    )
    got = lax.ppermute(give, "dp", pairs)
    keep = [term_t(comb_mine[:, i * quarter : (i + 1) * quarter], toks[i]) for i in range(2)]
    grad_x_rows, keep = lax.optimization_barrier((grad_x_rows, keep))
    ahead = [(s, (s // RING_Z) * RING_Z + (s % RING_Z + 1) % RING_Z) for s in range(seq_devices)]
    behind = [(b, a) for (a, b) in ahead]
    ends = []
    for i, perm in enumerate((ahead, behind)):

        def chunk(k):
            piece = slice(k * span, (k + 1) * span)
            return (
                keep[i][:, piece].astype(jnp.float32) + got[i][:, piece].astype(jnp.float32)
            ).astype(jnp.bfloat16)

        buf = chunk(0)
        for k in range(RING_Z - 1):
            arrived = lax.ppermute(buf, "seq", perm)
            buf = (arrived.astype(jnp.float32) + chunk(k + 1).astype(jnp.float32)).astype(jnp.bfloat16)
        ends.append(buf)
    by_y = jnp.concatenate(ends, axis=0).reshape(half, y_count, rows).transpose(1, 2, 0)
    from_y = direct_sum(by_y, "seq", y_count, RING_Z, position // RING_Z)
    total = from_y[0].astype(jnp.float32)
    for piece in from_y[1:]:
        total = total + piece.astype(jnp.float32)
    part = total.astype(jnp.bfloat16)
    chips = dp_devices // 2
    chip = dp_index // 2
    from_x = direct_sum(jnp.broadcast_to(part, (chips,) + part.shape), "dp", chips, 2, chip)
    by_offset = jnp.stack(from_x)
    in_order = jnp.take(by_offset, (chip - jnp.arange(chips)) % chips, axis=0)
    part = jnp.sum(in_order.astype(jnp.float32), axis=0).astype(jnp.bfloat16)
    other_half = lax.ppermute(part, "dp", pairs)
    first = jnp.where(core == 0, part, other_half)
    second = jnp.where(core == 0, other_half, part)
    grad_all = jnp.concatenate([first, second], axis=1)
    grad_wq = grad_all[:, :query_cols]
    grad_wk = grad_all[:, query_cols : query_cols + kv_cols]
    grad_wv = grad_all[:, query_cols + kv_cols :]
    return (out_rows[None], grad_x_rows[None], grad_wq, grad_wk, grad_wv)


def solution(mesh):
    placed = (
        P("dp", "seq", None),
        P("seq", None),
        P("seq", None),
        P("seq", None),
        P(),
        P(),
        P("dp", "seq", None),
    )
    return jax.shard_map(
        per_device,
        mesh=mesh,
        in_specs=placed,
        out_specs=(
            P("dp", "seq", None),
            P("dp", "seq", None),
            P("seq", None),
            P("seq", None),
            P("seq", None),
        ),
        check_vma=False,
    )
```

```python
import math

import jax
import jax.numpy as jnp
from jax import lax
from jax.experimental import pallas as pl
from jax.experimental.pallas import tpu as pltpu
from jax.sharding import PartitionSpec as P

HD = 64
GROUP = 8


masked_score = -1e30
query_group = 4
RING_Z = 8


def head_kernel(table_ref, count_ref, q_ref, g_ref, k_ref, v_ref,
                out_ref, gq_ref, dk_ref, dv_ref, k_cat, v_cat):
    b = pl.program_id(0)
    slot_count = table_ref.shape[0] // pl.num_programs(0)
    block_len = q_ref.shape[1]
    head_width = q_ref.shape[-1]
    score_scale = head_width ** (-0.5)

    @pl.when(b == 0)
    def _():
        dk_ref[...] = jnp.zeros_like(dk_ref)
        dv_ref[...] = jnp.zeros_like(dv_ref)

    q = q_ref[0]
    g = g_ref[0]
    used = 4 + count_ref[0]
    chosen = [table_ref[b * slot_count + j] for j in range(slot_count)]
    for j in range(slot_count):
        k_cat[j * block_len : (j + 1) * block_len, :] = k_ref[chosen[j]]
        v_cat[j * block_len : (j + 1) * block_len, :] = v_ref[chosen[j]]
    keys = k_cat[...]
    vals = v_cat[...]
    nt = (((1,), (1,)), ((), ()))
    tn = (((0,), (0,)), ((), ()))
    scores = lax.dot_general(q, keys, nt, preferred_element_type=jnp.float32) * score_scale
    slot_of = lax.broadcasted_iota(jnp.int32, (1, slot_count * block_len), 1) // block_len
    scores = jnp.where(slot_of < used, scores, masked_score)
    highest = scores.max(axis=-1, keepdims=True)
    exps = jnp.exp(scores - highest)
    shares = exps / exps.sum(axis=-1, keepdims=True)
    shares_low = shares.astype(jnp.bfloat16)
    attended = jnp.dot(shares_low, vals, preferred_element_type=jnp.float32)
    out_ref[0] = attended.astype(out_ref.dtype)
    grad_shares = lax.dot_general(g, vals, nt, preferred_element_type=jnp.float32)
    weighted = (grad_shares * shares).sum(axis=-1, keepdims=True)
    grad_scores = (shares * (grad_shares - weighted)).astype(jnp.bfloat16)
    grad_query = jnp.dot(grad_scores, keys, preferred_element_type=jnp.float32)
    gq_ref[0] = (grad_query * score_scale).astype(gq_ref.dtype)
    dk = lax.dot_general(grad_scores, q, tn, preferred_element_type=jnp.float32) * score_scale
    dv = lax.dot_general(shares_low, g, tn, preferred_element_type=jnp.float32)
    for j in range(slot_count):
        dk_ref[chosen[j]] += dk[j * block_len : (j + 1) * block_len]
        dv_ref[chosen[j]] += dv[j * block_len : (j + 1) * block_len]


def head_pass(queries, key_rows, value_rows, grad_head, blocks, extra_count):
    seq_len, head_width = queries.shape
    block_count, slot_count = blocks.shape
    block_len = seq_len // block_count
    tiles = (block_count, block_len, head_width)
    one_block = pl.BlockSpec((1, block_len, head_width), lambda b, t, c: (b, 0, 0))
    whole = pl.BlockSpec(tiles, lambda b, t, c: (0, 0, 0))
    grid_spec = pltpu.PrefetchScalarGridSpec(
        num_scalar_prefetch=2,
        grid=(block_count,),
        in_specs=[one_block, one_block, whole, whole],
        out_specs=[one_block, one_block, whole, whole],
        scratch_shapes=[
            pltpu.VMEM((slot_count * block_len, head_width), jnp.bfloat16),
            pltpu.VMEM((slot_count * block_len, head_width), jnp.bfloat16),
        ],
    )
    flops = 2 * seq_len * slot_count * block_len * head_width * 6
    attended, grad_query, grad_k, grad_v = pl.pallas_call(
        head_kernel,
        grid_spec=grid_spec,
        out_shape=[
            jax.ShapeDtypeStruct(tiles, jnp.bfloat16),
            jax.ShapeDtypeStruct(tiles, jnp.bfloat16),
            jax.ShapeDtypeStruct(tiles, jnp.float32),
            jax.ShapeDtypeStruct(tiles, jnp.float32),
        ],
        compiler_params=pltpu.CompilerParams(dimension_semantics=("arbitrary",)),
        cost_estimate=pl.CostEstimate(
            flops=flops,
            transcendentals=seq_len * slot_count * block_len,
            bytes_accessed=seq_len * head_width * 2 * 6 + seq_len * head_width * 4 * 2,
        ),
    )(
        blocks.reshape(-1),
        jnp.reshape(extra_count, (1,)),
        queries.reshape(tiles),
        grad_head.reshape(tiles),
        key_rows.reshape(tiles),
        value_rows.reshape(tiles),
    )
    summed = jnp.concatenate([grad_k, grad_v], axis=-1)
    return (
        attended.reshape(seq_len, head_width),
        grad_query.reshape(seq_len, head_width),
        summed.reshape(seq_len, 2 * head_width),
    )


def ring_reduce_scatter(chunk, ring, stride, position):
    seq_devices = lax.axis_size("seq")
    group = ring * stride
    me = (position // stride) % ring
    ahead = [
        (s, (s // group) * group + (((s // stride) % ring + 1) % ring) * stride + s % stride)
        for s in range(seq_devices)
    ]
    behind = [(b, a) for (a, b) in ahead]
    total = []
    for side, perm, sign in ((0, ahead, 1), (1, behind, -1)):
        buf = chunk((me - sign) % ring, side)
        for k in range(ring - 1):
            got = lax.ppermute(buf, "seq", perm)
            own = chunk((me - sign * (2 + k)) % ring, side)
            buf = (got.astype(jnp.float32) + own.astype(jnp.float32)).astype(jnp.bfloat16)
        total.append(buf)
    return jnp.concatenate(total, axis=-1)


def direct_sum(pieces, axis_name, size, stride, mine):
    devices = lax.axis_size(axis_name)
    group = size * stride
    got = [lax.dynamic_index_in_dim(pieces, mine, 0, keepdims=False)]
    for d in range(1, size):
        perm = [
            (i, (i // group) * group + (((i // stride) % size + d) % size) * stride + i % stride)
            for i in range(devices)
        ]
        got.append(lax.ppermute(
            lax.dynamic_index_in_dim(pieces, (mine + d) % size, 0, keepdims=False), axis_name, perm
        ))
    return got


def ring_gather_weights(piece, position, dp_index):
    dp_devices = lax.axis_size("dp")
    seq_devices = lax.axis_size("seq")
    y_count = seq_devices // RING_Z
    sizes = {"z": RING_Z, "y": y_count}

    def step_to(s, dim, shift):
        y, z = s // RING_Z, s % RING_Z
        if dim == "z":
            return y * RING_Z + (z + shift) % RING_Z
        return ((y + shift) % y_count) * RING_Z + z

    def ring(x, which, dim):
        n = sizes[dim]
        got = [x]
        for shift, steps in ((1, n // 2), (-1, n - 1 - n // 2)):
            perm = [
                (d * seq_devices + s, d * seq_devices + step_to(s, dim, shift))
                for d in range(dp_devices) if d % 2 == which
                for s in range(seq_devices)
            ]
            cur = x
            for _ in range(steps):
                cur = lax.ppermute(cur, ("dp", "seq"), perm)
                got.append(cur)
        ahead = got[1 : 1 + n // 2]
        behind = got[1 + n // 2 :]
        return jnp.stack([x] + ahead + behind[::-1])

    first = ring(ring(piece, 0, "z"), 0, "y")
    second = ring(ring(piece, 1, "y"), 1, "z")
    return first.reshape(-1, piece.shape[-1]), second.reshape(-1, piece.shape[-1])


def ring_blocks(position, z_first):
    seq_devices = lax.axis_size("seq")
    y_count = seq_devices // RING_Z
    y, z = position // RING_Z, position % RING_Z
    dy = jnp.arange(y_count)
    dz = jnp.arange(RING_Z)
    if z_first:
        origin = ((y - dy) % y_count)[:, None] * RING_Z + ((z - dz) % RING_Z)[None, :]
    else:
        origin = ((y - dy) % y_count)[None, :] * RING_Z + ((z - dz) % RING_Z)[:, None]
    return origin.reshape(-1)


def per_device(activations, w_query, w_key, w_value, key_blocks, random_count, grad_out):
    seq_devices = lax.axis_size("seq")
    dp_devices = lax.axis_size("dp")
    position = lax.axis_index("seq")
    dp_index = lax.axis_index("dp")
    tokens = activations[0]
    grad_rows = grad_out[0]
    tok_count = tokens.shape[0]
    heads = w_query.shape[1] // HD
    kv_heads = w_key.shape[1] // HD
    query_cols = heads * HD
    kv_cols = kv_heads * HD
    all_cols = query_cols + 2 * kv_cols
    w_local = jnp.concatenate([w_query, w_key, w_value], axis=1)
    half = all_cols // 2
    core = dp_index % 2
    pairs = [(i, i ^ 1) for i in range(dp_devices)]
    grad_pieces = grad_rows.reshape(tok_count, heads, HD).transpose(1, 0, 2)
    head_grad = lax.all_to_all(grad_pieces, "seq", split_axis=0, concat_axis=1, tiled=True)[0]
    by_z, by_y = ring_gather_weights(
        lax.dynamic_slice_in_dim(w_local, core * half, half, axis=1), position, dp_index
    )
    w_mine = jnp.where(core == 0, by_z, by_y)
    w_other = lax.ppermute(w_mine, "dp", pairs)
    order_z, order_y = ring_blocks(position, True), ring_blocks(position, False)
    order_mine = jnp.where(core == 0, order_z, order_y)
    order_other = jnp.where(core == 0, order_y, order_z)
    feat = w_local.shape[0]
    token_blocks = tokens.reshape(tok_count, seq_devices, feat)
    tokens_mine = jnp.take(token_blocks, order_mine, axis=1).reshape(tok_count, -1)
    tokens_other = jnp.take(token_blocks, order_other, axis=1).reshape(tok_count, -1)
    proj_mine = jnp.dot(tokens_mine, w_mine, preferred_element_type=jnp.float32).astype(jnp.bfloat16)
    proj_other = jnp.dot(tokens_other, w_other, preferred_element_type=jnp.float32).astype(jnp.bfloat16)
    projected = jnp.zeros((tok_count, all_cols), jnp.bfloat16)
    projected = lax.dynamic_update_slice_in_dim(projected, proj_mine, core * half, axis=1)
    projected = lax.dynamic_update_slice_in_dim(projected, proj_other, (1 - core) * half, axis=1)
    queries = projected[:, :query_cols]
    key_proj = projected[:, query_cols : query_cols + kv_cols]
    value_proj = projected[:, query_cols + kv_cols :]
    query_pieces = queries.reshape(tok_count, heads, HD).transpose(1, 0, 2)
    paired = jnp.concatenate(
        [key_proj.reshape(tok_count, kv_heads, HD), value_proj.reshape(tok_count, kv_heads, HD)],
        axis=2,
    )
    kv_pieces = jnp.repeat(paired.transpose(1, 0, 2), GROUP, axis=0)
    sent = jnp.concatenate([query_pieces, kv_pieces], axis=2)
    landed = lax.all_to_all(sent, "seq", split_axis=0, concat_axis=1, tiled=True)[0]
    head_q = landed[:, :HD]
    head_k = landed[:, HD : 2 * HD]
    head_v = landed[:, 2 * HD :]
    blocks_mine = lax.dynamic_index_in_dim(key_blocks, position, 0, keepdims=False)
    count_mine = lax.dynamic_index_in_dim(random_count, position, 0, keepdims=False)
    attended, grad_query, grad_kv = head_pass(
        head_q, head_k, head_v, head_grad, blocks_mine, count_mine
    )
    back_sent = jnp.concatenate(
        [
            attended.reshape(seq_devices, tok_count, HD),
            grad_query.reshape(seq_devices, tok_count, HD),
            grad_kv.astype(jnp.bfloat16).reshape(seq_devices, tok_count, 2 * HD),
        ],
        axis=2,
    )
    back = lax.all_to_all(back_sent, "seq", split_axis=0, concat_axis=0, tiled=True)
    back_out = back[:, :, :HD]
    back_query = back[:, :, HD : 2 * HD]
    back_kv = back[:, :, 2 * HD :]
    out_rows = back_out.transpose(1, 0, 2).reshape(tok_count, heads * HD)
    grad_q_rows = back_query.transpose(1, 0, 2).reshape(tok_count, heads * HD)
    kv_sum = jnp.sum(
        back_kv.reshape(kv_heads, GROUP, tok_count, 2 * HD), axis=1, dtype=jnp.float32
    ).astype(jnp.bfloat16)
    grad_k_rows = kv_sum[:, :, :HD].transpose(1, 0, 2).reshape(tok_count, kv_heads * HD)
    grad_v_rows = kv_sum[:, :, HD:].transpose(1, 0, 2).reshape(tok_count, kv_heads * HD)
    combined = jnp.concatenate([grad_q_rows, grad_k_rows, grad_v_rows], axis=1)
    contract = (((1,), (1,)), ((), ()))
    comb_mine = lax.dynamic_slice_in_dim(combined, core * half, half, axis=1)
    comb_other = lax.dynamic_slice_in_dim(combined, (1 - core) * half, half, axis=1)
    def natural(part, order):
        back = jnp.zeros_like(order).at[order].set(jnp.arange(seq_devices, dtype=order.dtype))
        return jnp.take(part.reshape(tok_count, seq_devices, feat), back, axis=1).reshape(tok_count, -1)

    grad_x_rows = (
        natural(lax.dot_general(comb_mine, w_mine, contract, preferred_element_type=jnp.float32), order_mine)
        + natural(lax.dot_general(comb_other, w_other, contract, preferred_element_type=jnp.float32), order_other)
    ).astype(jnp.bfloat16)
    factor = 1.0 / math.sqrt(tok_count * seq_devices * dp_devices)
    over_tokens = (((0,), (0,)), ((), ()))
    y_count = seq_devices // RING_Z
    rows = tokens.shape[1] // seq_devices
    span = y_count * rows
    quarter = half // 2
    tok4 = tokens.reshape(tok_count, y_count, RING_Z, rows)
    z_me = position % RING_Z

    def ring_tokens(sign):
        order = (z_me - sign * (1 + jnp.arange(RING_Z))) % RING_Z
        return jnp.take(tok4, order, axis=2).transpose(0, 2, 1, 3).reshape(tok_count, -1)

    def term_t(columns, toks):
        return (
            lax.dot_general(columns, toks, over_tokens, preferred_element_type=jnp.float32)
            * factor
        ).astype(jnp.bfloat16)

    signs = (1, -1)
    toks = [ring_tokens(sign) for sign in signs]
    give = jnp.stack(
        [term_t(comb_other[:, i * quarter : (i + 1) * quarter], toks[i]) for i in range(2)]
    )
    got = lax.ppermute(give, "dp", pairs)
    keep = [term_t(comb_mine[:, i * quarter : (i + 1) * quarter], toks[i]) for i in range(2)]
    grad_x_rows, keep = lax.optimization_barrier((grad_x_rows, keep))
    ahead = [(s, (s // RING_Z) * RING_Z + (s % RING_Z + 1) % RING_Z) for s in range(seq_devices)]
    behind = [(b, a) for (a, b) in ahead]
    ends = []
    for i, perm in enumerate((ahead, behind)):

        def chunk(k):
            piece = slice(k * span, (k + 1) * span)
            return (
                keep[i][:, piece].astype(jnp.float32) + got[i][:, piece].astype(jnp.float32)
            ).astype(jnp.bfloat16)

        buf = chunk(0)
        for k in range(RING_Z - 1):
            arrived = lax.ppermute(buf, "seq", perm)
            buf = (arrived.astype(jnp.float32) + chunk(k + 1).astype(jnp.float32)).astype(jnp.bfloat16)
        ends.append(buf)
    by_y = jnp.concatenate(ends, axis=0).reshape(half, y_count, rows).transpose(1, 2, 0)
    from_y = direct_sum(by_y, "seq", y_count, RING_Z, position // RING_Z)
    total = from_y[0].astype(jnp.float32)
    for piece in from_y[1:]:
        total = total + piece.astype(jnp.float32)
    part = total.astype(jnp.bfloat16)
    chips = dp_devices // 2
    chip = dp_index // 2
    from_x = direct_sum(jnp.broadcast_to(part, (chips,) + part.shape), "dp", chips, 2, chip)
    by_offset = jnp.stack(from_x)
    in_order = jnp.take(by_offset, (chip - jnp.arange(chips)) % chips, axis=0)
    part = jnp.sum(in_order.astype(jnp.float32), axis=0).astype(jnp.bfloat16)
    other_half = lax.ppermute(part, "dp", pairs)
    first = jnp.where(core == 0, part, other_half)
    second = jnp.where(core == 0, other_half, part)
    grad_all = jnp.concatenate([first, second], axis=1)
    grad_wq = grad_all[:, :query_cols]
    grad_wk = grad_all[:, query_cols : query_cols + kv_cols]
    grad_wv = grad_all[:, query_cols + kv_cols :]
    return (out_rows[None], grad_x_rows[None], grad_wq, grad_wk, grad_wv)


def solution(mesh):
    placed = (
        P("dp", "seq", None),
        P("seq", None),
        P("seq", None),
        P("seq", None),
        P(),
        P(),
        P("dp", "seq", None),
    )
    return jax.shard_map(
        per_device,
        mesh=mesh,
        in_specs=placed,
        out_specs=(
            P("dp", "seq", None),
            P("dp", "seq", None),
            P("seq", None),
            P("seq", None),
            P("seq", None),
        ),
        check_vma=False,
    )
```

```python
import math

import jax
import jax.numpy as jnp
from jax import lax
from jax.experimental import pallas as pl
from jax.experimental.pallas import tpu as pltpu
from jax.sharding import PartitionSpec as P

HD = 64
GROUP = 8


masked_score = -1e30
query_group = 4
RING_Z = 8


def head_kernel(table_ref, count_ref, q_ref, g_ref, k_ref, v_ref,
                out_ref, gq_ref, dk_ref, dv_ref, k_cat, v_cat):
    step = pl.program_id(0)
    per_step = q_ref.shape[0]
    slot_count = table_ref.shape[0] // (pl.num_programs(0) * per_step)
    block_len = q_ref.shape[1]
    head_width = q_ref.shape[-1]
    score_scale = head_width ** (-0.5)

    @pl.when(step == 0)
    def _():
        dk_ref[...] = jnp.zeros_like(dk_ref)
        dv_ref[...] = jnp.zeros_like(dv_ref)

    used = 4 + count_ref[0]
    nt = (((1,), (1,)), ((), ()))
    tn = (((0,), (0,)), ((), ()))
    for sub in range(per_step):
        b = step * per_step + sub
        q = q_ref[sub]
        g = g_ref[sub]
        chosen = [table_ref[b * slot_count + j] for j in range(slot_count)]
        for j in range(slot_count):
            k_cat[j * block_len : (j + 1) * block_len, :] = k_ref[chosen[j]]
            v_cat[j * block_len : (j + 1) * block_len, :] = v_ref[chosen[j]]
        keys = k_cat[...]
        vals = v_cat[...]
        scores = lax.dot_general(q, keys, nt, preferred_element_type=jnp.float32) * score_scale
        slot_of = lax.broadcasted_iota(jnp.int32, (1, slot_count * block_len), 1) // block_len
        scores = jnp.where(slot_of < used, scores, masked_score)
        highest = scores.max(axis=-1, keepdims=True)
        exps = jnp.exp(scores - highest)
        shares = exps / exps.sum(axis=-1, keepdims=True)
        shares_low = shares.astype(jnp.bfloat16)
        attended = jnp.dot(shares_low, vals, preferred_element_type=jnp.float32)
        out_ref[sub] = attended.astype(out_ref.dtype)
        grad_shares = lax.dot_general(g, vals, nt, preferred_element_type=jnp.float32)
        weighted = (grad_shares * shares).sum(axis=-1, keepdims=True)
        grad_scores = (shares * (grad_shares - weighted)).astype(jnp.bfloat16)
        grad_query = jnp.dot(grad_scores, keys, preferred_element_type=jnp.float32)
        gq_ref[sub] = (grad_query * score_scale).astype(gq_ref.dtype)
        dk = lax.dot_general(grad_scores, q, tn, preferred_element_type=jnp.float32) * score_scale
        dv = lax.dot_general(shares_low, g, tn, preferred_element_type=jnp.float32)
        for j in range(slot_count):
            dk_ref[chosen[j]] += dk[j * block_len : (j + 1) * block_len]
            dv_ref[chosen[j]] += dv[j * block_len : (j + 1) * block_len]


def head_pass(queries, key_rows, value_rows, grad_head, blocks, extra_count):
    seq_len, head_width = queries.shape
    block_count, slot_count = blocks.shape
    block_len = seq_len // block_count
    tiles = (block_count, block_len, head_width)
    per_step = 2
    one_block = pl.BlockSpec((per_step, block_len, head_width), lambda b, t, c: (b, 0, 0))
    whole = pl.BlockSpec(tiles, lambda b, t, c: (0, 0, 0))
    grid_spec = pltpu.PrefetchScalarGridSpec(
        num_scalar_prefetch=2,
        grid=(block_count // per_step,),
        in_specs=[one_block, one_block, whole, whole],
        out_specs=[one_block, one_block, whole, whole],
        scratch_shapes=[
            pltpu.VMEM((slot_count * block_len, head_width), jnp.bfloat16),
            pltpu.VMEM((slot_count * block_len, head_width), jnp.bfloat16),
        ],
    )
    flops = 2 * seq_len * slot_count * block_len * head_width * 6
    attended, grad_query, grad_k, grad_v = pl.pallas_call(
        head_kernel,
        grid_spec=grid_spec,
        out_shape=[
            jax.ShapeDtypeStruct(tiles, jnp.bfloat16),
            jax.ShapeDtypeStruct(tiles, jnp.bfloat16),
            jax.ShapeDtypeStruct(tiles, jnp.float32),
            jax.ShapeDtypeStruct(tiles, jnp.float32),
        ],
        compiler_params=pltpu.CompilerParams(dimension_semantics=("arbitrary",)),
        cost_estimate=pl.CostEstimate(
            flops=flops,
            transcendentals=seq_len * slot_count * block_len,
            bytes_accessed=seq_len * head_width * 2 * 6 + seq_len * head_width * 4 * 2,
        ),
    )(
        blocks.reshape(-1),
        jnp.reshape(extra_count, (1,)),
        queries.reshape(tiles),
        grad_head.reshape(tiles),
        key_rows.reshape(tiles),
        value_rows.reshape(tiles),
    )
    summed = jnp.concatenate([grad_k, grad_v], axis=-1)
    return (
        attended.reshape(seq_len, head_width),
        grad_query.reshape(seq_len, head_width),
        summed.reshape(seq_len, 2 * head_width),
    )


def ring_reduce_scatter(chunk, ring, stride, position):
    seq_devices = lax.axis_size("seq")
    group = ring * stride
    me = (position // stride) % ring
    ahead = [
        (s, (s // group) * group + (((s // stride) % ring + 1) % ring) * stride + s % stride)
        for s in range(seq_devices)
    ]
    behind = [(b, a) for (a, b) in ahead]
    total = []
    for side, perm, sign in ((0, ahead, 1), (1, behind, -1)):
        buf = chunk((me - sign) % ring, side)
        for k in range(ring - 1):
            got = lax.ppermute(buf, "seq", perm)
            own = chunk((me - sign * (2 + k)) % ring, side)
            buf = (got.astype(jnp.float32) + own.astype(jnp.float32)).astype(jnp.bfloat16)
        total.append(buf)
    return jnp.concatenate(total, axis=-1)


def direct_sum(pieces, axis_name, size, stride, mine):
    devices = lax.axis_size(axis_name)
    group = size * stride
    got = [lax.dynamic_index_in_dim(pieces, mine, 0, keepdims=False)]
    for d in range(1, size):
        perm = [
            (i, (i // group) * group + (((i // stride) % size + d) % size) * stride + i % stride)
            for i in range(devices)
        ]
        got.append(lax.ppermute(
            lax.dynamic_index_in_dim(pieces, (mine + d) % size, 0, keepdims=False), axis_name, perm
        ))
    return got


def ring_gather_weights(piece, position, dp_index):
    dp_devices = lax.axis_size("dp")
    seq_devices = lax.axis_size("seq")
    y_count = seq_devices // RING_Z
    sizes = {"z": RING_Z, "y": y_count}

    def step_to(s, dim, shift):
        y, z = s // RING_Z, s % RING_Z
        if dim == "z":
            return y * RING_Z + (z + shift) % RING_Z
        return ((y + shift) % y_count) * RING_Z + z

    def ring(x, which, dim):
        n = sizes[dim]
        got = [x]
        for shift, steps in ((1, n // 2), (-1, n - 1 - n // 2)):
            perm = [
                (d * seq_devices + s, d * seq_devices + step_to(s, dim, shift))
                for d in range(dp_devices) if d % 2 == which
                for s in range(seq_devices)
            ]
            cur = x
            for _ in range(steps):
                cur = lax.ppermute(cur, ("dp", "seq"), perm)
                got.append(cur)
        ahead = got[1 : 1 + n // 2]
        behind = got[1 + n // 2 :]
        return jnp.stack([x] + ahead + behind[::-1])

    first = ring(ring(piece, 0, "z"), 0, "y")
    second = ring(ring(piece, 1, "y"), 1, "z")
    return first.reshape(-1, piece.shape[-1]), second.reshape(-1, piece.shape[-1])


def ring_blocks(position, z_first):
    seq_devices = lax.axis_size("seq")
    y_count = seq_devices // RING_Z
    y, z = position // RING_Z, position % RING_Z
    dy = jnp.arange(y_count)
    dz = jnp.arange(RING_Z)
    if z_first:
        origin = ((y - dy) % y_count)[:, None] * RING_Z + ((z - dz) % RING_Z)[None, :]
    else:
        origin = ((y - dy) % y_count)[None, :] * RING_Z + ((z - dz) % RING_Z)[:, None]
    return origin.reshape(-1)


def per_device(activations, w_query, w_key, w_value, key_blocks, random_count, grad_out):
    seq_devices = lax.axis_size("seq")
    dp_devices = lax.axis_size("dp")
    position = lax.axis_index("seq")
    dp_index = lax.axis_index("dp")
    tokens = activations[0]
    grad_rows = grad_out[0]
    tok_count = tokens.shape[0]
    heads = w_query.shape[1] // HD
    kv_heads = w_key.shape[1] // HD
    query_cols = heads * HD
    kv_cols = kv_heads * HD
    all_cols = query_cols + 2 * kv_cols
    w_local = jnp.concatenate([w_query, w_key, w_value], axis=1)
    half = all_cols // 2
    core = dp_index % 2
    pairs = [(i, i ^ 1) for i in range(dp_devices)]
    grad_pieces = grad_rows.reshape(tok_count, heads, HD).transpose(1, 0, 2)
    head_grad = lax.all_to_all(grad_pieces, "seq", split_axis=0, concat_axis=1, tiled=True)[0]
    by_z, by_y = ring_gather_weights(
        lax.dynamic_slice_in_dim(w_local, core * half, half, axis=1), position, dp_index
    )
    w_mine = jnp.where(core == 0, by_z, by_y)
    w_other = lax.ppermute(w_mine, "dp", pairs)
    order_z, order_y = ring_blocks(position, True), ring_blocks(position, False)
    order_mine = jnp.where(core == 0, order_z, order_y)
    order_other = jnp.where(core == 0, order_y, order_z)
    feat = w_local.shape[0]
    token_blocks = tokens.reshape(tok_count, seq_devices, feat)
    tokens_mine = jnp.take(token_blocks, order_mine, axis=1).reshape(tok_count, -1)
    tokens_other = jnp.take(token_blocks, order_other, axis=1).reshape(tok_count, -1)
    proj_mine = jnp.dot(tokens_mine, w_mine, preferred_element_type=jnp.float32).astype(jnp.bfloat16)
    proj_other = jnp.dot(tokens_other, w_other, preferred_element_type=jnp.float32).astype(jnp.bfloat16)
    projected = jnp.zeros((tok_count, all_cols), jnp.bfloat16)
    projected = lax.dynamic_update_slice_in_dim(projected, proj_mine, core * half, axis=1)
    projected = lax.dynamic_update_slice_in_dim(projected, proj_other, (1 - core) * half, axis=1)
    queries = projected[:, :query_cols]
    key_proj = projected[:, query_cols : query_cols + kv_cols]
    value_proj = projected[:, query_cols + kv_cols :]
    query_pieces = queries.reshape(tok_count, heads, HD).transpose(1, 0, 2)
    paired = jnp.concatenate(
        [key_proj.reshape(tok_count, kv_heads, HD), value_proj.reshape(tok_count, kv_heads, HD)],
        axis=2,
    )
    kv_pieces = jnp.repeat(paired.transpose(1, 0, 2), GROUP, axis=0)
    sent = jnp.concatenate([query_pieces, kv_pieces], axis=2)
    landed = lax.all_to_all(sent, "seq", split_axis=0, concat_axis=1, tiled=True)[0]
    head_q = landed[:, :HD]
    head_k = landed[:, HD : 2 * HD]
    head_v = landed[:, 2 * HD :]
    blocks_mine = lax.dynamic_index_in_dim(key_blocks, position, 0, keepdims=False)
    count_mine = lax.dynamic_index_in_dim(random_count, position, 0, keepdims=False)
    attended, grad_query, grad_kv = head_pass(
        head_q, head_k, head_v, head_grad, blocks_mine, count_mine
    )
    back_sent = jnp.concatenate(
        [
            attended.reshape(seq_devices, tok_count, HD),
            grad_query.reshape(seq_devices, tok_count, HD),
            grad_kv.astype(jnp.bfloat16).reshape(seq_devices, tok_count, 2 * HD),
        ],
        axis=2,
    )
    back = lax.all_to_all(back_sent, "seq", split_axis=0, concat_axis=0, tiled=True)
    back_out = back[:, :, :HD]
    back_query = back[:, :, HD : 2 * HD]
    back_kv = back[:, :, 2 * HD :]
    out_rows = back_out.transpose(1, 0, 2).reshape(tok_count, heads * HD)
    grad_q_rows = back_query.transpose(1, 0, 2).reshape(tok_count, heads * HD)
    kv_sum = jnp.sum(
        back_kv.reshape(kv_heads, GROUP, tok_count, 2 * HD), axis=1, dtype=jnp.float32
    ).astype(jnp.bfloat16)
    grad_k_rows = kv_sum[:, :, :HD].transpose(1, 0, 2).reshape(tok_count, kv_heads * HD)
    grad_v_rows = kv_sum[:, :, HD:].transpose(1, 0, 2).reshape(tok_count, kv_heads * HD)
    combined = jnp.concatenate([grad_q_rows, grad_k_rows, grad_v_rows], axis=1)
    contract = (((1,), (1,)), ((), ()))
    comb_mine = lax.dynamic_slice_in_dim(combined, core * half, half, axis=1)
    comb_other = lax.dynamic_slice_in_dim(combined, (1 - core) * half, half, axis=1)
    def natural(part, order):
        back = jnp.zeros_like(order).at[order].set(jnp.arange(seq_devices, dtype=order.dtype))
        return jnp.take(part.reshape(tok_count, seq_devices, feat), back, axis=1).reshape(tok_count, -1)

    grad_x_rows = (
        natural(lax.dot_general(comb_mine, w_mine, contract, preferred_element_type=jnp.float32), order_mine)
        + natural(lax.dot_general(comb_other, w_other, contract, preferred_element_type=jnp.float32), order_other)
    ).astype(jnp.bfloat16)
    factor = 1.0 / math.sqrt(tok_count * seq_devices * dp_devices)
    over_tokens = (((0,), (0,)), ((), ()))
    y_count = seq_devices // RING_Z
    rows = tokens.shape[1] // seq_devices
    span = y_count * rows
    quarter = half // 2
    tok4 = tokens.reshape(tok_count, y_count, RING_Z, rows)
    z_me = position % RING_Z

    def ring_tokens(sign):
        order = (z_me - sign * (1 + jnp.arange(RING_Z))) % RING_Z
        return jnp.take(tok4, order, axis=2).transpose(0, 2, 1, 3).reshape(tok_count, -1)

    def term_t(columns, toks):
        return (
            lax.dot_general(columns, toks, over_tokens, preferred_element_type=jnp.float32)
            * factor
        ).astype(jnp.bfloat16)

    signs = (1, -1)
    toks = [ring_tokens(sign) for sign in signs]
    give = jnp.stack(
        [term_t(comb_other[:, i * quarter : (i + 1) * quarter], toks[i]) for i in range(2)]
    )
    got = lax.ppermute(give, "dp", pairs)
    keep = [term_t(comb_mine[:, i * quarter : (i + 1) * quarter], toks[i]) for i in range(2)]
    grad_x_rows, keep = lax.optimization_barrier((grad_x_rows, keep))
    ahead = [(s, (s // RING_Z) * RING_Z + (s % RING_Z + 1) % RING_Z) for s in range(seq_devices)]
    behind = [(b, a) for (a, b) in ahead]
    ends = []
    for i, perm in enumerate((ahead, behind)):

        def chunk(k):
            piece = slice(k * span, (k + 1) * span)
            return (
                keep[i][:, piece].astype(jnp.float32) + got[i][:, piece].astype(jnp.float32)
            ).astype(jnp.bfloat16)

        buf = chunk(0)
        for k in range(RING_Z - 1):
            arrived = lax.ppermute(buf, "seq", perm)
            buf = (arrived.astype(jnp.float32) + chunk(k + 1).astype(jnp.float32)).astype(jnp.bfloat16)
        ends.append(buf)
    by_y = jnp.concatenate(ends, axis=0).reshape(half, y_count, rows).transpose(1, 2, 0)
    from_y = direct_sum(by_y, "seq", y_count, RING_Z, position // RING_Z)
    total = from_y[0].astype(jnp.float32)
    for piece in from_y[1:]:
        total = total + piece.astype(jnp.float32)
    part = total.astype(jnp.bfloat16)
    chips = dp_devices // 2
    chip = dp_index // 2
    from_x = direct_sum(jnp.broadcast_to(part, (chips,) + part.shape), "dp", chips, 2, chip)
    by_offset = jnp.stack(from_x)
    in_order = jnp.take(by_offset, (chip - jnp.arange(chips)) % chips, axis=0)
    part = jnp.sum(in_order.astype(jnp.float32), axis=0).astype(jnp.bfloat16)
    other_half = lax.ppermute(part, "dp", pairs)
    first = jnp.where(core == 0, part, other_half)
    second = jnp.where(core == 0, other_half, part)
    grad_all = jnp.concatenate([first, second], axis=1)
    grad_wq = grad_all[:, :query_cols]
    grad_wk = grad_all[:, query_cols : query_cols + kv_cols]
    grad_wv = grad_all[:, query_cols + kv_cols :]
    return (out_rows[None], grad_x_rows[None], grad_wq, grad_wk, grad_wv)


def solution(mesh):
    placed = (
        P("dp", "seq", None),
        P("seq", None),
        P("seq", None),
        P("seq", None),
        P(),
        P(),
        P("dp", "seq", None),
    )
    return jax.shard_map(
        per_device,
        mesh=mesh,
        in_specs=placed,
        out_specs=(
            P("dp", "seq", None),
            P("dp", "seq", None),
            P("seq", None),
            P("seq", None),
            P("seq", None),
        ),
        check_vma=False,
    )
```

```python
import math

import jax
import jax.numpy as jnp
from jax import lax
from jax.experimental import pallas as pl
from jax.experimental.pallas import tpu as pltpu
from jax.sharding import PartitionSpec as P

HD = 64
GROUP = 8


masked_score = -1e30
query_group = 4
RING_Z = 8


def head_kernel(table_ref, count_ref, q_ref, g_ref, k_ref, v_ref,
                out_ref, gq_ref, dk_ref, dv_ref, k_cat, v_cat):
    step = pl.program_id(0)
    per_step = q_ref.shape[0]
    slot_count = table_ref.shape[0] // (pl.num_programs(0) * per_step)
    block_len = q_ref.shape[1]
    head_width = q_ref.shape[-1]
    score_scale = head_width ** (-0.5)

    @pl.when(step == 0)
    def _():
        dk_ref[...] = jnp.zeros_like(dk_ref)
        dv_ref[...] = jnp.zeros_like(dv_ref)

    used = 4 + count_ref[0]
    nt = (((1,), (1,)), ((), ()))
    tn = (((0,), (0,)), ((), ()))
    for sub in range(per_step):
        b = step * per_step + sub
        q = q_ref[sub]
        g = g_ref[sub]
        chosen = [table_ref[b * slot_count + j] for j in range(slot_count)]
        for j in range(slot_count):
            k_cat[j * block_len : (j + 1) * block_len, :] = k_ref[chosen[j]]
            v_cat[j * block_len : (j + 1) * block_len, :] = v_ref[chosen[j]]
        keys = k_cat[...]
        vals = v_cat[...]
        scores = lax.dot_general(q, keys, nt, preferred_element_type=jnp.float32) * score_scale
        slot_of = lax.broadcasted_iota(jnp.int32, (1, slot_count * block_len), 1) // block_len
        scores = jnp.where(slot_of < used, scores, masked_score)
        highest = scores.max(axis=-1, keepdims=True)
        exps = jnp.exp(scores - highest)
        shares = exps / exps.sum(axis=-1, keepdims=True)
        shares_low = shares.astype(jnp.bfloat16)
        attended = jnp.dot(shares_low, vals, preferred_element_type=jnp.float32)
        out_ref[sub] = attended.astype(out_ref.dtype)
        grad_shares = lax.dot_general(g, vals, nt, preferred_element_type=jnp.float32)
        weighted = (grad_shares * shares).sum(axis=-1, keepdims=True)
        grad_scores = (shares * (grad_shares - weighted)).astype(jnp.bfloat16)
        grad_query = jnp.dot(grad_scores, keys, preferred_element_type=jnp.float32)
        gq_ref[sub] = (grad_query * score_scale).astype(gq_ref.dtype)
        dk = lax.dot_general(grad_scores, q, tn, preferred_element_type=jnp.float32) * score_scale
        dv = lax.dot_general(shares_low, g, tn, preferred_element_type=jnp.float32)
        for j in range(slot_count):
            dk_ref[chosen[j]] += dk[j * block_len : (j + 1) * block_len]
            dv_ref[chosen[j]] += dv[j * block_len : (j + 1) * block_len]


def head_pass(queries, key_rows, value_rows, grad_head, blocks, extra_count):
    seq_len, head_width = queries.shape
    block_count, slot_count = blocks.shape
    block_len = seq_len // block_count
    tiles = (block_count, block_len, head_width)
    per_step = 4
    one_block = pl.BlockSpec((per_step, block_len, head_width), lambda b, t, c: (b, 0, 0))
    whole = pl.BlockSpec(tiles, lambda b, t, c: (0, 0, 0))
    grid_spec = pltpu.PrefetchScalarGridSpec(
        num_scalar_prefetch=2,
        grid=(block_count // per_step,),
        in_specs=[one_block, one_block, whole, whole],
        out_specs=[one_block, one_block, whole, whole],
        scratch_shapes=[
            pltpu.VMEM((slot_count * block_len, head_width), jnp.bfloat16),
            pltpu.VMEM((slot_count * block_len, head_width), jnp.bfloat16),
        ],
    )
    flops = 2 * seq_len * slot_count * block_len * head_width * 6
    attended, grad_query, grad_k, grad_v = pl.pallas_call(
        head_kernel,
        grid_spec=grid_spec,
        out_shape=[
            jax.ShapeDtypeStruct(tiles, jnp.bfloat16),
            jax.ShapeDtypeStruct(tiles, jnp.bfloat16),
            jax.ShapeDtypeStruct(tiles, jnp.float32),
            jax.ShapeDtypeStruct(tiles, jnp.float32),
        ],
        compiler_params=pltpu.CompilerParams(dimension_semantics=("arbitrary",)),
        cost_estimate=pl.CostEstimate(
            flops=flops,
            transcendentals=seq_len * slot_count * block_len,
            bytes_accessed=seq_len * head_width * 2 * 6 + seq_len * head_width * 4 * 2,
        ),
    )(
        blocks.reshape(-1),
        jnp.reshape(extra_count, (1,)),
        queries.reshape(tiles),
        grad_head.reshape(tiles),
        key_rows.reshape(tiles),
        value_rows.reshape(tiles),
    )
    summed = jnp.concatenate([grad_k, grad_v], axis=-1)
    return (
        attended.reshape(seq_len, head_width),
        grad_query.reshape(seq_len, head_width),
        summed.reshape(seq_len, 2 * head_width),
    )


def ring_reduce_scatter(chunk, ring, stride, position):
    seq_devices = lax.axis_size("seq")
    group = ring * stride
    me = (position // stride) % ring
    ahead = [
        (s, (s // group) * group + (((s // stride) % ring + 1) % ring) * stride + s % stride)
        for s in range(seq_devices)
    ]
    behind = [(b, a) for (a, b) in ahead]
    total = []
    for side, perm, sign in ((0, ahead, 1), (1, behind, -1)):
        buf = chunk((me - sign) % ring, side)
        for k in range(ring - 1):
            got = lax.ppermute(buf, "seq", perm)
            own = chunk((me - sign * (2 + k)) % ring, side)
            buf = (got.astype(jnp.float32) + own.astype(jnp.float32)).astype(jnp.bfloat16)
        total.append(buf)
    return jnp.concatenate(total, axis=-1)


def direct_sum(pieces, axis_name, size, stride, mine):
    devices = lax.axis_size(axis_name)
    group = size * stride
    got = [lax.dynamic_index_in_dim(pieces, mine, 0, keepdims=False)]
    for d in range(1, size):
        perm = [
            (i, (i // group) * group + (((i // stride) % size + d) % size) * stride + i % stride)
            for i in range(devices)
        ]
        got.append(lax.ppermute(
            lax.dynamic_index_in_dim(pieces, (mine + d) % size, 0, keepdims=False), axis_name, perm
        ))
    return got


def ring_gather_weights(piece, position, dp_index):
    dp_devices = lax.axis_size("dp")
    seq_devices = lax.axis_size("seq")
    y_count = seq_devices // RING_Z
    sizes = {"z": RING_Z, "y": y_count}

    def step_to(s, dim, shift):
        y, z = s // RING_Z, s % RING_Z
        if dim == "z":
            return y * RING_Z + (z + shift) % RING_Z
        return ((y + shift) % y_count) * RING_Z + z

    def ring(x, which, dim):
        n = sizes[dim]
        got = [x]
        for shift, steps in ((1, n // 2), (-1, n - 1 - n // 2)):
            perm = [
                (d * seq_devices + s, d * seq_devices + step_to(s, dim, shift))
                for d in range(dp_devices) if d % 2 == which
                for s in range(seq_devices)
            ]
            cur = x
            for _ in range(steps):
                cur = lax.ppermute(cur, ("dp", "seq"), perm)
                got.append(cur)
        ahead = got[1 : 1 + n // 2]
        behind = got[1 + n // 2 :]
        return jnp.stack([x] + ahead + behind[::-1])

    first = ring(ring(piece, 0, "z"), 0, "y")
    second = ring(ring(piece, 1, "y"), 1, "z")
    return first.reshape(-1, piece.shape[-1]), second.reshape(-1, piece.shape[-1])


def ring_blocks(position, z_first):
    seq_devices = lax.axis_size("seq")
    y_count = seq_devices // RING_Z
    y, z = position // RING_Z, position % RING_Z
    dy = jnp.arange(y_count)
    dz = jnp.arange(RING_Z)
    if z_first:
        origin = ((y - dy) % y_count)[:, None] * RING_Z + ((z - dz) % RING_Z)[None, :]
    else:
        origin = ((y - dy) % y_count)[None, :] * RING_Z + ((z - dz) % RING_Z)[:, None]
    return origin.reshape(-1)


def per_device(activations, w_query, w_key, w_value, key_blocks, random_count, grad_out):
    seq_devices = lax.axis_size("seq")
    dp_devices = lax.axis_size("dp")
    position = lax.axis_index("seq")
    dp_index = lax.axis_index("dp")
    tokens = activations[0]
    grad_rows = grad_out[0]
    tok_count = tokens.shape[0]
    heads = w_query.shape[1] // HD
    kv_heads = w_key.shape[1] // HD
    query_cols = heads * HD
    kv_cols = kv_heads * HD
    all_cols = query_cols + 2 * kv_cols
    w_local = jnp.concatenate([w_query, w_key, w_value], axis=1)
    half = all_cols // 2
    core = dp_index % 2
    pairs = [(i, i ^ 1) for i in range(dp_devices)]
    grad_pieces = grad_rows.reshape(tok_count, heads, HD).transpose(1, 0, 2)
    head_grad = lax.all_to_all(grad_pieces, "seq", split_axis=0, concat_axis=1, tiled=True)[0]
    by_z, by_y = ring_gather_weights(
        lax.dynamic_slice_in_dim(w_local, core * half, half, axis=1), position, dp_index
    )
    w_mine = jnp.where(core == 0, by_z, by_y)
    w_other = lax.ppermute(w_mine, "dp", pairs)
    order_z, order_y = ring_blocks(position, True), ring_blocks(position, False)
    order_mine = jnp.where(core == 0, order_z, order_y)
    order_other = jnp.where(core == 0, order_y, order_z)
    feat = w_local.shape[0]
    token_blocks = tokens.reshape(tok_count, seq_devices, feat)
    tokens_mine = jnp.take(token_blocks, order_mine, axis=1).reshape(tok_count, -1)
    tokens_other = jnp.take(token_blocks, order_other, axis=1).reshape(tok_count, -1)
    proj_mine = jnp.dot(tokens_mine, w_mine, preferred_element_type=jnp.float32).astype(jnp.bfloat16)
    proj_other = jnp.dot(tokens_other, w_other, preferred_element_type=jnp.float32).astype(jnp.bfloat16)
    projected = jnp.zeros((tok_count, all_cols), jnp.bfloat16)
    projected = lax.dynamic_update_slice_in_dim(projected, proj_mine, core * half, axis=1)
    projected = lax.dynamic_update_slice_in_dim(projected, proj_other, (1 - core) * half, axis=1)
    queries = projected[:, :query_cols]
    key_proj = projected[:, query_cols : query_cols + kv_cols]
    value_proj = projected[:, query_cols + kv_cols :]
    query_pieces = queries.reshape(tok_count, heads, HD).transpose(1, 0, 2)
    paired = jnp.concatenate(
        [key_proj.reshape(tok_count, kv_heads, HD), value_proj.reshape(tok_count, kv_heads, HD)],
        axis=2,
    )
    kv_pieces = jnp.repeat(paired.transpose(1, 0, 2), GROUP, axis=0)
    sent = jnp.concatenate([query_pieces, kv_pieces], axis=2)
    landed = lax.all_to_all(sent, "seq", split_axis=0, concat_axis=1, tiled=True)[0]
    head_q = landed[:, :HD]
    head_k = landed[:, HD : 2 * HD]
    head_v = landed[:, 2 * HD :]
    blocks_mine = lax.dynamic_index_in_dim(key_blocks, position, 0, keepdims=False)
    count_mine = lax.dynamic_index_in_dim(random_count, position, 0, keepdims=False)
    attended, grad_query, grad_kv = head_pass(
        head_q, head_k, head_v, head_grad, blocks_mine, count_mine
    )
    back_sent = jnp.concatenate(
        [
            attended.reshape(seq_devices, tok_count, HD),
            grad_query.reshape(seq_devices, tok_count, HD),
            grad_kv.astype(jnp.bfloat16).reshape(seq_devices, tok_count, 2 * HD),
        ],
        axis=2,
    )
    back = lax.all_to_all(back_sent, "seq", split_axis=0, concat_axis=0, tiled=True)
    back_out = back[:, :, :HD]
    back_query = back[:, :, HD : 2 * HD]
    back_kv = back[:, :, 2 * HD :]
    out_rows = back_out.transpose(1, 0, 2).reshape(tok_count, heads * HD)
    grad_q_rows = back_query.transpose(1, 0, 2).reshape(tok_count, heads * HD)
    kv_sum = jnp.sum(
        back_kv.reshape(kv_heads, GROUP, tok_count, 2 * HD), axis=1, dtype=jnp.float32
    ).astype(jnp.bfloat16)
    grad_k_rows = kv_sum[:, :, :HD].transpose(1, 0, 2).reshape(tok_count, kv_heads * HD)
    grad_v_rows = kv_sum[:, :, HD:].transpose(1, 0, 2).reshape(tok_count, kv_heads * HD)
    combined = jnp.concatenate([grad_q_rows, grad_k_rows, grad_v_rows], axis=1)
    contract = (((1,), (1,)), ((), ()))
    comb_mine = lax.dynamic_slice_in_dim(combined, core * half, half, axis=1)
    comb_other = lax.dynamic_slice_in_dim(combined, (1 - core) * half, half, axis=1)
    def natural(part, order):
        back = jnp.zeros_like(order).at[order].set(jnp.arange(seq_devices, dtype=order.dtype))
        return jnp.take(part.reshape(tok_count, seq_devices, feat), back, axis=1).reshape(tok_count, -1)

    grad_x_rows = (
        natural(lax.dot_general(comb_mine, w_mine, contract, preferred_element_type=jnp.float32), order_mine)
        + natural(lax.dot_general(comb_other, w_other, contract, preferred_element_type=jnp.float32), order_other)
    ).astype(jnp.bfloat16)
    factor = 1.0 / math.sqrt(tok_count * seq_devices * dp_devices)
    over_tokens = (((0,), (0,)), ((), ()))
    y_count = seq_devices // RING_Z
    rows = tokens.shape[1] // seq_devices
    span = y_count * rows
    quarter = half // 2
    tok4 = tokens.reshape(tok_count, y_count, RING_Z, rows)
    z_me = position % RING_Z

    def ring_tokens(sign):
        order = (z_me - sign * (1 + jnp.arange(RING_Z))) % RING_Z
        return jnp.take(tok4, order, axis=2).transpose(0, 2, 1, 3).reshape(tok_count, -1)

    def term_t(columns, toks):
        return (
            lax.dot_general(columns, toks, over_tokens, preferred_element_type=jnp.float32)
            * factor
        ).astype(jnp.bfloat16)

    signs = (1, -1)
    toks = [ring_tokens(sign) for sign in signs]
    give = jnp.stack(
        [term_t(comb_other[:, i * quarter : (i + 1) * quarter], toks[i]) for i in range(2)]
    )
    got = lax.ppermute(give, "dp", pairs)
    keep = [term_t(comb_mine[:, i * quarter : (i + 1) * quarter], toks[i]) for i in range(2)]
    grad_x_rows, keep = lax.optimization_barrier((grad_x_rows, keep))
    ahead = [(s, (s // RING_Z) * RING_Z + (s % RING_Z + 1) % RING_Z) for s in range(seq_devices)]
    behind = [(b, a) for (a, b) in ahead]
    ends = []
    for i, perm in enumerate((ahead, behind)):

        def chunk(k):
            piece = slice(k * span, (k + 1) * span)
            return (
                keep[i][:, piece].astype(jnp.float32) + got[i][:, piece].astype(jnp.float32)
            ).astype(jnp.bfloat16)

        buf = chunk(0)
        for k in range(RING_Z - 1):
            arrived = lax.ppermute(buf, "seq", perm)
            buf = (arrived.astype(jnp.float32) + chunk(k + 1).astype(jnp.float32)).astype(jnp.bfloat16)
        ends.append(buf)
    by_y = jnp.concatenate(ends, axis=0).reshape(half, y_count, rows).transpose(1, 2, 0)
    from_y = direct_sum(by_y, "seq", y_count, RING_Z, position // RING_Z)
    total = from_y[0].astype(jnp.float32)
    for piece in from_y[1:]:
        total = total + piece.astype(jnp.float32)
    part = total.astype(jnp.bfloat16)
    chips = dp_devices // 2
    chip = dp_index // 2
    from_x = direct_sum(jnp.broadcast_to(part, (chips,) + part.shape), "dp", chips, 2, chip)
    by_offset = jnp.stack(from_x)
    in_order = jnp.take(by_offset, (chip - jnp.arange(chips)) % chips, axis=0)
    part = jnp.sum(in_order.astype(jnp.float32), axis=0).astype(jnp.bfloat16)
    other_half = lax.ppermute(part, "dp", pairs)
    first = jnp.where(core == 0, part, other_half)
    second = jnp.where(core == 0, other_half, part)
    grad_all = jnp.concatenate([first, second], axis=1)
    grad_wq = grad_all[:, :query_cols]
    grad_wk = grad_all[:, query_cols : query_cols + kv_cols]
    grad_wv = grad_all[:, query_cols + kv_cols :]
    return (out_rows[None], grad_x_rows[None], grad_wq, grad_wk, grad_wv)


def solution(mesh):
    placed = (
        P("dp", "seq", None),
        P("seq", None),
        P("seq", None),
        P("seq", None),
        P(),
        P(),
        P("dp", "seq", None),
    )
    return jax.shard_map(
        per_device,
        mesh=mesh,
        in_specs=placed,
        out_specs=(
            P("dp", "seq", None),
            P("dp", "seq", None),
            P("seq", None),
            P("seq", None),
            P("seq", None),
        ),
        check_vma=False,
    )
```

```python
import math

import jax
import jax.numpy as jnp
from jax import lax
from jax.experimental import pallas as pl
from jax.experimental.pallas import tpu as pltpu
from jax.sharding import PartitionSpec as P

HD = 64
GROUP = 8


masked_score = -1e30
query_group = 4
RING_Z = 8


def head_kernel(table_ref, count_ref, q_ref, g_ref, k_ref, v_ref,
                out_ref, gq_ref, dk_out, dv_out, k_cat, v_cat, dk_ref, dv_ref):
    step = pl.program_id(0)
    per_step = q_ref.shape[0]
    slot_count = table_ref.shape[0] // (pl.num_programs(0) * per_step)
    block_len = q_ref.shape[1]
    head_width = q_ref.shape[-1]
    score_scale = head_width ** (-0.5)

    @pl.when(step == 0)
    def _():
        dk_ref[...] = jnp.zeros_like(dk_ref)
        dv_ref[...] = jnp.zeros_like(dv_ref)

    used = 4 + count_ref[0]
    nt = (((1,), (1,)), ((), ()))
    tn = (((0,), (0,)), ((), ()))
    for sub in range(per_step):
        b = step * per_step + sub
        q = q_ref[sub]
        g = g_ref[sub]
        chosen = [table_ref[b * slot_count + j] for j in range(slot_count)]
        for j in range(slot_count):
            k_cat[j * block_len : (j + 1) * block_len, :] = k_ref[chosen[j]]
            v_cat[j * block_len : (j + 1) * block_len, :] = v_ref[chosen[j]]
        keys = k_cat[...]
        vals = v_cat[...]
        scores = lax.dot_general(q, keys, nt, preferred_element_type=jnp.float32) * score_scale
        slot_of = lax.broadcasted_iota(jnp.int32, (1, slot_count * block_len), 1) // block_len
        scores = jnp.where(slot_of < used, scores, masked_score)
        highest = scores.max(axis=-1, keepdims=True)
        exps = jnp.exp(scores - highest)
        shares = exps / exps.sum(axis=-1, keepdims=True)
        shares_low = shares.astype(jnp.bfloat16)
        attended = jnp.dot(shares_low, vals, preferred_element_type=jnp.float32)
        out_ref[sub] = attended.astype(out_ref.dtype)
        grad_shares = lax.dot_general(g, vals, nt, preferred_element_type=jnp.float32)
        weighted = (grad_shares * shares).sum(axis=-1, keepdims=True)
        grad_scores = (shares * (grad_shares - weighted)).astype(jnp.bfloat16)
        grad_query = jnp.dot(grad_scores, keys, preferred_element_type=jnp.float32)
        gq_ref[sub] = (grad_query * score_scale).astype(gq_ref.dtype)
        dk = lax.dot_general(grad_scores, q, tn, preferred_element_type=jnp.float32) * score_scale
        dv = lax.dot_general(shares_low, g, tn, preferred_element_type=jnp.float32)
        for j in range(slot_count):
            dk_ref[chosen[j]] += dk[j * block_len : (j + 1) * block_len]
            dv_ref[chosen[j]] += dv[j * block_len : (j + 1) * block_len]

    @pl.when(step == pl.num_programs(0) - 1)
    def _():
        dk_out[...] = dk_ref[...].astype(dk_out.dtype)
        dv_out[...] = dv_ref[...].astype(dv_out.dtype)


def head_pass(queries, key_rows, value_rows, grad_head, blocks, extra_count):
    seq_len, head_width = queries.shape
    block_count, slot_count = blocks.shape
    block_len = seq_len // block_count
    tiles = (block_count, block_len, head_width)
    per_step = 4
    one_block = pl.BlockSpec((per_step, block_len, head_width), lambda b, t, c: (b, 0, 0))
    whole = pl.BlockSpec(tiles, lambda b, t, c: (0, 0, 0))
    grid_spec = pltpu.PrefetchScalarGridSpec(
        num_scalar_prefetch=2,
        grid=(block_count // per_step,),
        in_specs=[one_block, one_block, whole, whole],
        out_specs=[one_block, one_block, whole, whole],
        scratch_shapes=[
            pltpu.VMEM((slot_count * block_len, head_width), jnp.bfloat16),
            pltpu.VMEM((slot_count * block_len, head_width), jnp.bfloat16),
            pltpu.VMEM(tiles, jnp.float32),
            pltpu.VMEM(tiles, jnp.float32),
        ],
    )
    flops = 2 * seq_len * slot_count * block_len * head_width * 6
    attended, grad_query, grad_k, grad_v = pl.pallas_call(
        head_kernel,
        grid_spec=grid_spec,
        out_shape=[
            jax.ShapeDtypeStruct(tiles, jnp.bfloat16),
            jax.ShapeDtypeStruct(tiles, jnp.bfloat16),
            jax.ShapeDtypeStruct(tiles, jnp.bfloat16),
            jax.ShapeDtypeStruct(tiles, jnp.bfloat16),
        ],
        compiler_params=pltpu.CompilerParams(dimension_semantics=("arbitrary",)),
        cost_estimate=pl.CostEstimate(
            flops=flops,
            transcendentals=seq_len * slot_count * block_len,
            bytes_accessed=seq_len * head_width * 2 * 6 + seq_len * head_width * 4 * 2,
        ),
    )(
        blocks.reshape(-1),
        jnp.reshape(extra_count, (1,)),
        queries.reshape(tiles),
        grad_head.reshape(tiles),
        key_rows.reshape(tiles),
        value_rows.reshape(tiles),
    )
    summed = jnp.concatenate([grad_k, grad_v], axis=-1)
    return (
        attended.reshape(seq_len, head_width),
        grad_query.reshape(seq_len, head_width),
        summed.reshape(seq_len, 2 * head_width),
    )


def ring_reduce_scatter(chunk, ring, stride, position):
    seq_devices = lax.axis_size("seq")
    group = ring * stride
    me = (position // stride) % ring
    ahead = [
        (s, (s // group) * group + (((s // stride) % ring + 1) % ring) * stride + s % stride)
        for s in range(seq_devices)
    ]
    behind = [(b, a) for (a, b) in ahead]
    total = []
    for side, perm, sign in ((0, ahead, 1), (1, behind, -1)):
        buf = chunk((me - sign) % ring, side)
        for k in range(ring - 1):
            got = lax.ppermute(buf, "seq", perm)
            own = chunk((me - sign * (2 + k)) % ring, side)
            buf = (got.astype(jnp.float32) + own.astype(jnp.float32)).astype(jnp.bfloat16)
        total.append(buf)
    return jnp.concatenate(total, axis=-1)


def direct_sum(pieces, axis_name, size, stride, mine):
    devices = lax.axis_size(axis_name)
    group = size * stride
    got = [lax.dynamic_index_in_dim(pieces, mine, 0, keepdims=False)]
    for d in range(1, size):
        perm = [
            (i, (i // group) * group + (((i // stride) % size + d) % size) * stride + i % stride)
            for i in range(devices)
        ]
        got.append(lax.ppermute(
            lax.dynamic_index_in_dim(pieces, (mine + d) % size, 0, keepdims=False), axis_name, perm
        ))
    return got


def ring_gather_weights(piece, position, dp_index):
    dp_devices = lax.axis_size("dp")
    seq_devices = lax.axis_size("seq")
    y_count = seq_devices // RING_Z
    sizes = {"z": RING_Z, "y": y_count}

    def step_to(s, dim, shift):
        y, z = s // RING_Z, s % RING_Z
        if dim == "z":
            return y * RING_Z + (z + shift) % RING_Z
        return ((y + shift) % y_count) * RING_Z + z

    def ring(x, which, dim):
        n = sizes[dim]
        got = [x]
        for shift, steps in ((1, n // 2), (-1, n - 1 - n // 2)):
            perm = [
                (d * seq_devices + s, d * seq_devices + step_to(s, dim, shift))
                for d in range(dp_devices) if d % 2 == which
                for s in range(seq_devices)
            ]
            cur = x
            for _ in range(steps):
                cur = lax.ppermute(cur, ("dp", "seq"), perm)
                got.append(cur)
        ahead = got[1 : 1 + n // 2]
        behind = got[1 + n // 2 :]
        return jnp.stack([x] + ahead + behind[::-1])

    first = ring(ring(piece, 0, "z"), 0, "y")
    second = ring(ring(piece, 1, "y"), 1, "z")
    return first.reshape(-1, piece.shape[-1]), second.reshape(-1, piece.shape[-1])


def ring_blocks(position, z_first):
    seq_devices = lax.axis_size("seq")
    y_count = seq_devices // RING_Z
    y, z = position // RING_Z, position % RING_Z
    dy = jnp.arange(y_count)
    dz = jnp.arange(RING_Z)
    if z_first:
        origin = ((y - dy) % y_count)[:, None] * RING_Z + ((z - dz) % RING_Z)[None, :]
    else:
        origin = ((y - dy) % y_count)[None, :] * RING_Z + ((z - dz) % RING_Z)[:, None]
    return origin.reshape(-1)


def per_device(activations, w_query, w_key, w_value, key_blocks, random_count, grad_out):
    seq_devices = lax.axis_size("seq")
    dp_devices = lax.axis_size("dp")
    position = lax.axis_index("seq")
    dp_index = lax.axis_index("dp")
    tokens = activations[0]
    grad_rows = grad_out[0]
    tok_count = tokens.shape[0]
    heads = w_query.shape[1] // HD
    kv_heads = w_key.shape[1] // HD
    query_cols = heads * HD
    kv_cols = kv_heads * HD
    all_cols = query_cols + 2 * kv_cols
    w_local = jnp.concatenate([w_query, w_key, w_value], axis=1)
    half = all_cols // 2
    core = dp_index % 2
    pairs = [(i, i ^ 1) for i in range(dp_devices)]
    grad_pieces = grad_rows.reshape(tok_count, heads, HD).transpose(1, 0, 2)
    head_grad = lax.all_to_all(grad_pieces, "seq", split_axis=0, concat_axis=1, tiled=True)[0]
    by_z, by_y = ring_gather_weights(
        lax.dynamic_slice_in_dim(w_local, core * half, half, axis=1), position, dp_index
    )
    w_mine = jnp.where(core == 0, by_z, by_y)
    w_other = lax.ppermute(w_mine, "dp", pairs)
    order_z, order_y = ring_blocks(position, True), ring_blocks(position, False)
    order_mine = jnp.where(core == 0, order_z, order_y)
    order_other = jnp.where(core == 0, order_y, order_z)
    feat = w_local.shape[0]
    token_blocks = tokens.reshape(tok_count, seq_devices, feat)
    tokens_mine = jnp.take(token_blocks, order_mine, axis=1).reshape(tok_count, -1)
    tokens_other = jnp.take(token_blocks, order_other, axis=1).reshape(tok_count, -1)
    proj_mine = jnp.dot(tokens_mine, w_mine, preferred_element_type=jnp.float32).astype(jnp.bfloat16)
    proj_other = jnp.dot(tokens_other, w_other, preferred_element_type=jnp.float32).astype(jnp.bfloat16)
    projected = jnp.zeros((tok_count, all_cols), jnp.bfloat16)
    projected = lax.dynamic_update_slice_in_dim(projected, proj_mine, core * half, axis=1)
    projected = lax.dynamic_update_slice_in_dim(projected, proj_other, (1 - core) * half, axis=1)
    queries = projected[:, :query_cols]
    key_proj = projected[:, query_cols : query_cols + kv_cols]
    value_proj = projected[:, query_cols + kv_cols :]
    query_pieces = queries.reshape(tok_count, heads, HD).transpose(1, 0, 2)
    paired = jnp.concatenate(
        [key_proj.reshape(tok_count, kv_heads, HD), value_proj.reshape(tok_count, kv_heads, HD)],
        axis=2,
    )
    kv_pieces = jnp.repeat(paired.transpose(1, 0, 2), GROUP, axis=0)
    sent = jnp.concatenate([query_pieces, kv_pieces], axis=2)
    landed = lax.all_to_all(sent, "seq", split_axis=0, concat_axis=1, tiled=True)[0]
    head_q = landed[:, :HD]
    head_k = landed[:, HD : 2 * HD]
    head_v = landed[:, 2 * HD :]
    blocks_mine = lax.dynamic_index_in_dim(key_blocks, position, 0, keepdims=False)
    count_mine = lax.dynamic_index_in_dim(random_count, position, 0, keepdims=False)
    attended, grad_query, grad_kv = head_pass(
        head_q, head_k, head_v, head_grad, blocks_mine, count_mine
    )
    back_sent = jnp.concatenate(
        [
            attended.reshape(seq_devices, tok_count, HD),
            grad_query.reshape(seq_devices, tok_count, HD),
            grad_kv.astype(jnp.bfloat16).reshape(seq_devices, tok_count, 2 * HD),
        ],
        axis=2,
    )
    back = lax.all_to_all(back_sent, "seq", split_axis=0, concat_axis=0, tiled=True)
    back_out = back[:, :, :HD]
    back_query = back[:, :, HD : 2 * HD]
    back_kv = back[:, :, 2 * HD :]
    out_rows = back_out.transpose(1, 0, 2).reshape(tok_count, heads * HD)
    grad_q_rows = back_query.transpose(1, 0, 2).reshape(tok_count, heads * HD)
    kv_sum = jnp.sum(
        back_kv.reshape(kv_heads, GROUP, tok_count, 2 * HD), axis=1, dtype=jnp.float32
    ).astype(jnp.bfloat16)
    grad_k_rows = kv_sum[:, :, :HD].transpose(1, 0, 2).reshape(tok_count, kv_heads * HD)
    grad_v_rows = kv_sum[:, :, HD:].transpose(1, 0, 2).reshape(tok_count, kv_heads * HD)
    combined = jnp.concatenate([grad_q_rows, grad_k_rows, grad_v_rows], axis=1)
    contract = (((1,), (1,)), ((), ()))
    comb_mine = lax.dynamic_slice_in_dim(combined, core * half, half, axis=1)
    comb_other = lax.dynamic_slice_in_dim(combined, (1 - core) * half, half, axis=1)
    def natural(part, order):
        back = jnp.zeros_like(order).at[order].set(jnp.arange(seq_devices, dtype=order.dtype))
        return jnp.take(part.reshape(tok_count, seq_devices, feat), back, axis=1).reshape(tok_count, -1)

    grad_x_rows = (
        natural(lax.dot_general(comb_mine, w_mine, contract, preferred_element_type=jnp.float32), order_mine)
        + natural(lax.dot_general(comb_other, w_other, contract, preferred_element_type=jnp.float32), order_other)
    ).astype(jnp.bfloat16)
    factor = 1.0 / math.sqrt(tok_count * seq_devices * dp_devices)
    over_tokens = (((0,), (0,)), ((), ()))
    y_count = seq_devices // RING_Z
    rows = tokens.shape[1] // seq_devices
    span = y_count * rows
    quarter = half // 2
    tok4 = tokens.reshape(tok_count, y_count, RING_Z, rows)
    z_me = position % RING_Z

    def ring_tokens(sign):
        order = (z_me - sign * (1 + jnp.arange(RING_Z))) % RING_Z
        return jnp.take(tok4, order, axis=2).transpose(0, 2, 1, 3).reshape(tok_count, -1)

    def term_t(columns, toks):
        return (
            lax.dot_general(columns, toks, over_tokens, preferred_element_type=jnp.float32)
            * factor
        ).astype(jnp.bfloat16)

    signs = (1, -1)
    toks = [ring_tokens(sign) for sign in signs]
    give = jnp.stack(
        [term_t(comb_other[:, i * quarter : (i + 1) * quarter], toks[i]) for i in range(2)]
    )
    got = lax.ppermute(give, "dp", pairs)
    keep = [term_t(comb_mine[:, i * quarter : (i + 1) * quarter], toks[i]) for i in range(2)]
    grad_x_rows, keep = lax.optimization_barrier((grad_x_rows, keep))
    ahead = [(s, (s // RING_Z) * RING_Z + (s % RING_Z + 1) % RING_Z) for s in range(seq_devices)]
    behind = [(b, a) for (a, b) in ahead]
    ends = []
    for i, perm in enumerate((ahead, behind)):

        def chunk(k):
            piece = slice(k * span, (k + 1) * span)
            return (
                keep[i][:, piece].astype(jnp.float32) + got[i][:, piece].astype(jnp.float32)
            ).astype(jnp.bfloat16)

        buf = chunk(0)
        for k in range(RING_Z - 1):
            arrived = lax.ppermute(buf, "seq", perm)
            buf = (arrived.astype(jnp.float32) + chunk(k + 1).astype(jnp.float32)).astype(jnp.bfloat16)
        ends.append(buf)
    by_y = jnp.concatenate(ends, axis=0).reshape(half, y_count, rows).transpose(1, 2, 0)
    from_y = direct_sum(by_y, "seq", y_count, RING_Z, position // RING_Z)
    total = from_y[0].astype(jnp.float32)
    for piece in from_y[1:]:
        total = total + piece.astype(jnp.float32)
    part = total.astype(jnp.bfloat16)
    chips = dp_devices // 2
    chip = dp_index // 2
    from_x = direct_sum(jnp.broadcast_to(part, (chips,) + part.shape), "dp", chips, 2, chip)
    by_offset = jnp.stack(from_x)
    in_order = jnp.take(by_offset, (chip - jnp.arange(chips)) % chips, axis=0)
    part = jnp.sum(in_order.astype(jnp.float32), axis=0).astype(jnp.bfloat16)
    other_half = lax.ppermute(part, "dp", pairs)
    first = jnp.where(core == 0, part, other_half)
    second = jnp.where(core == 0, other_half, part)
    grad_all = jnp.concatenate([first, second], axis=1)
    grad_wq = grad_all[:, :query_cols]
    grad_wk = grad_all[:, query_cols : query_cols + kv_cols]
    grad_wv = grad_all[:, query_cols + kv_cols :]
    return (out_rows[None], grad_x_rows[None], grad_wq, grad_wk, grad_wv)


def solution(mesh):
    placed = (
        P("dp", "seq", None),
        P("seq", None),
        P("seq", None),
        P("seq", None),
        P(),
        P(),
        P("dp", "seq", None),
    )
    return jax.shard_map(
        per_device,
        mesh=mesh,
        in_specs=placed,
        out_specs=(
            P("dp", "seq", None),
            P("dp", "seq", None),
            P("seq", None),
            P("seq", None),
            P("seq", None),
        ),
        check_vma=False,
    )
```

```python
import math

import jax
import jax.numpy as jnp
from jax import lax
from jax.experimental import pallas as pl
from jax.experimental.pallas import tpu as pltpu
from jax.sharding import PartitionSpec as P

HD = 64
GROUP = 8


masked_score = -1e30
query_group = 4
RING_Z = 8


def head_kernel(table_ref, count_ref, q_ref, g_ref, k_ref, v_ref,
                out_ref, gq_ref, dk_ref, dv_ref, k_cat, v_cat):
    step = pl.program_id(0)
    per_step = q_ref.shape[0]
    slot_count = table_ref.shape[0] // (pl.num_programs(0) * per_step)
    block_len = q_ref.shape[1]
    head_width = q_ref.shape[-1]
    score_scale = head_width ** (-0.5)

    @pl.when(step == 0)
    def _():
        dk_ref[...] = jnp.zeros_like(dk_ref)
        dv_ref[...] = jnp.zeros_like(dv_ref)

    used = 4 + count_ref[0]
    nt = (((1,), (1,)), ((), ()))
    tn = (((0,), (0,)), ((), ()))
    for sub in range(per_step):
        b = step * per_step + sub
        q = q_ref[sub]
        g = g_ref[sub]
        chosen = [table_ref[b * slot_count + j] for j in range(slot_count)]
        for j in range(slot_count):
            k_cat[j * block_len : (j + 1) * block_len, :] = k_ref[chosen[j]]
            v_cat[j * block_len : (j + 1) * block_len, :] = v_ref[chosen[j]]
        keys = k_cat[...]
        vals = v_cat[...]
        scores = lax.dot_general(q, keys, nt, preferred_element_type=jnp.float32) * score_scale
        slot_of = lax.broadcasted_iota(jnp.int32, (1, slot_count * block_len), 1) // block_len
        scores = jnp.where(slot_of < used, scores, masked_score)
        highest = scores.max(axis=-1, keepdims=True)
        exps = jnp.exp(scores - highest)
        shares = exps / exps.sum(axis=-1, keepdims=True)
        shares_low = shares.astype(jnp.bfloat16)
        attended = jnp.dot(shares_low, vals, preferred_element_type=jnp.float32)
        out_ref[sub] = attended.astype(out_ref.dtype)
        grad_shares = lax.dot_general(g, vals, nt, preferred_element_type=jnp.float32)
        weighted = (grad_shares * shares).sum(axis=-1, keepdims=True)
        grad_scores = (shares * (grad_shares - weighted)).astype(jnp.bfloat16)
        grad_query = jnp.dot(grad_scores, keys, preferred_element_type=jnp.float32)
        gq_ref[sub] = (grad_query * score_scale).astype(gq_ref.dtype)
        dk = lax.dot_general(grad_scores, q, tn, preferred_element_type=jnp.float32) * score_scale
        dv = lax.dot_general(shares_low, g, tn, preferred_element_type=jnp.float32)
        for j in range(slot_count):
            dk_ref[chosen[j]] += dk[j * block_len : (j + 1) * block_len]
            dv_ref[chosen[j]] += dv[j * block_len : (j + 1) * block_len]


def head_pass(queries, key_rows, value_rows, grad_head, blocks, extra_count):
    seq_len, head_width = queries.shape
    block_count, slot_count = blocks.shape
    block_len = seq_len // block_count
    tiles = (block_count, block_len, head_width)
    per_step = 4
    one_block = pl.BlockSpec((per_step, block_len, head_width), lambda b, t, c: (b, 0, 0))
    whole = pl.BlockSpec(tiles, lambda b, t, c: (0, 0, 0))
    grid_spec = pltpu.PrefetchScalarGridSpec(
        num_scalar_prefetch=2,
        grid=(block_count // per_step,),
        in_specs=[one_block, one_block, whole, whole],
        out_specs=[one_block, one_block, whole, whole],
        scratch_shapes=[
            pltpu.VMEM((slot_count * block_len, head_width), jnp.bfloat16),
            pltpu.VMEM((slot_count * block_len, head_width), jnp.bfloat16),
        ],
    )
    flops = 2 * seq_len * slot_count * block_len * head_width * 6
    attended, grad_query, grad_k, grad_v = pl.pallas_call(
        head_kernel,
        grid_spec=grid_spec,
        out_shape=[
            jax.ShapeDtypeStruct(tiles, jnp.bfloat16),
            jax.ShapeDtypeStruct(tiles, jnp.bfloat16),
            jax.ShapeDtypeStruct(tiles, jnp.float32),
            jax.ShapeDtypeStruct(tiles, jnp.float32),
        ],
        compiler_params=pltpu.CompilerParams(dimension_semantics=("arbitrary",)),
        cost_estimate=pl.CostEstimate(
            flops=flops,
            transcendentals=seq_len * slot_count * block_len,
            bytes_accessed=seq_len * head_width * 2 * 6 + seq_len * head_width * 4 * 2,
        ),
    )(
        blocks.reshape(-1),
        jnp.reshape(extra_count, (1,)),
        queries.reshape(tiles),
        grad_head.reshape(tiles),
        key_rows.reshape(tiles),
        value_rows.reshape(tiles),
    )
    summed = jnp.concatenate([grad_k, grad_v], axis=-1)
    return (
        attended.reshape(seq_len, head_width),
        grad_query.reshape(seq_len, head_width),
        summed.reshape(seq_len, 2 * head_width),
    )


def ring_reduce_scatter(chunk, ring, stride, position):
    seq_devices = lax.axis_size("seq")
    group = ring * stride
    me = (position // stride) % ring
    ahead = [
        (s, (s // group) * group + (((s // stride) % ring + 1) % ring) * stride + s % stride)
        for s in range(seq_devices)
    ]
    behind = [(b, a) for (a, b) in ahead]
    total = []
    for side, perm, sign in ((0, ahead, 1), (1, behind, -1)):
        buf = chunk((me - sign) % ring, side)
        for k in range(ring - 1):
            got = lax.ppermute(buf, "seq", perm)
            own = chunk((me - sign * (2 + k)) % ring, side)
            buf = (got.astype(jnp.float32) + own.astype(jnp.float32)).astype(jnp.bfloat16)
        total.append(buf)
    return jnp.concatenate(total, axis=-1)


def direct_sum(pieces, axis_name, size, stride, mine):
    devices = lax.axis_size(axis_name)
    group = size * stride
    got = [lax.dynamic_index_in_dim(pieces, mine, 0, keepdims=False)]
    for d in range(1, size):
        perm = [
            (i, (i // group) * group + (((i // stride) % size + d) % size) * stride + i % stride)
            for i in range(devices)
        ]
        got.append(lax.ppermute(
            lax.dynamic_index_in_dim(pieces, (mine + d) % size, 0, keepdims=False), axis_name, perm
        ))
    return got


def ring_gather_weights(piece, position, dp_index):
    dp_devices = lax.axis_size("dp")
    seq_devices = lax.axis_size("seq")
    y_count = seq_devices // RING_Z
    sizes = {"z": RING_Z, "y": y_count}

    def step_to(s, dim, shift):
        y, z = s // RING_Z, s % RING_Z
        if dim == "z":
            return y * RING_Z + (z + shift) % RING_Z
        return ((y + shift) % y_count) * RING_Z + z

    def ring(x, which, dim):
        n = sizes[dim]
        got = [x]
        for shift, steps in ((1, n // 2), (-1, n - 1 - n // 2)):
            perm = [
                (d * seq_devices + s, d * seq_devices + step_to(s, dim, shift))
                for d in range(dp_devices) if d % 2 == which
                for s in range(seq_devices)
            ]
            cur = x
            for _ in range(steps):
                cur = lax.ppermute(cur, ("dp", "seq"), perm)
                got.append(cur)
        ahead = got[1 : 1 + n // 2]
        behind = got[1 + n // 2 :]
        return jnp.stack([x] + ahead + behind[::-1])

    n_z, n_y = sizes["z"], sizes["y"]
    got = {0: [], 1: []}
    for shift, steps in ((1, {0: n_z // 2, 1: n_y // 2}), (-1, {0: n_z - 1 - n_z // 2, 1: n_y - 1 - n_y // 2})):
        cur = piece
        for k in range(max(steps.values())):
            perm = [
                (d * seq_devices + s, d * seq_devices + step_to(s, "z" if d % 2 == 0 else "y", shift))
                for d in range(dp_devices) if k < steps[d % 2]
                for s in range(seq_devices)
            ]
            cur = lax.ppermute(cur, ("dp", "seq"), perm)
            for which in (0, 1):
                if k < steps[which]:
                    got[which].append(cur)
    lists = {}
    for which, n in ((0, n_z), (1, n_y)):
        ahead = got[which][: n // 2]
        behind = got[which][n // 2 :]
        lists[which] = jnp.stack([piece] + ahead + behind[::-1])
    first = ring(lists[0], 0, "y")
    second = ring(lists[1], 1, "z")
    return first.reshape(-1, piece.shape[-1]), second.reshape(-1, piece.shape[-1])


def ring_blocks(position, z_first):
    seq_devices = lax.axis_size("seq")
    y_count = seq_devices // RING_Z
    y, z = position // RING_Z, position % RING_Z
    dy = jnp.arange(y_count)
    dz = jnp.arange(RING_Z)
    if z_first:
        origin = ((y - dy) % y_count)[:, None] * RING_Z + ((z - dz) % RING_Z)[None, :]
    else:
        origin = ((y - dy) % y_count)[None, :] * RING_Z + ((z - dz) % RING_Z)[:, None]
    return origin.reshape(-1)


def per_device(activations, w_query, w_key, w_value, key_blocks, random_count, grad_out):
    seq_devices = lax.axis_size("seq")
    dp_devices = lax.axis_size("dp")
    position = lax.axis_index("seq")
    dp_index = lax.axis_index("dp")
    tokens = activations[0]
    grad_rows = grad_out[0]
    tok_count = tokens.shape[0]
    heads = w_query.shape[1] // HD
    kv_heads = w_key.shape[1] // HD
    query_cols = heads * HD
    kv_cols = kv_heads * HD
    all_cols = query_cols + 2 * kv_cols
    w_local = jnp.concatenate([w_query, w_key, w_value], axis=1)
    half = all_cols // 2
    core = dp_index % 2
    pairs = [(i, i ^ 1) for i in range(dp_devices)]
    grad_pieces = grad_rows.reshape(tok_count, heads, HD).transpose(1, 0, 2)
    head_grad = lax.all_to_all(grad_pieces, "seq", split_axis=0, concat_axis=1, tiled=True)[0]
    by_z, by_y = ring_gather_weights(
        lax.dynamic_slice_in_dim(w_local, core * half, half, axis=1), position, dp_index
    )
    w_mine = jnp.where(core == 0, by_z, by_y)
    w_other = lax.ppermute(w_mine, "dp", pairs)
    order_z, order_y = ring_blocks(position, True), ring_blocks(position, False)
    order_mine = jnp.where(core == 0, order_z, order_y)
    order_other = jnp.where(core == 0, order_y, order_z)
    feat = w_local.shape[0]
    token_blocks = tokens.reshape(tok_count, seq_devices, feat)
    tokens_mine = jnp.take(token_blocks, order_mine, axis=1).reshape(tok_count, -1)
    tokens_other = jnp.take(token_blocks, order_other, axis=1).reshape(tok_count, -1)
    proj_mine = jnp.dot(tokens_mine, w_mine, preferred_element_type=jnp.float32).astype(jnp.bfloat16)
    proj_other = jnp.dot(tokens_other, w_other, preferred_element_type=jnp.float32).astype(jnp.bfloat16)
    projected = jnp.zeros((tok_count, all_cols), jnp.bfloat16)
    projected = lax.dynamic_update_slice_in_dim(projected, proj_mine, core * half, axis=1)
    projected = lax.dynamic_update_slice_in_dim(projected, proj_other, (1 - core) * half, axis=1)
    queries = projected[:, :query_cols]
    key_proj = projected[:, query_cols : query_cols + kv_cols]
    value_proj = projected[:, query_cols + kv_cols :]
    query_pieces = queries.reshape(tok_count, heads, HD).transpose(1, 0, 2)
    paired = jnp.concatenate(
        [key_proj.reshape(tok_count, kv_heads, HD), value_proj.reshape(tok_count, kv_heads, HD)],
        axis=2,
    )
    kv_pieces = jnp.repeat(paired.transpose(1, 0, 2), GROUP, axis=0)
    sent = jnp.concatenate([query_pieces, kv_pieces], axis=2)
    landed = lax.all_to_all(sent, "seq", split_axis=0, concat_axis=1, tiled=True)[0]
    head_q = landed[:, :HD]
    head_k = landed[:, HD : 2 * HD]
    head_v = landed[:, 2 * HD :]
    blocks_mine = lax.dynamic_index_in_dim(key_blocks, position, 0, keepdims=False)
    count_mine = lax.dynamic_index_in_dim(random_count, position, 0, keepdims=False)
    attended, grad_query, grad_kv = head_pass(
        head_q, head_k, head_v, head_grad, blocks_mine, count_mine
    )
    back_sent = jnp.concatenate(
        [
            attended.reshape(seq_devices, tok_count, HD),
            grad_query.reshape(seq_devices, tok_count, HD),
            grad_kv.astype(jnp.bfloat16).reshape(seq_devices, tok_count, 2 * HD),
        ],
        axis=2,
    )
    back = lax.all_to_all(back_sent, "seq", split_axis=0, concat_axis=0, tiled=True)
    back_out = back[:, :, :HD]
    back_query = back[:, :, HD : 2 * HD]
    back_kv = back[:, :, 2 * HD :]
    out_rows = back_out.transpose(1, 0, 2).reshape(tok_count, heads * HD)
    grad_q_rows = back_query.transpose(1, 0, 2).reshape(tok_count, heads * HD)
    kv_sum = jnp.sum(
        back_kv.reshape(kv_heads, GROUP, tok_count, 2 * HD), axis=1, dtype=jnp.float32
    ).astype(jnp.bfloat16)
    grad_k_rows = kv_sum[:, :, :HD].transpose(1, 0, 2).reshape(tok_count, kv_heads * HD)
    grad_v_rows = kv_sum[:, :, HD:].transpose(1, 0, 2).reshape(tok_count, kv_heads * HD)
    combined = jnp.concatenate([grad_q_rows, grad_k_rows, grad_v_rows], axis=1)
    contract = (((1,), (1,)), ((), ()))
    comb_mine = lax.dynamic_slice_in_dim(combined, core * half, half, axis=1)
    comb_other = lax.dynamic_slice_in_dim(combined, (1 - core) * half, half, axis=1)
    def natural(part, order):
        back = jnp.zeros_like(order).at[order].set(jnp.arange(seq_devices, dtype=order.dtype))
        return jnp.take(part.reshape(tok_count, seq_devices, feat), back, axis=1).reshape(tok_count, -1)

    grad_x_rows = (
        natural(lax.dot_general(comb_mine, w_mine, contract, preferred_element_type=jnp.float32), order_mine)
        + natural(lax.dot_general(comb_other, w_other, contract, preferred_element_type=jnp.float32), order_other)
    ).astype(jnp.bfloat16)
    factor = 1.0 / math.sqrt(tok_count * seq_devices * dp_devices)
    over_tokens = (((0,), (0,)), ((), ()))
    y_count = seq_devices // RING_Z
    rows = tokens.shape[1] // seq_devices
    span = y_count * rows
    quarter = half // 2
    tok4 = tokens.reshape(tok_count, y_count, RING_Z, rows)
    z_me = position % RING_Z

    def ring_tokens(sign):
        order = (z_me - sign * (1 + jnp.arange(RING_Z))) % RING_Z
        return jnp.take(tok4, order, axis=2).transpose(0, 2, 1, 3).reshape(tok_count, -1)

    def term_t(columns, toks):
        return (
            lax.dot_general(columns, toks, over_tokens, preferred_element_type=jnp.float32)
            * factor
        ).astype(jnp.bfloat16)

    signs = (1, -1)
    toks = [ring_tokens(sign) for sign in signs]
    give = jnp.stack(
        [term_t(comb_other[:, i * quarter : (i + 1) * quarter], toks[i]) for i in range(2)]
    )
    got = lax.ppermute(give, "dp", pairs)
    keep = [term_t(comb_mine[:, i * quarter : (i + 1) * quarter], toks[i]) for i in range(2)]
    grad_x_rows, keep = lax.optimization_barrier((grad_x_rows, keep))
    ahead = [(s, (s // RING_Z) * RING_Z + (s % RING_Z + 1) % RING_Z) for s in range(seq_devices)]
    behind = [(b, a) for (a, b) in ahead]
    ends = []
    for i, perm in enumerate((ahead, behind)):

        def chunk(k):
            piece = slice(k * span, (k + 1) * span)
            return (
                keep[i][:, piece].astype(jnp.float32) + got[i][:, piece].astype(jnp.float32)
            ).astype(jnp.bfloat16)

        buf = chunk(0)
        for k in range(RING_Z - 1):
            arrived = lax.ppermute(buf, "seq", perm)
            buf = (arrived.astype(jnp.float32) + chunk(k + 1).astype(jnp.float32)).astype(jnp.bfloat16)
        ends.append(buf)
    by_y = jnp.concatenate(ends, axis=0).reshape(half, y_count, rows).transpose(1, 2, 0)
    from_y = direct_sum(by_y, "seq", y_count, RING_Z, position // RING_Z)
    total = from_y[0].astype(jnp.float32)
    for piece in from_y[1:]:
        total = total + piece.astype(jnp.float32)
    part = total.astype(jnp.bfloat16)
    chips = dp_devices // 2
    chip = dp_index // 2
    from_x = direct_sum(jnp.broadcast_to(part, (chips,) + part.shape), "dp", chips, 2, chip)
    by_offset = jnp.stack(from_x)
    in_order = jnp.take(by_offset, (chip - jnp.arange(chips)) % chips, axis=0)
    part = jnp.sum(in_order.astype(jnp.float32), axis=0).astype(jnp.bfloat16)
    other_half = lax.ppermute(part, "dp", pairs)
    first = jnp.where(core == 0, part, other_half)
    second = jnp.where(core == 0, other_half, part)
    grad_all = jnp.concatenate([first, second], axis=1)
    grad_wq = grad_all[:, :query_cols]
    grad_wk = grad_all[:, query_cols : query_cols + kv_cols]
    grad_wv = grad_all[:, query_cols + kv_cols :]
    return (out_rows[None], grad_x_rows[None], grad_wq, grad_wk, grad_wv)


def solution(mesh):
    placed = (
        P("dp", "seq", None),
        P("seq", None),
        P("seq", None),
        P("seq", None),
        P(),
        P(),
        P("dp", "seq", None),
    )
    return jax.shard_map(
        per_device,
        mesh=mesh,
        in_specs=placed,
        out_specs=(
            P("dp", "seq", None),
            P("dp", "seq", None),
            P("seq", None),
            P("seq", None),
            P("seq", None),
        ),
        check_vma=False,
    )
```

```python
import math

import jax
import jax.numpy as jnp
from jax import lax
from jax.experimental import pallas as pl
from jax.experimental.pallas import tpu as pltpu
from jax.sharding import PartitionSpec as P

HD = 64
GROUP = 8


masked_score = -1e30
query_group = 4
RING_Z = 8


def head_kernel(table_ref, count_ref, q_ref, g_ref, k_ref, v_ref,
                out_ref, gq_ref, dk_ref, dv_ref, k_cat, v_cat):
    step = pl.program_id(0)
    per_step = q_ref.shape[0]
    slot_count = table_ref.shape[0] // (pl.num_programs(0) * per_step)
    block_len = q_ref.shape[1]
    head_width = q_ref.shape[-1]
    score_scale = head_width ** (-0.5)

    @pl.when(step == 0)
    def _():
        dk_ref[...] = jnp.zeros_like(dk_ref)
        dv_ref[...] = jnp.zeros_like(dv_ref)

    used = 4 + count_ref[0]
    nt = (((1,), (1,)), ((), ()))
    tn = (((0,), (0,)), ((), ()))
    for sub in range(per_step):
        b = step * per_step + sub
        q = q_ref[sub]
        g = g_ref[sub]
        chosen = [table_ref[b * slot_count + j] for j in range(slot_count)]
        for j in range(slot_count):
            k_cat[j * block_len : (j + 1) * block_len, :] = k_ref[chosen[j]]
            v_cat[j * block_len : (j + 1) * block_len, :] = v_ref[chosen[j]]
        keys = k_cat[...]
        vals = v_cat[...]
        scores = lax.dot_general(q, keys, nt, preferred_element_type=jnp.float32) * score_scale
        slot_of = lax.broadcasted_iota(jnp.int32, (1, slot_count * block_len), 1) // block_len
        scores = jnp.where(slot_of < used, scores, masked_score)
        highest = scores.max(axis=-1, keepdims=True)
        exps = jnp.exp(scores - highest)
        shares = exps / exps.sum(axis=-1, keepdims=True)
        shares_low = shares.astype(jnp.bfloat16)
        attended = jnp.dot(shares_low, vals, preferred_element_type=jnp.float32)
        out_ref[sub] = attended.astype(out_ref.dtype)
        grad_shares = lax.dot_general(g, vals, nt, preferred_element_type=jnp.float32)
        weighted = (grad_shares * shares).sum(axis=-1, keepdims=True)
        grad_scores = (shares * (grad_shares - weighted)).astype(jnp.bfloat16)
        grad_query = jnp.dot(grad_scores, keys, preferred_element_type=jnp.float32)
        gq_ref[sub] = (grad_query * score_scale).astype(gq_ref.dtype)
        dk = lax.dot_general(grad_scores, q, tn, preferred_element_type=jnp.float32) * score_scale
        dv = lax.dot_general(shares_low, g, tn, preferred_element_type=jnp.float32)
        for j in range(slot_count):
            dk_ref[chosen[j]] += dk[j * block_len : (j + 1) * block_len]
            dv_ref[chosen[j]] += dv[j * block_len : (j + 1) * block_len]


def head_pass(queries, key_rows, value_rows, grad_head, blocks, extra_count):
    seq_len, head_width = queries.shape
    block_count, slot_count = blocks.shape
    block_len = seq_len // block_count
    tiles = (block_count, block_len, head_width)
    per_step = 4
    one_block = pl.BlockSpec((per_step, block_len, head_width), lambda b, t, c: (b, 0, 0))
    whole = pl.BlockSpec(tiles, lambda b, t, c: (0, 0, 0))
    grid_spec = pltpu.PrefetchScalarGridSpec(
        num_scalar_prefetch=2,
        grid=(block_count // per_step,),
        in_specs=[one_block, one_block, whole, whole],
        out_specs=[one_block, one_block, whole, whole],
        scratch_shapes=[
            pltpu.VMEM((slot_count * block_len, head_width), jnp.bfloat16),
            pltpu.VMEM((slot_count * block_len, head_width), jnp.bfloat16),
        ],
    )
    flops = 2 * seq_len * slot_count * block_len * head_width * 6
    attended, grad_query, grad_k, grad_v = pl.pallas_call(
        head_kernel,
        grid_spec=grid_spec,
        out_shape=[
            jax.ShapeDtypeStruct(tiles, jnp.bfloat16),
            jax.ShapeDtypeStruct(tiles, jnp.bfloat16),
            jax.ShapeDtypeStruct(tiles, jnp.float32),
            jax.ShapeDtypeStruct(tiles, jnp.float32),
        ],
        compiler_params=pltpu.CompilerParams(dimension_semantics=("arbitrary",)),
        cost_estimate=pl.CostEstimate(
            flops=flops,
            transcendentals=seq_len * slot_count * block_len,
            bytes_accessed=seq_len * head_width * 2 * 6 + seq_len * head_width * 4 * 2,
        ),
    )(
        blocks.reshape(-1),
        jnp.reshape(extra_count, (1,)),
        queries.reshape(tiles),
        grad_head.reshape(tiles),
        key_rows.reshape(tiles),
        value_rows.reshape(tiles),
    )
    summed = jnp.concatenate([grad_k, grad_v], axis=-1)
    return (
        attended.reshape(seq_len, head_width),
        grad_query.reshape(seq_len, head_width),
        summed.reshape(seq_len, 2 * head_width),
    )


def ring_reduce_scatter(chunk, ring, stride, position):
    seq_devices = lax.axis_size("seq")
    group = ring * stride
    me = (position // stride) % ring
    ahead = [
        (s, (s // group) * group + (((s // stride) % ring + 1) % ring) * stride + s % stride)
        for s in range(seq_devices)
    ]
    behind = [(b, a) for (a, b) in ahead]
    total = []
    for side, perm, sign in ((0, ahead, 1), (1, behind, -1)):
        buf = chunk((me - sign) % ring, side)
        for k in range(ring - 1):
            got = lax.ppermute(buf, "seq", perm)
            own = chunk((me - sign * (2 + k)) % ring, side)
            buf = (got.astype(jnp.float32) + own.astype(jnp.float32)).astype(jnp.bfloat16)
        total.append(buf)
    return jnp.concatenate(total, axis=-1)


def direct_sum(pieces, axis_name, size, stride, mine):
    devices = lax.axis_size(axis_name)
    group = size * stride
    got = [lax.dynamic_index_in_dim(pieces, mine, 0, keepdims=False)]
    for d in range(1, size):
        perm = [
            (i, (i // group) * group + (((i // stride) % size + d) % size) * stride + i % stride)
            for i in range(devices)
        ]
        got.append(lax.ppermute(
            lax.dynamic_index_in_dim(pieces, (mine + d) % size, 0, keepdims=False), axis_name, perm
        ))
    return got


def ring_gather_weights(piece, position, dp_index):
    dp_devices = lax.axis_size("dp")
    seq_devices = lax.axis_size("seq")
    y_count = seq_devices // RING_Z
    sizes = {"z": RING_Z, "y": y_count}

    def step_to(s, dim, shift):
        y, z = s // RING_Z, s % RING_Z
        if dim == "z":
            return y * RING_Z + (z + shift) % RING_Z
        return ((y + shift) % y_count) * RING_Z + z

    def ring(x, which, dim):
        n = sizes[dim]
        got = [x]
        for shift, steps in ((1, n // 2), (-1, n - 1 - n // 2)):
            perm = [
                (d * seq_devices + s, d * seq_devices + step_to(s, dim, shift))
                for d in range(dp_devices) if d % 2 == which
                for s in range(seq_devices)
            ]
            cur = x
            for _ in range(steps):
                cur = lax.ppermute(cur, ("dp", "seq"), perm)
                got.append(cur)
        ahead = got[1 : 1 + n // 2]
        behind = got[1 + n // 2 :]
        return jnp.stack([x] + ahead + behind[::-1])

    n_z, n_y = sizes["z"], sizes["y"]
    got = {0: [], 1: []}
    for shift, steps in ((1, {0: n_z // 2, 1: n_y // 2}), (-1, {0: n_z - 1 - n_z // 2, 1: n_y - 1 - n_y // 2})):
        cur = piece
        for k in range(max(steps.values())):
            perm = [
                (d * seq_devices + s, d * seq_devices + step_to(s, "z" if d % 2 == 0 else "y", shift))
                for d in range(dp_devices) if k < steps[d % 2]
                for s in range(seq_devices)
            ]
            cur = lax.ppermute(cur, ("dp", "seq"), perm)
            for which in (0, 1):
                if k < steps[which]:
                    got[which].append(cur)
    lists = {}
    for which, n in ((0, n_z), (1, n_y)):
        ahead = got[which][: n // 2]
        behind = got[which][n // 2 :]
        lists[which] = jnp.stack([piece] + ahead + behind[::-1])
    core = dp_index % 2
    halves = [lists[0][: n_z // 2], lists[0][n_z // 2 :]]
    plans = {0: {1: n_y // 2, -1: n_y - 1 - n_y // 2}, 1: {1: n_z // 2, -1: n_z - 1 - n_z // 2}}
    dims = {0: "y", 1: "z"}
    arrived = {0: {}, 1: {}}
    for shift in (1, -1):
        sends = {0: 2 * plans[0][shift], 1: plans[1][shift]}
        recv = []
        for j in range(max(sends.values())):
            op0 = halves[j] if j < 2 else recv[j - 2]
            op1 = lists[1] if j == 0 else recv[j - 1]
            perm = [
                (d * seq_devices + s, d * seq_devices + step_to(s, dims[d % 2], shift))
                for d in range(dp_devices) if j < sends[d % 2]
                for s in range(seq_devices)
            ]
            recv.append(lax.ppermute(jnp.where(core == 0, op0, op1), ("dp", "seq"), perm))
        arrived[0][shift] = [
            jnp.concatenate(recv[2 * k : 2 * k + 2]) for k in range(plans[0][shift])
        ]
        arrived[1][shift] = recv[: plans[1][shift]]
    first = jnp.stack([lists[0]] + arrived[0][1] + arrived[0][-1][::-1])
    second = jnp.stack([lists[1]] + arrived[1][1] + arrived[1][-1][::-1])
    return first.reshape(-1, piece.shape[-1]), second.reshape(-1, piece.shape[-1])


def ring_blocks(position, z_first):
    seq_devices = lax.axis_size("seq")
    y_count = seq_devices // RING_Z
    y, z = position // RING_Z, position % RING_Z
    dy = jnp.arange(y_count)
    dz = jnp.arange(RING_Z)
    if z_first:
        origin = ((y - dy) % y_count)[:, None] * RING_Z + ((z - dz) % RING_Z)[None, :]
    else:
        origin = ((y - dy) % y_count)[None, :] * RING_Z + ((z - dz) % RING_Z)[:, None]
    return origin.reshape(-1)


def per_device(activations, w_query, w_key, w_value, key_blocks, random_count, grad_out):
    seq_devices = lax.axis_size("seq")
    dp_devices = lax.axis_size("dp")
    position = lax.axis_index("seq")
    dp_index = lax.axis_index("dp")
    tokens = activations[0]
    grad_rows = grad_out[0]
    tok_count = tokens.shape[0]
    heads = w_query.shape[1] // HD
    kv_heads = w_key.shape[1] // HD
    query_cols = heads * HD
    kv_cols = kv_heads * HD
    all_cols = query_cols + 2 * kv_cols
    w_local = jnp.concatenate([w_query, w_key, w_value], axis=1)
    half = all_cols // 2
    core = dp_index % 2
    pairs = [(i, i ^ 1) for i in range(dp_devices)]
    grad_pieces = grad_rows.reshape(tok_count, heads, HD).transpose(1, 0, 2)
    head_grad = lax.all_to_all(grad_pieces, "seq", split_axis=0, concat_axis=1, tiled=True)[0]
    by_z, by_y = ring_gather_weights(
        lax.dynamic_slice_in_dim(w_local, core * half, half, axis=1), position, dp_index
    )
    w_mine = jnp.where(core == 0, by_z, by_y)
    w_other = lax.ppermute(w_mine, "dp", pairs)
    order_z, order_y = ring_blocks(position, True), ring_blocks(position, False)
    order_mine = jnp.where(core == 0, order_z, order_y)
    order_other = jnp.where(core == 0, order_y, order_z)
    feat = w_local.shape[0]
    token_blocks = tokens.reshape(tok_count, seq_devices, feat)
    tokens_mine = jnp.take(token_blocks, order_mine, axis=1).reshape(tok_count, -1)
    tokens_other = jnp.take(token_blocks, order_other, axis=1).reshape(tok_count, -1)
    proj_mine = jnp.dot(tokens_mine, w_mine, preferred_element_type=jnp.float32).astype(jnp.bfloat16)
    proj_other = jnp.dot(tokens_other, w_other, preferred_element_type=jnp.float32).astype(jnp.bfloat16)
    projected = jnp.zeros((tok_count, all_cols), jnp.bfloat16)
    projected = lax.dynamic_update_slice_in_dim(projected, proj_mine, core * half, axis=1)
    projected = lax.dynamic_update_slice_in_dim(projected, proj_other, (1 - core) * half, axis=1)
    queries = projected[:, :query_cols]
    key_proj = projected[:, query_cols : query_cols + kv_cols]
    value_proj = projected[:, query_cols + kv_cols :]
    query_pieces = queries.reshape(tok_count, heads, HD).transpose(1, 0, 2)
    paired = jnp.concatenate(
        [key_proj.reshape(tok_count, kv_heads, HD), value_proj.reshape(tok_count, kv_heads, HD)],
        axis=2,
    )
    kv_pieces = jnp.repeat(paired.transpose(1, 0, 2), GROUP, axis=0)
    sent = jnp.concatenate([query_pieces, kv_pieces], axis=2)
    landed = lax.all_to_all(sent, "seq", split_axis=0, concat_axis=1, tiled=True)[0]
    head_q = landed[:, :HD]
    head_k = landed[:, HD : 2 * HD]
    head_v = landed[:, 2 * HD :]
    blocks_mine = lax.dynamic_index_in_dim(key_blocks, position, 0, keepdims=False)
    count_mine = lax.dynamic_index_in_dim(random_count, position, 0, keepdims=False)
    attended, grad_query, grad_kv = head_pass(
        head_q, head_k, head_v, head_grad, blocks_mine, count_mine
    )
    back_sent = jnp.concatenate(
        [
            attended.reshape(seq_devices, tok_count, HD),
            grad_query.reshape(seq_devices, tok_count, HD),
            grad_kv.astype(jnp.bfloat16).reshape(seq_devices, tok_count, 2 * HD),
        ],
        axis=2,
    )
    back = lax.all_to_all(back_sent, "seq", split_axis=0, concat_axis=0, tiled=True)
    back_out = back[:, :, :HD]
    back_query = back[:, :, HD : 2 * HD]
    back_kv = back[:, :, 2 * HD :]
    out_rows = back_out.transpose(1, 0, 2).reshape(tok_count, heads * HD)
    grad_q_rows = back_query.transpose(1, 0, 2).reshape(tok_count, heads * HD)
    kv_sum = jnp.sum(
        back_kv.reshape(kv_heads, GROUP, tok_count, 2 * HD), axis=1, dtype=jnp.float32
    ).astype(jnp.bfloat16)
    grad_k_rows = kv_sum[:, :, :HD].transpose(1, 0, 2).reshape(tok_count, kv_heads * HD)
    grad_v_rows = kv_sum[:, :, HD:].transpose(1, 0, 2).reshape(tok_count, kv_heads * HD)
    combined = jnp.concatenate([grad_q_rows, grad_k_rows, grad_v_rows], axis=1)
    contract = (((1,), (1,)), ((), ()))
    comb_mine = lax.dynamic_slice_in_dim(combined, core * half, half, axis=1)
    comb_other = lax.dynamic_slice_in_dim(combined, (1 - core) * half, half, axis=1)
    def natural(part, order):
        back = jnp.zeros_like(order).at[order].set(jnp.arange(seq_devices, dtype=order.dtype))
        return jnp.take(part.reshape(tok_count, seq_devices, feat), back, axis=1).reshape(tok_count, -1)

    grad_x_rows = (
        natural(lax.dot_general(comb_mine, w_mine, contract, preferred_element_type=jnp.float32), order_mine)
        + natural(lax.dot_general(comb_other, w_other, contract, preferred_element_type=jnp.float32), order_other)
    ).astype(jnp.bfloat16)
    factor = 1.0 / math.sqrt(tok_count * seq_devices * dp_devices)
    over_tokens = (((0,), (0,)), ((), ()))
    y_count = seq_devices // RING_Z
    rows = tokens.shape[1] // seq_devices
    span = y_count * rows
    quarter = half // 2
    tok4 = tokens.reshape(tok_count, y_count, RING_Z, rows)
    z_me = position % RING_Z

    def ring_tokens(sign):
        order = (z_me - sign * (1 + jnp.arange(RING_Z))) % RING_Z
        return jnp.take(tok4, order, axis=2).transpose(0, 2, 1, 3).reshape(tok_count, -1)

    def term_t(columns, toks):
        return (
            lax.dot_general(columns, toks, over_tokens, preferred_element_type=jnp.float32)
            * factor
        ).astype(jnp.bfloat16)

    signs = (1, -1)
    toks = [ring_tokens(sign) for sign in signs]
    give = jnp.stack(
        [term_t(comb_other[:, i * quarter : (i + 1) * quarter], toks[i]) for i in range(2)]
    )
    got = lax.ppermute(give, "dp", pairs)
    keep = [term_t(comb_mine[:, i * quarter : (i + 1) * quarter], toks[i]) for i in range(2)]
    grad_x_rows, keep = lax.optimization_barrier((grad_x_rows, keep))
    ahead = [(s, (s // RING_Z) * RING_Z + (s % RING_Z + 1) % RING_Z) for s in range(seq_devices)]
    behind = [(b, a) for (a, b) in ahead]
    ends = []
    for i, perm in enumerate((ahead, behind)):

        def chunk(k):
            piece = slice(k * span, (k + 1) * span)
            return (
                keep[i][:, piece].astype(jnp.float32) + got[i][:, piece].astype(jnp.float32)
            ).astype(jnp.bfloat16)

        buf = chunk(0)
        for k in range(RING_Z - 1):
            arrived = lax.ppermute(buf, "seq", perm)
            buf = (arrived.astype(jnp.float32) + chunk(k + 1).astype(jnp.float32)).astype(jnp.bfloat16)
        ends.append(buf)
    by_y = jnp.concatenate(ends, axis=0).reshape(half, y_count, rows).transpose(1, 2, 0)
    from_y = direct_sum(by_y, "seq", y_count, RING_Z, position // RING_Z)
    total = from_y[0].astype(jnp.float32)
    for piece in from_y[1:]:
        total = total + piece.astype(jnp.float32)
    part = total.astype(jnp.bfloat16)
    chips = dp_devices // 2
    chip = dp_index // 2
    from_x = direct_sum(jnp.broadcast_to(part, (chips,) + part.shape), "dp", chips, 2, chip)
    by_offset = jnp.stack(from_x)
    in_order = jnp.take(by_offset, (chip - jnp.arange(chips)) % chips, axis=0)
    part = jnp.sum(in_order.astype(jnp.float32), axis=0).astype(jnp.bfloat16)
    other_half = lax.ppermute(part, "dp", pairs)
    first = jnp.where(core == 0, part, other_half)
    second = jnp.where(core == 0, other_half, part)
    grad_all = jnp.concatenate([first, second], axis=1)
    grad_wq = grad_all[:, :query_cols]
    grad_wk = grad_all[:, query_cols : query_cols + kv_cols]
    grad_wv = grad_all[:, query_cols + kv_cols :]
    return (out_rows[None], grad_x_rows[None], grad_wq, grad_wk, grad_wv)


def solution(mesh):
    placed = (
        P("dp", "seq", None),
        P("seq", None),
        P("seq", None),
        P("seq", None),
        P(),
        P(),
        P("dp", "seq", None),
    )
    return jax.shard_map(
        per_device,
        mesh=mesh,
        in_specs=placed,
        out_specs=(
            P("dp", "seq", None),
            P("dp", "seq", None),
            P("seq", None),
            P("seq", None),
            P("seq", None),
        ),
        check_vma=False,
    )
```

```python
import math

import jax
import jax.numpy as jnp
from jax import lax
from jax.experimental import pallas as pl
from jax.experimental.pallas import tpu as pltpu
from jax.sharding import PartitionSpec as P

HD = 64
GROUP = 8


masked_score = -1e30
query_group = 4
RING_Z = 8


def head_kernel(table_ref, count_ref, q_ref, g_ref, k_ref, v_ref,
                out_ref, gq_ref, dk_ref, dv_ref, k_cat, v_cat):
    step = pl.program_id(0)
    per_step = q_ref.shape[0]
    slot_count = table_ref.shape[0] // (pl.num_programs(0) * per_step)
    block_len = q_ref.shape[1]
    head_width = q_ref.shape[-1]
    score_scale = head_width ** (-0.5)

    @pl.when(step == 0)
    def _():
        dk_ref[...] = jnp.zeros_like(dk_ref)
        dv_ref[...] = jnp.zeros_like(dv_ref)

    used = 4 + count_ref[0]
    nt = (((1,), (1,)), ((), ()))
    tn = (((0,), (0,)), ((), ()))
    for sub in range(per_step):
        b = step * per_step + sub
        q = q_ref[sub]
        g = g_ref[sub]
        chosen = [table_ref[b * slot_count + j] for j in range(slot_count)]
        for j in range(slot_count):
            k_cat[j * block_len : (j + 1) * block_len, :] = k_ref[chosen[j]]
            v_cat[j * block_len : (j + 1) * block_len, :] = v_ref[chosen[j]]
        keys = k_cat[...]
        vals = v_cat[...]
        scores = lax.dot_general(q, keys, nt, preferred_element_type=jnp.float32) * score_scale
        slot_of = lax.broadcasted_iota(jnp.int32, (1, slot_count * block_len), 1) // block_len
        scores = jnp.where(slot_of < used, scores, masked_score)
        highest = scores.max(axis=-1, keepdims=True)
        exps = jnp.exp(scores - highest)
        shares = exps / exps.sum(axis=-1, keepdims=True)
        shares_low = shares.astype(jnp.bfloat16)
        attended = jnp.dot(shares_low, vals, preferred_element_type=jnp.float32)
        out_ref[sub] = attended.astype(out_ref.dtype)
        grad_shares = lax.dot_general(g, vals, nt, preferred_element_type=jnp.float32)
        weighted = (grad_shares * shares).sum(axis=-1, keepdims=True)
        grad_scores = (shares * (grad_shares - weighted)).astype(jnp.bfloat16)
        grad_query = jnp.dot(grad_scores, keys, preferred_element_type=jnp.float32)
        gq_ref[sub] = (grad_query * score_scale).astype(gq_ref.dtype)
        dk = lax.dot_general(grad_scores, q, tn, preferred_element_type=jnp.float32) * score_scale
        dv = lax.dot_general(shares_low, g, tn, preferred_element_type=jnp.float32)
        for j in range(slot_count):
            dk_ref[chosen[j]] += dk[j * block_len : (j + 1) * block_len]
            dv_ref[chosen[j]] += dv[j * block_len : (j + 1) * block_len]


def head_pass(queries, key_rows, value_rows, grad_head, blocks, extra_count):
    seq_len, head_width = queries.shape
    block_count, slot_count = blocks.shape
    block_len = seq_len // block_count
    tiles = (block_count, block_len, head_width)
    per_step = 8
    one_block = pl.BlockSpec((per_step, block_len, head_width), lambda b, t, c: (b, 0, 0))
    whole = pl.BlockSpec(tiles, lambda b, t, c: (0, 0, 0))
    grid_spec = pltpu.PrefetchScalarGridSpec(
        num_scalar_prefetch=2,
        grid=(block_count // per_step,),
        in_specs=[one_block, one_block, whole, whole],
        out_specs=[one_block, one_block, whole, whole],
        scratch_shapes=[
            pltpu.VMEM((slot_count * block_len, head_width), jnp.bfloat16),
            pltpu.VMEM((slot_count * block_len, head_width), jnp.bfloat16),
        ],
    )
    flops = 2 * seq_len * slot_count * block_len * head_width * 6
    attended, grad_query, grad_k, grad_v = pl.pallas_call(
        head_kernel,
        grid_spec=grid_spec,
        out_shape=[
            jax.ShapeDtypeStruct(tiles, jnp.bfloat16),
            jax.ShapeDtypeStruct(tiles, jnp.bfloat16),
            jax.ShapeDtypeStruct(tiles, jnp.float32),
            jax.ShapeDtypeStruct(tiles, jnp.float32),
        ],
        compiler_params=pltpu.CompilerParams(dimension_semantics=("arbitrary",)),
        cost_estimate=pl.CostEstimate(
            flops=flops,
            transcendentals=seq_len * slot_count * block_len,
            bytes_accessed=seq_len * head_width * 2 * 6 + seq_len * head_width * 4 * 2,
        ),
    )(
        blocks.reshape(-1),
        jnp.reshape(extra_count, (1,)),
        queries.reshape(tiles),
        grad_head.reshape(tiles),
        key_rows.reshape(tiles),
        value_rows.reshape(tiles),
    )
    summed = jnp.concatenate([grad_k, grad_v], axis=-1)
    return (
        attended.reshape(seq_len, head_width),
        grad_query.reshape(seq_len, head_width),
        summed.reshape(seq_len, 2 * head_width),
    )


def ring_reduce_scatter(chunk, ring, stride, position):
    seq_devices = lax.axis_size("seq")
    group = ring * stride
    me = (position // stride) % ring
    ahead = [
        (s, (s // group) * group + (((s // stride) % ring + 1) % ring) * stride + s % stride)
        for s in range(seq_devices)
    ]
    behind = [(b, a) for (a, b) in ahead]
    total = []
    for side, perm, sign in ((0, ahead, 1), (1, behind, -1)):
        buf = chunk((me - sign) % ring, side)
        for k in range(ring - 1):
            got = lax.ppermute(buf, "seq", perm)
            own = chunk((me - sign * (2 + k)) % ring, side)
            buf = (got.astype(jnp.float32) + own.astype(jnp.float32)).astype(jnp.bfloat16)
        total.append(buf)
    return jnp.concatenate(total, axis=-1)


def direct_sum(pieces, axis_name, size, stride, mine):
    devices = lax.axis_size(axis_name)
    group = size * stride
    got = [lax.dynamic_index_in_dim(pieces, mine, 0, keepdims=False)]
    for d in range(1, size):
        perm = [
            (i, (i // group) * group + (((i // stride) % size + d) % size) * stride + i % stride)
            for i in range(devices)
        ]
        got.append(lax.ppermute(
            lax.dynamic_index_in_dim(pieces, (mine + d) % size, 0, keepdims=False), axis_name, perm
        ))
    return got


def ring_gather_weights(piece, position, dp_index):
    dp_devices = lax.axis_size("dp")
    seq_devices = lax.axis_size("seq")
    y_count = seq_devices // RING_Z
    sizes = {"z": RING_Z, "y": y_count}

    def step_to(s, dim, shift):
        y, z = s // RING_Z, s % RING_Z
        if dim == "z":
            return y * RING_Z + (z + shift) % RING_Z
        return ((y + shift) % y_count) * RING_Z + z

    def ring(x, which, dim):
        n = sizes[dim]
        got = [x]
        for shift, steps in ((1, n // 2), (-1, n - 1 - n // 2)):
            perm = [
                (d * seq_devices + s, d * seq_devices + step_to(s, dim, shift))
                for d in range(dp_devices) if d % 2 == which
                for s in range(seq_devices)
            ]
            cur = x
            for _ in range(steps):
                cur = lax.ppermute(cur, ("dp", "seq"), perm)
                got.append(cur)
        ahead = got[1 : 1 + n // 2]
        behind = got[1 + n // 2 :]
        return jnp.stack([x] + ahead + behind[::-1])

    n_z, n_y = sizes["z"], sizes["y"]
    got = {0: [], 1: []}
    for shift, steps in ((1, {0: n_z // 2, 1: n_y // 2}), (-1, {0: n_z - 1 - n_z // 2, 1: n_y - 1 - n_y // 2})):
        cur = piece
        for k in range(max(steps.values())):
            perm = [
                (d * seq_devices + s, d * seq_devices + step_to(s, "z" if d % 2 == 0 else "y", shift))
                for d in range(dp_devices) if k < steps[d % 2]
                for s in range(seq_devices)
            ]
            cur = lax.ppermute(cur, ("dp", "seq"), perm)
            for which in (0, 1):
                if k < steps[which]:
                    got[which].append(cur)
    lists = {}
    for which, n in ((0, n_z), (1, n_y)):
        ahead = got[which][: n // 2]
        behind = got[which][n // 2 :]
        lists[which] = jnp.stack([piece] + ahead + behind[::-1])
    core = dp_index % 2
    halves = [lists[0][: n_z // 2], lists[0][n_z // 2 :]]
    plans = {0: {1: n_y // 2, -1: n_y - 1 - n_y // 2}, 1: {1: n_z // 2, -1: n_z - 1 - n_z // 2}}
    dims = {0: "y", 1: "z"}
    arrived = {0: {}, 1: {}}
    for shift in (1, -1):
        sends = {0: 2 * plans[0][shift], 1: plans[1][shift]}
        recv = []
        for j in range(max(sends.values())):
            op0 = halves[j] if j < 2 else recv[j - 2]
            op1 = lists[1] if j == 0 else recv[j - 1]
            perm = [
                (d * seq_devices + s, d * seq_devices + step_to(s, dims[d % 2], shift))
                for d in range(dp_devices) if j < sends[d % 2]
                for s in range(seq_devices)
            ]
            recv.append(lax.ppermute(jnp.where(core == 0, op0, op1), ("dp", "seq"), perm))
        arrived[0][shift] = [
            jnp.concatenate(recv[2 * k : 2 * k + 2]) for k in range(plans[0][shift])
        ]
        arrived[1][shift] = recv[: plans[1][shift]]
    first = jnp.stack([lists[0]] + arrived[0][1] + arrived[0][-1][::-1])
    second = jnp.stack([lists[1]] + arrived[1][1] + arrived[1][-1][::-1])
    return first.reshape(-1, piece.shape[-1]), second.reshape(-1, piece.shape[-1])


def ring_blocks(position, z_first):
    seq_devices = lax.axis_size("seq")
    y_count = seq_devices // RING_Z
    y, z = position // RING_Z, position % RING_Z
    dy = jnp.arange(y_count)
    dz = jnp.arange(RING_Z)
    if z_first:
        origin = ((y - dy) % y_count)[:, None] * RING_Z + ((z - dz) % RING_Z)[None, :]
    else:
        origin = ((y - dy) % y_count)[None, :] * RING_Z + ((z - dz) % RING_Z)[:, None]
    return origin.reshape(-1)


def per_device(activations, w_query, w_key, w_value, key_blocks, random_count, grad_out):
    seq_devices = lax.axis_size("seq")
    dp_devices = lax.axis_size("dp")
    position = lax.axis_index("seq")
    dp_index = lax.axis_index("dp")
    tokens = activations[0]
    grad_rows = grad_out[0]
    tok_count = tokens.shape[0]
    heads = w_query.shape[1] // HD
    kv_heads = w_key.shape[1] // HD
    query_cols = heads * HD
    kv_cols = kv_heads * HD
    all_cols = query_cols + 2 * kv_cols
    w_local = jnp.concatenate([w_query, w_key, w_value], axis=1)
    half = all_cols // 2
    core = dp_index % 2
    pairs = [(i, i ^ 1) for i in range(dp_devices)]
    grad_pieces = grad_rows.reshape(tok_count, heads, HD).transpose(1, 0, 2)
    head_grad = lax.all_to_all(grad_pieces, "seq", split_axis=0, concat_axis=1, tiled=True)[0]
    by_z, by_y = ring_gather_weights(
        lax.dynamic_slice_in_dim(w_local, core * half, half, axis=1), position, dp_index
    )
    w_mine = jnp.where(core == 0, by_z, by_y)
    w_other = lax.ppermute(w_mine, "dp", pairs)
    order_z, order_y = ring_blocks(position, True), ring_blocks(position, False)
    order_mine = jnp.where(core == 0, order_z, order_y)
    order_other = jnp.where(core == 0, order_y, order_z)
    feat = w_local.shape[0]
    token_blocks = tokens.reshape(tok_count, seq_devices, feat)
    tokens_mine = jnp.take(token_blocks, order_mine, axis=1).reshape(tok_count, -1)
    tokens_other = jnp.take(token_blocks, order_other, axis=1).reshape(tok_count, -1)
    proj_mine = jnp.dot(tokens_mine, w_mine, preferred_element_type=jnp.float32).astype(jnp.bfloat16)
    proj_other = jnp.dot(tokens_other, w_other, preferred_element_type=jnp.float32).astype(jnp.bfloat16)
    projected = jnp.zeros((tok_count, all_cols), jnp.bfloat16)
    projected = lax.dynamic_update_slice_in_dim(projected, proj_mine, core * half, axis=1)
    projected = lax.dynamic_update_slice_in_dim(projected, proj_other, (1 - core) * half, axis=1)
    queries = projected[:, :query_cols]
    key_proj = projected[:, query_cols : query_cols + kv_cols]
    value_proj = projected[:, query_cols + kv_cols :]
    query_pieces = queries.reshape(tok_count, heads, HD).transpose(1, 0, 2)
    paired = jnp.concatenate(
        [key_proj.reshape(tok_count, kv_heads, HD), value_proj.reshape(tok_count, kv_heads, HD)],
        axis=2,
    )
    kv_pieces = jnp.repeat(paired.transpose(1, 0, 2), GROUP, axis=0)
    sent = jnp.concatenate([query_pieces, kv_pieces], axis=2)
    landed = lax.all_to_all(sent, "seq", split_axis=0, concat_axis=1, tiled=True)[0]
    head_q = landed[:, :HD]
    head_k = landed[:, HD : 2 * HD]
    head_v = landed[:, 2 * HD :]
    blocks_mine = lax.dynamic_index_in_dim(key_blocks, position, 0, keepdims=False)
    count_mine = lax.dynamic_index_in_dim(random_count, position, 0, keepdims=False)
    attended, grad_query, grad_kv = head_pass(
        head_q, head_k, head_v, head_grad, blocks_mine, count_mine
    )
    back_sent = jnp.concatenate(
        [
            attended.reshape(seq_devices, tok_count, HD),
            grad_query.reshape(seq_devices, tok_count, HD),
            grad_kv.astype(jnp.bfloat16).reshape(seq_devices, tok_count, 2 * HD),
        ],
        axis=2,
    )
    back = lax.all_to_all(back_sent, "seq", split_axis=0, concat_axis=0, tiled=True)
    back_out = back[:, :, :HD]
    back_query = back[:, :, HD : 2 * HD]
    back_kv = back[:, :, 2 * HD :]
    out_rows = back_out.transpose(1, 0, 2).reshape(tok_count, heads * HD)
    grad_q_rows = back_query.transpose(1, 0, 2).reshape(tok_count, heads * HD)
    kv_sum = jnp.sum(
        back_kv.reshape(kv_heads, GROUP, tok_count, 2 * HD), axis=1, dtype=jnp.float32
    ).astype(jnp.bfloat16)
    grad_k_rows = kv_sum[:, :, :HD].transpose(1, 0, 2).reshape(tok_count, kv_heads * HD)
    grad_v_rows = kv_sum[:, :, HD:].transpose(1, 0, 2).reshape(tok_count, kv_heads * HD)
    combined = jnp.concatenate([grad_q_rows, grad_k_rows, grad_v_rows], axis=1)
    contract = (((1,), (1,)), ((), ()))
    comb_mine = lax.dynamic_slice_in_dim(combined, core * half, half, axis=1)
    comb_other = lax.dynamic_slice_in_dim(combined, (1 - core) * half, half, axis=1)
    def natural(part, order):
        back = jnp.zeros_like(order).at[order].set(jnp.arange(seq_devices, dtype=order.dtype))
        return jnp.take(part.reshape(tok_count, seq_devices, feat), back, axis=1).reshape(tok_count, -1)

    grad_x_rows = (
        natural(lax.dot_general(comb_mine, w_mine, contract, preferred_element_type=jnp.float32), order_mine)
        + natural(lax.dot_general(comb_other, w_other, contract, preferred_element_type=jnp.float32), order_other)
    ).astype(jnp.bfloat16)
    factor = 1.0 / math.sqrt(tok_count * seq_devices * dp_devices)
    over_tokens = (((0,), (0,)), ((), ()))
    y_count = seq_devices // RING_Z
    rows = tokens.shape[1] // seq_devices
    span = y_count * rows
    quarter = half // 2
    tok4 = tokens.reshape(tok_count, y_count, RING_Z, rows)
    z_me = position % RING_Z

    def ring_tokens(sign):
        order = (z_me - sign * (1 + jnp.arange(RING_Z))) % RING_Z
        return jnp.take(tok4, order, axis=2).transpose(0, 2, 1, 3).reshape(tok_count, -1)

    def term_t(columns, toks):
        return (
            lax.dot_general(columns, toks, over_tokens, preferred_element_type=jnp.float32)
            * factor
        ).astype(jnp.bfloat16)

    signs = (1, -1)
    toks = [ring_tokens(sign) for sign in signs]
    give = jnp.stack(
        [term_t(comb_other[:, i * quarter : (i + 1) * quarter], toks[i]) for i in range(2)]
    )
    got = lax.ppermute(give, "dp", pairs)
    keep = [term_t(comb_mine[:, i * quarter : (i + 1) * quarter], toks[i]) for i in range(2)]
    grad_x_rows, keep = lax.optimization_barrier((grad_x_rows, keep))
    ahead = [(s, (s // RING_Z) * RING_Z + (s % RING_Z + 1) % RING_Z) for s in range(seq_devices)]
    behind = [(b, a) for (a, b) in ahead]
    ends = []
    for i, perm in enumerate((ahead, behind)):

        def chunk(k):
            piece = slice(k * span, (k + 1) * span)
            return (
                keep[i][:, piece].astype(jnp.float32) + got[i][:, piece].astype(jnp.float32)
            ).astype(jnp.bfloat16)

        buf = chunk(0)
        for k in range(RING_Z - 1):
            arrived = lax.ppermute(buf, "seq", perm)
            buf = (arrived.astype(jnp.float32) + chunk(k + 1).astype(jnp.float32)).astype(jnp.bfloat16)
        ends.append(buf)
    by_y = jnp.concatenate(ends, axis=0).reshape(half, y_count, rows).transpose(1, 2, 0)
    from_y = direct_sum(by_y, "seq", y_count, RING_Z, position // RING_Z)
    total = from_y[0].astype(jnp.float32)
    for piece in from_y[1:]:
        total = total + piece.astype(jnp.float32)
    part = total.astype(jnp.bfloat16)
    chips = dp_devices // 2
    chip = dp_index // 2
    from_x = direct_sum(jnp.broadcast_to(part, (chips,) + part.shape), "dp", chips, 2, chip)
    by_offset = jnp.stack(from_x)
    in_order = jnp.take(by_offset, (chip - jnp.arange(chips)) % chips, axis=0)
    part = jnp.sum(in_order.astype(jnp.float32), axis=0).astype(jnp.bfloat16)
    other_half = lax.ppermute(part, "dp", pairs)
    first = jnp.where(core == 0, part, other_half)
    second = jnp.where(core == 0, other_half, part)
    grad_all = jnp.concatenate([first, second], axis=1)
    grad_wq = grad_all[:, :query_cols]
    grad_wk = grad_all[:, query_cols : query_cols + kv_cols]
    grad_wv = grad_all[:, query_cols + kv_cols :]
    return (out_rows[None], grad_x_rows[None], grad_wq, grad_wk, grad_wv)


def solution(mesh):
    placed = (
        P("dp", "seq", None),
        P("seq", None),
        P("seq", None),
        P("seq", None),
        P(),
        P(),
        P("dp", "seq", None),
    )
    return jax.shard_map(
        per_device,
        mesh=mesh,
        in_specs=placed,
        out_specs=(
            P("dp", "seq", None),
            P("dp", "seq", None),
            P("seq", None),
            P("seq", None),
            P("seq", None),
        ),
        check_vma=False,
    )
```
